128 devices in a mesh: dp: 32 (over x, z, core), cls: 4 (over y).
Axes of the slice: x: 4, y: 4, z: 4, core: 2. Of those that a mesh axis runs over, the one named last changes fastest.
Arguments:
- images: bfloat16 [4096, 64, 512], P('dp'), may hold values from -12 to 12
- pose_slot: int32 [4096], P('dp'), may hold values from 0 to 4095, as said below
- references: bfloat16 [256, 64, 512], P('cls'), may hold values from -4 to 4
- rotation_response: float32 [36, 512], replicated, may hold values from -1 to 1
- shell_weight: float32 [64], replicated, may hold values from 0.003 to 0.03
- class_lists: int32 [4096, 2], P('dp'), may hold values from 0 to 255, as said below
- class_counts: int32 [256], P('cls'), may hold values from 0 to 19999
Outputs:
- class_gradient: float32 [4, 64, 64, 512], P('cls', 'dp')
- log_evidence: float32 [4096], P('dp')
The draws below stay inside these ranges and needn't reach their ends.
Inputs may be any that keep to these rules, and one draw needn't show every extreme that they name: `pose_slot`: the particles of each micrograph block of 128 rows land exactly 4 in every pose block of 128 positions; each position is taken once. `class_lists`: each row names 2 different classes. Within each pose block of 128 rows every class that the block names is named by exactly 2 of its rows.
All inputs are finite; a program needn't handle non-finite values.
Results may differ from the reference program's by a relative error of at most 0.04.
Values may be sent and summed in bfloat16 or wider, within the bound.
No kernel may reach another device: no remote copies, remote signals or barrier semaphores. Data moves between devices by JAX's collectives and lax.ppermute only.
A program may use at most 192 MiB of HBM per device.

```python
import math
import jax
import jax.numpy as jnp
from jax import lax

NSHELL = 64
NANG = 256
K = 256
NROT = 36
LIST = 2
P_BLK = 128
MOST = 2
P_SIZE = 4096
KCOL = 64
N_DP = 32
N_CLS = 4


def pose_table(key):
    block_count = P_SIZE // P_BLK
    per_pair = P_BLK // block_count
    source_key, target_key = jax.random.split(jax.random.fold_in(key, 7))
    source_perm = jax.vmap(lambda sub_key: jax.random.permutation(sub_key, P_BLK))(jax.random.split(source_key, block_count))
    target_perm = jax.vmap(lambda sub_key: jax.random.permutation(sub_key, P_BLK))(jax.random.split(target_key, block_count))
    local_pos = jnp.arange(P_BLK, dtype=jnp.int32)[None, :]
    source_block = jnp.arange(block_count, dtype=jnp.int32)[:, None]
    dest_block = jnp.broadcast_to(local_pos // per_pair, (block_count, P_BLK))
    arrival = source_block * per_pair + local_pos % per_pair
    slot_value = dest_block * P_BLK + target_perm[dest_block, arrival]
    inverse_perm = jnp.argsort(source_perm, axis=1)
    return jnp.take_along_axis(slot_value, inverse_perm, axis=1).reshape(P_SIZE).astype(jnp.int32)


def list_table(key):
    block_count = P_SIZE // P_BLK
    used_classes = P_BLK * LIST // MOST
    base_key = jax.random.fold_in(key, 9)
    heat_level = jax.random.randint(jax.random.fold_in(base_key, 1), (K,), 0, 2)

    def one_block(block_key):
        rank_key, perm_key = jax.random.split(block_key)
        noise_rank = jax.random.randint(rank_key, (K,), 0, 1 << 16)
        class_score = (heat_level * (1 << 15) + noise_rank) * K + jnp.arange(K, dtype=jnp.int32)
        class_order = jnp.argsort(-class_score)
        chosen = class_order[:used_classes]
        item_rows = jnp.repeat(chosen, MOST, total_repeat_length=used_classes * MOST).reshape(LIST, P_BLK)
        row_perms = jax.vmap(lambda sub_key: jax.random.permutation(sub_key, P_BLK))(jax.random.split(perm_key, LIST))
        list_rows = jnp.take_along_axis(item_rows, jnp.argsort(row_perms, axis=1), axis=1)
        return list_rows.T
    tables = jax.vmap(one_block)(jax.random.split(base_key, block_count))
    return tables.reshape(P_SIZE, LIST).astype(jnp.int32)


def reference_field(key):
    values = jax.random.normal(jax.random.fold_in(key, 31), (K, NSHELL, 2 * NANG), jnp.float32)
    return jnp.clip(values, -4.0, 4.0)


def draw_pose_slot(key, part):
    return pose_table(key)


def draw_class_lists(key, part):
    return list_table(key)


def draw_references(key, part):
    return reference_field(key).astype(jnp.bfloat16)


def draw_rotation_response(key, part):
    amplitude = jax.random.uniform(jax.random.fold_in(key, 41), (NROT, NANG), jnp.float32, 0.4, 1.0)
    frequency = jnp.arange(NANG, dtype=jnp.int32)
    signed = jnp.where(frequency < NANG // 2, frequency, frequency - NANG).astype(jnp.float32)
    rot_angle = jnp.arange(NROT, dtype=jnp.int32).astype(jnp.float32) * (2.0 * math.pi / NROT)
    phase_shift = -signed[None, :] * rot_angle[:, None]
    return jnp.concatenate([amplitude * jnp.cos(phase_shift), amplitude * jnp.sin(phase_shift)], axis=1)


def draw_images(key, part):
    drawn_rows = jnp.clip(jax.random.normal(jax.random.fold_in(key, 21), (P_SIZE, NSHELL, 2 * NANG), jnp.float32), -4.0, 4.0)
    ref_field = reference_field(key)
    pose_rows = pose_table(key)
    picked = list_table(key)[pose_rows]
    strength = jnp.array([0.5, 1.0, 2.0], jnp.float32)[jnp.arange(P_SIZE) % 3]
    aligned = strength[:, None, None] * (ref_field[picked[:, 0]] + ref_field[picked[:, 1]]) * 0.7071
    chosen_rows = jnp.arange(P_SIZE) % 4 == 0
    drawn_rows = jnp.where(chosen_rows[:, None, None], aligned, drawn_rows)
    return drawn_rows.astype(jnp.bfloat16)


def plant(entries, own_key, low, top_value):
    index_at = [jax.random.randint(jax.random.fold_in(own_key, axis), (), 0, length) for axis, length in enumerate(entries.shape)]
    longest = entries.shape.index(max(entries.shape))
    next_to = index_at[:longest] + [(index_at[longest] + 1) % entries.shape[longest]] + index_at[longest + 1:]
    return entries.at[tuple(index_at)].set(low).at[tuple(next_to)].set(top_value)


def setup_inputs(seed: int = 0) -> dict:
    splits = jax.random.split(jax.random.key(seed), 8)
    return {
        "images": draw_images(jax.random.fold_in(splits[7], 71), 0),
        "pose_slot": draw_pose_slot(jax.random.fold_in(splits[7], 71), 0),
        "references": draw_references(jax.random.fold_in(splits[7], 71), 0),
        "rotation_response": draw_rotation_response(jax.random.fold_in(splits[7], 71), 0),
        "shell_weight": jnp.clip(jnp.exp(jax.random.uniform(splits[4], (NSHELL,), jnp.float32, math.log(0.003), math.log(0.03))), 0.003, 0.03),
        "class_lists": draw_class_lists(jax.random.fold_in(splits[7], 71), 0),
        "class_counts": plant(jax.random.randint(splits[6], (K,), 0, 20000), jax.random.fold_in(splits[6], 1), 0, 19999).astype(jnp.int32),
    }


def angular_tables(points):
    positions = jnp.arange(points, dtype=jnp.int32)
    product = positions[:, None] * positions[None, :] % points
    angles = product.astype(jnp.float32) * (2.0 * math.pi / points)
    cosine = jnp.cos(angles) / math.sqrt(points)
    sine_part = jnp.sin(angles) / math.sqrt(points)
    upper_half = jnp.concatenate([cosine, -sine_part], axis=1)
    lower_half = jnp.concatenate([sine_part, cosine], axis=1)
    return jnp.concatenate([upper_half, lower_half], axis=0)

def reference(images, pose_slot, references, rotation_response, shell_weight, class_lists, class_counts):
    full_table = angular_tables(NANG)
    forward = full_table.astype(jnp.bfloat16)
    inverse = full_table.T
    row_width = 2 * NANG
    total_rows = images.shape[0]
    placed = jnp.zeros_like(images).at[pose_slot].set(images)
    image_hat = jnp.dot(placed.reshape(-1, row_width), forward, preferred_element_type=jnp.float32).astype(jnp.bfloat16).reshape(total_rows, NSHELL, row_width)
    ref_hat = jnp.dot(references.reshape(-1, row_width), forward, preferred_element_type=jnp.float32).astype(jnp.bfloat16).reshape(K, NSHELL, row_width)
    weighted = (ref_hat.astype(jnp.float32) * shell_weight[None, :, None]).astype(jnp.bfloat16)
    log_prior = jnp.log1p(class_counts.astype(jnp.float32))
    rot_re = rotation_response[:, :NANG]
    rot_im = rotation_response[:, NANG:]
    coef_table = jnp.concatenate([rot_re, -rot_im, rot_re * rot_re + rot_im * rot_im], axis=1)
    blocks_hat = image_hat.reshape(N_DP, P_BLK, NSHELL, row_width)
    blocks_list = class_lists.reshape(N_DP, P_BLK, LIST)

    def scan_block(carry_sums, inputs):
        numer_sum, denom_sum = carry_sums
        block_hat, block_list = inputs
        image_f = block_hat.astype(jnp.float32)[:, None]
        near_ref = weighted[block_list].astype(jnp.float32)
        cross_re = lax.optimization_barrier(jnp.sum(image_f[..., :NANG] * near_ref[..., :NANG] + image_f[..., NANG:] * near_ref[..., NANG:], axis=2))
        cross_im = lax.optimization_barrier(jnp.sum(image_f[..., NANG:] * near_ref[..., :NANG] - image_f[..., :NANG] * near_ref[..., NANG:], axis=2))
        cross_term = jnp.concatenate([cross_re, cross_im], axis=-1)
        scores = jnp.einsum('bln,rn->blr', cross_term, rotation_response, precision=lax.Precision.HIGHEST) + log_prior[block_list][..., None]
        top_score = lax.optimization_barrier(jnp.max(scores, axis=(1, 2)))
        expo_terms = jnp.exp(scores - top_score[:, None, None])
        total_sum = lax.optimization_barrier(jnp.sum(expo_terms, axis=(1, 2)))
        posterior = expo_terms / total_sum[:, None, None]
        evidence = top_score + jnp.log(total_sum)
        coef_rows = jnp.einsum('blr,rn->bln', posterior, coef_table, precision=lax.Precision.HIGHEST)
        coef_re = coef_rows[..., None, :NANG]
        coef_im = coef_rows[..., None, NANG:2 * NANG]
        volume = coef_rows[..., None, 2 * NANG:]
        post_sum = lax.optimization_barrier(jnp.sum(posterior, axis=2))
        own_ref = ref_hat[block_list].astype(jnp.float32)
        grad_re = image_f[..., :NANG] * coef_re - image_f[..., NANG:] * coef_im - volume * own_ref[..., :NANG]
        grad_im = image_f[..., :NANG] * coef_im + image_f[..., NANG:] * coef_re - volume * own_ref[..., NANG:]
        grad_rows = jnp.concatenate([grad_re, grad_im], axis=-1).reshape(-1, NSHELL, row_width)
        flat_list = block_list.reshape(-1)
        numer_sum = numer_sum + jax.ops.segment_sum(grad_rows, flat_list, num_segments=K)
        denom_sum = denom_sum + jax.ops.segment_sum(post_sum.reshape(-1), flat_list, num_segments=K)
        return ((numer_sum, denom_sum), evidence)
    start_sums = (jnp.zeros((K, NSHELL, row_width), jnp.float32), jnp.zeros((K,), jnp.float32))
    (numer_sum, denom_sum), evidence = lax.scan(scan_block, start_sums, (blocks_hat, blocks_list))
    scaled = numer_sum / (1.0 + denom_sum)[:, None, None]
    gradient = jnp.dot(scaled.reshape(-1, row_width), inverse, precision=lax.Precision.HIGHEST)
    gradient = gradient.reshape(N_CLS, KCOL, NSHELL, row_width)
    return (gradient, evidence.reshape(-1))
```

```python
import math

import jax
import jax.numpy as jnp
from jax import lax
from jax.sharding import PartitionSpec as P

NSHELL = 64
NANG = 256
LIST = 2

HIGHEST = lax.Precision.HIGHEST


def angular_tables(points):
    positions = jnp.arange(points, dtype=jnp.int32)
    product = positions[:, None] * positions[None, :] % points
    angles = product.astype(jnp.float32) * (2.0 * math.pi / points)
    cosine = jnp.cos(angles) / math.sqrt(points)
    sine_part = jnp.sin(angles) / math.sqrt(points)
    upper_half = jnp.concatenate([cosine, -sine_part], axis=1)
    lower_half = jnp.concatenate([sine_part, cosine], axis=1)
    return jnp.concatenate([upper_half, lower_half], axis=0)


def split_bf16(x):
    high = x.astype(jnp.bfloat16)
    low = (x - high.astype(jnp.float32)).astype(jnp.bfloat16)
    return high, low


def local(
    images, pose_slot, references, rotation_response, shell_weight, class_lists, class_counts
):
    dp_index = lax.axis_index("dp")
    column = lax.axis_index("cls")
    blocksize = images.shape[0]
    col_classes = references.shape[0]
    full_table = angular_tables(NANG)
    forward = full_table.astype(jnp.bfloat16)
    inverse = full_table.T

    all_lists = lax.all_gather(class_lists, "dp", tiled=True)
    all_slots = lax.all_gather(pose_slot, "dp", tiled=True)
    my_lists = all_lists[pose_slot]
    local_class = (my_lists - column * col_classes).T
    inside = (local_class >= 0) & (local_class < col_classes)
    class_ids = jnp.arange(col_classes, dtype=jnp.int32)
    pick = local_class[:, None, :] == class_ids[None, :, None]

    image_t = jnp.einsum(
        "pjn,nm->mjp", images, forward, preferred_element_type=jnp.float32
    ).astype(jnp.bfloat16)
    image_re = image_t[:NANG]
    image_im = image_t[NANG:]
    ref_t = jnp.einsum(
        "kjn,nm->mkj", references, forward, preferred_element_type=jnp.float32
    ).astype(jnp.bfloat16)
    weighted_t = (ref_t.astype(jnp.float32) * shell_weight[None, None, :]).astype(jnp.bfloat16)
    w_re = weighted_t[:NANG]
    w_im = weighted_t[NANG:]
    stack_re = jnp.concatenate([w_re, -w_im], axis=1)
    stack_im = jnp.concatenate([w_im, w_re], axis=1)
    cross = jnp.einsum(
        "mkj,mjp->mkp", stack_re, image_re, preferred_element_type=jnp.float32
    ) + jnp.einsum("mkj,mjp->mkp", stack_im, image_im, preferred_element_type=jnp.float32)
    cross = cross.reshape(NANG, 2, col_classes, blocksize)
    cross_sel = jnp.sum(
        jnp.where(pick[None, None], cross[:, :, None], 0.0), axis=3
    )
    rot = rotation_response.reshape(-1, 2, NANG)
    log_prior = jnp.log1p(class_counts.astype(jnp.float32))
    prior_sel = jnp.sum(jnp.where(pick, log_prior[None, :, None], 0.0), axis=1)
    scores = (
        jnp.einsum("rtm,mtap->rap", rot, cross_sel, precision=HIGHEST) + prior_sel[None]
    )
    scores = jnp.where(inside[None], scores, -1e30)
    top_local = jnp.max(scores, axis=(0, 1))
    total_local = jnp.sum(
        jnp.where(inside[None], jnp.exp(scores - top_local[None, None]), 0.0), axis=(0, 1)
    )
    tops = lax.all_gather(top_local, "cls")
    totals = lax.all_gather(total_local, "cls")
    top_score = jnp.max(tops, axis=0)
    total_sum = jnp.sum(totals * jnp.exp(tops - top_score[None]), axis=0)
    posterior = (
        jnp.where(inside[None], jnp.exp(scores - top_score[None, None]), 0.0)
        / total_sum[None, None]
    )
    evidence = top_score + jnp.log(total_sum)

    rot_re = rotation_response[:, :NANG]
    rot_im = rotation_response[:, NANG:]
    coef_table = jnp.concatenate([rot_re, -rot_im, rot_re * rot_re + rot_im * rot_im], axis=1)
    coef = jnp.einsum("rn,rap->nap", coef_table, posterior, precision=HIGHEST)
    coef = coef.reshape(3, NANG, LIST, blocksize)
    post_sum = jnp.sum(posterior, axis=0)
    pick_f = pick.astype(jnp.float32)
    spread = jnp.sum(
        jnp.where(pick[None, None], coef[:2, :, :, None], 0.0), axis=2
    )
    spread = jnp.concatenate([spread[0], spread[1]], axis=1)
    volume = jnp.einsum("map,akp->mk", coef[2], pick_f, precision=HIGHEST)
    denom = jnp.einsum("ap,akp->k", post_sum, pick_f, precision=HIGHEST)
    spread_hi, spread_lo = split_bf16(spread)

    def against(image_part):
        return jnp.einsum(
            "mjp,mqp->mjq", image_part, spread_hi, preferred_element_type=jnp.float32
        ) + jnp.einsum("mjp,mqp->mjq", image_part, spread_lo, preferred_element_type=jnp.float32)

    q_re = against(image_re)
    q_im = against(image_im)
    ref_jk = jnp.swapaxes(ref_t, 1, 2).astype(jnp.float32)
    numer_re = q_re[..., :col_classes] - q_im[..., col_classes:] - volume[:, None, :] * ref_jk[:NANG]
    numer_im = q_re[..., col_classes:] + q_im[..., :col_classes] - volume[:, None, :] * ref_jk[NANG:]
    numer = jnp.concatenate([numer_re, numer_im], axis=0)
    partial = jnp.einsum("mjk,mn->kjn", numer, inverse, precision=lax.Precision.HIGH)
    summed = lax.psum_scatter(partial, "dp", scatter_dimension=0, tiled=True)
    denom_sum = lax.psum_scatter(denom, "dp", scatter_dimension=0, tiled=True)
    gradient = summed / (1.0 + denom_sum)[:, None, None]

    all_evidence = lax.all_gather(evidence, "dp", tiled=True)
    wanted = dp_index * blocksize + jnp.arange(blocksize, dtype=jnp.int32)
    placed = jnp.sum(
        jnp.where(all_slots[None, :] == wanted[:, None], all_evidence[None, :], 0.0), axis=1
    )
    return (gradient[None], placed)


def solution(mesh):
    return jax.shard_map(
        local,
        mesh=mesh,
        in_specs=(
            P("dp", None, None),
            P("dp"),
            P("cls", None, None),
            P(),
            P(),
            P("dp", None),
            P("cls"),
        ),
        out_specs=(P("cls", "dp", None, None), P("dp")),
        check_vma=False,
    )
```

```python
import math

import jax
import jax.numpy as jnp
from jax import lax
from jax.sharding import PartitionSpec as P

NSHELL = 64
NANG = 256
LIST = 2

HIGHEST = lax.Precision.HIGHEST


def angular_tables(points):
    positions = jnp.arange(points, dtype=jnp.int32)
    product = positions[:, None] * positions[None, :] % points
    angles = product.astype(jnp.float32) * (2.0 * math.pi / points)
    cosine = jnp.cos(angles) / math.sqrt(points)
    sine_part = jnp.sin(angles) / math.sqrt(points)
    upper_half = jnp.concatenate([cosine, -sine_part], axis=1)
    lower_half = jnp.concatenate([sine_part, cosine], axis=1)
    return jnp.concatenate([upper_half, lower_half], axis=0)


def split_bf16(x):
    high = x.astype(jnp.bfloat16)
    low = (x - high.astype(jnp.float32)).astype(jnp.bfloat16)
    return high, low


def local(
    images, pose_slot, references, rotation_response, shell_weight, class_lists, class_counts
):
    dp_index = lax.axis_index("dp")
    column = lax.axis_index("cls")
    dp_count = lax.axis_size("dp")
    blocksize = images.shape[0]
    col_classes = references.shape[0]
    row_width = 2 * NANG
    full_table = angular_tables(NANG)
    forward_ms = full_table.astype(jnp.bfloat16).reshape(row_width, 2, NANG).transpose(0, 2, 1)
    inverse_ms = full_table.T.reshape(2, NANG, row_width).transpose(1, 0, 2)

    packed = jnp.concatenate([class_lists, pose_slot[:, None]], axis=1)
    all_packed = lax.all_gather(packed, "dp", tiled=True)
    all_lists = all_packed[:, :LIST]
    all_slots = all_packed[:, LIST]
    slot_hit = jnp.arange(all_slots.shape[0], dtype=jnp.int32)[None, :] == pose_slot[:, None]
    my_lists = jnp.stack(
        [jnp.sum(jnp.where(slot_hit, all_lists[None, :, a], 0), axis=1) for a in range(LIST)]
    )
    local_class = my_lists - column * col_classes
    inside = (local_class >= 0) & (local_class < col_classes)
    class_ids = jnp.arange(col_classes, dtype=jnp.int32)
    pick = local_class[:, None, :] == class_ids[None, :, None]

    image_x = jnp.einsum(
        "pjn,nms->msjp", images, forward_ms, preferred_element_type=jnp.float32
    ).astype(jnp.bfloat16)
    image_c = image_x.reshape(NANG, 2 * NSHELL, blocksize)
    ref_x = jnp.einsum(
        "kjn,nms->mskj", references, forward_ms, preferred_element_type=jnp.float32
    ).astype(jnp.bfloat16)
    weighted = (ref_x.astype(jnp.float32) * shell_weight[None, None, None, :]).astype(jnp.bfloat16)
    w_re = weighted[:, 0]
    w_im = weighted[:, 1]
    row_re = jnp.concatenate([w_re, w_im], axis=-1)
    row_im = jnp.concatenate([-w_im, w_re], axis=-1)
    stacked = jnp.concatenate([row_re, row_im], axis=1)
    cross = jnp.einsum("mqc,mcp->mqp", stacked, image_c, preferred_element_type=jnp.float32)
    cross = cross.reshape(NANG, 2, col_classes, blocksize)
    cross_sel = jnp.sum(jnp.where(pick[None, None], cross[:, :, None], 0.0), axis=3)
    rot = rotation_response.reshape(-1, 2, NANG)
    log_prior = jnp.log1p(class_counts.astype(jnp.float32))
    prior_sel = jnp.sum(jnp.where(pick, log_prior[None, :, None], 0.0), axis=1)
    scores = jnp.einsum("rtm,mtap->rap", rot, cross_sel, precision=HIGHEST) + prior_sel[None]
    scores = jnp.where(inside[None], scores, -1e30)
    top_local = jnp.max(scores, axis=(0, 1))
    total_local = jnp.sum(
        jnp.where(inside[None], jnp.exp(scores - top_local[None, None]), 0.0), axis=(0, 1)
    )
    gathered = lax.all_gather(jnp.stack([top_local, total_local]), "cls")
    tops = gathered[:, 0]
    totals = gathered[:, 1]
    top_score = jnp.max(tops, axis=0)
    total_sum = jnp.sum(totals * jnp.exp(tops - top_score[None]), axis=0)
    posterior = (
        jnp.where(inside[None], jnp.exp(scores - top_score[None, None]), 0.0)
        / total_sum[None, None]
    )
    evidence = top_score + jnp.log(total_sum)
    post_sum = jnp.sum(posterior, axis=0)

    rot_re = rotation_response[:, :NANG]
    rot_im = rotation_response[:, NANG:]
    coef_table = jnp.concatenate([rot_re, -rot_im, rot_re * rot_re + rot_im * rot_im], axis=1)
    coef = jnp.einsum("rn,rap->nap", coef_table, posterior, precision=HIGHEST)
    coef = coef.reshape(3, NANG, LIST, blocksize)
    coef_mu = jnp.transpose(coef[:2], (1, 0, 2, 3))
    spread = jnp.sum(jnp.where(pick[None, None], coef_mu[:, :, :, None], 0.0), axis=2)
    spread = spread.reshape(NANG, 2 * col_classes, blocksize)
    volume = jnp.einsum("map,akp->mk", coef[2], pick.astype(jnp.float32), precision=HIGHEST)
    spread_hi, spread_lo = split_bf16(spread)
    grad_q = jnp.einsum(
        "mqp,mcp->mqc", spread_hi, image_c, preferred_element_type=jnp.float32
    ) + jnp.einsum("mqp,mcp->mqc", spread_lo, image_c, preferred_element_type=jnp.float32)
    grad_q = grad_q.reshape(NANG, 2, col_classes, 2, NSHELL)
    ref_f = ref_x.astype(jnp.float32)
    vol = volume[:, :, None]
    numer_re = grad_q[:, 0, :, 0] - grad_q[:, 1, :, 1] - vol * ref_f[:, 0]
    numer_im = grad_q[:, 1, :, 0] + grad_q[:, 0, :, 1] - vol * ref_f[:, 1]
    numer = jnp.stack([numer_re, numer_im], axis=1)
    partial = jnp.einsum("mskj,msn->kjn", numer, inverse_ms, precision=lax.Precision.HIGH)

    outgoing = partial.reshape(dp_count, col_classes // dp_count, NSHELL, row_width)
    arrived = lax.all_to_all(
        outgoing.astype(jnp.bfloat16), "dp", split_axis=0, concat_axis=0, tiled=True
    )
    summed = jnp.sum(arrived.astype(jnp.float32), axis=0)

    denom_part = jnp.einsum("ap,akp->k", post_sum, pick.astype(jnp.float32), precision=HIGHEST)
    tail = jnp.concatenate([evidence, denom_part])
    all_tail = lax.all_gather(tail, "dp")
    all_evidence = all_tail[:, :blocksize].reshape(-1)
    per_owner = col_classes // dp_count
    denom_all = jnp.sum(all_tail[:, blocksize:], axis=0)
    own_denom = lax.dynamic_slice_in_dim(denom_all, dp_index * per_owner, per_owner)
    gradient = summed / (1.0 + own_denom)[:, None, None]
    wanted = dp_index * blocksize + jnp.arange(blocksize, dtype=jnp.int32)
    placed = jnp.sum(
        jnp.where(all_slots[None, :] == wanted[:, None], all_evidence[None, :], 0.0), axis=1
    )
    return (gradient[None], placed)


def solution(mesh):
    return jax.shard_map(
        local,
        mesh=mesh,
        in_specs=(
            P("dp", None, None),
            P("dp"),
            P("cls", None, None),
            P(),
            P(),
            P("dp", None),
            P("cls"),
        ),
        out_specs=(P("cls", "dp", None, None), P("dp")),
        check_vma=False,
    )
```

```python
import math

import jax
import jax.numpy as jnp
from jax import lax
from jax.experimental import pallas as pl
from jax.experimental.pallas import tpu as pltpu
from jax.sharding import PartitionSpec as P

NSHELL = 64
NANG = 256
LIST = 2

HIGHEST = lax.Precision.HIGHEST
F32 = jnp.float32


def angular_tables(points):
    positions = jnp.arange(points, dtype=jnp.int32)
    product = positions[:, None] * positions[None, :] % points
    angles = product.astype(jnp.float32) * (2.0 * math.pi / points)
    cosine = jnp.cos(angles) / math.sqrt(points)
    sine_part = jnp.sin(angles) / math.sqrt(points)
    upper_half = jnp.concatenate([cosine, -sine_part], axis=1)
    lower_half = jnp.concatenate([sine_part, cosine], axis=1)
    return jnp.concatenate([upper_half, lower_half], axis=0)


def cross_kernel(count_ref, ent_p_ref, ent_k_ref, image_ref, weight_ref, out_ref):
    out_ref[...] = jnp.zeros_like(out_ref)

    def body(e, carry):
        x = image_ref[ent_p_ref[e]].astype(F32)
        w = weight_ref[ent_k_ref[e]].astype(F32)
        x_re = x[:, :NANG]
        x_im = x[:, NANG:]
        w_re = w[:, :NANG]
        w_im = w[:, NANG:]
        c_re = jnp.sum(x_re * w_re + x_im * w_im, axis=0, keepdims=True)
        c_im = jnp.sum(x_im * w_re - x_re * w_im, axis=0, keepdims=True)
        out_ref[pl.ds(e, 1), :] = jnp.concatenate([c_re, c_im], axis=1)
        return carry

    lax.fori_loop(0, count_ref[0], body, 0)


def grad_kernel(count_ref, ent_p_ref, ent_k_ref, image_ref, coef_ref, acc_ref):
    acc_ref[...] = jnp.zeros_like(acc_ref)

    def body(e, carry):
        x = image_ref[ent_p_ref[e]].astype(F32)
        c = coef_ref[pl.ds(e, 1), :]
        c_re = c[:, :NANG]
        c_im = c[:, NANG:]
        x_re = x[:, :NANG]
        x_im = x[:, NANG:]
        g_re = x_re * c_re - x_im * c_im
        g_im = x_re * c_im + x_im * c_re
        k = ent_k_ref[e]
        acc_ref[k] = acc_ref[k] + jnp.concatenate([g_re, g_im], axis=1)
        return carry

    lax.fori_loop(0, count_ref[0], body, 0)


def smem():
    return pl.BlockSpec(memory_space=pltpu.SMEM)


def vmem():
    return pl.BlockSpec(memory_space=pltpu.VMEM)


def local(
    images, pose_slot, references, rotation_response, shell_weight, class_lists, class_counts
):
    dp_index = lax.axis_index("dp")
    column = lax.axis_index("cls")
    dp_count = lax.axis_size("dp")
    blocksize = images.shape[0]
    col_classes = references.shape[0]
    per_owner = col_classes // dp_count
    per_pair = blocksize // dp_count
    row_width = 2 * NANG
    entries = blocksize * LIST
    full_table = angular_tables(NANG)
    forward = full_table.astype(jnp.bfloat16)
    inverse = full_table.T

    packed = jnp.concatenate([class_lists, pose_slot[:, None]], axis=1)
    all_packed = lax.all_to_all(
        jnp.broadcast_to(packed[None], (dp_count,) + packed.shape), "dp", 0, 0, tiled=True
    ).reshape(dp_count * blocksize, LIST + 1)
    all_lists = all_packed[:, :LIST]
    slot_hit = jnp.arange(all_lists.shape[0], dtype=jnp.int32)[None, :] == pose_slot[:, None]
    my_lists = jnp.stack(
        [jnp.sum(jnp.where(slot_hit, all_lists[None, :, a], 0), axis=1) for a in range(LIST)],
        axis=1,
    )
    local_class = (my_lists - column * col_classes).reshape(entries)
    inside = (local_class >= 0) & (local_class < col_classes)
    inside_i = inside.astype(jnp.int32)
    count = jnp.sum(inside_i)
    before_in = jnp.cumsum(inside_i) - inside_i
    before_out = jnp.cumsum(1 - inside_i) - (1 - inside_i)
    rank = jnp.where(inside, before_in, count + before_out)
    slots = jnp.arange(entries, dtype=jnp.int32)
    at_rank = rank[None, :] == slots[:, None]
    order = jnp.sum(jnp.where(at_rank, slots[None, :], 0), axis=1)
    safe_class = jnp.clip(local_class, 0, col_classes - 1)
    ent_p = order // LIST
    ent_k = jnp.sum(jnp.where(at_rank, safe_class[None, :], 0), axis=1)
    count_arr = count.reshape(1)

    image_hat = jnp.dot(
        images.reshape(-1, row_width), forward, preferred_element_type=F32
    ).astype(jnp.bfloat16).reshape(images.shape)
    ref_hat = jnp.dot(
        references.reshape(-1, row_width), forward, preferred_element_type=F32
    ).astype(jnp.bfloat16).reshape(references.shape)
    weighted = (ref_hat.astype(F32) * shell_weight[None, :, None]).astype(jnp.bfloat16)

    cross_c = pl.pallas_call(
        cross_kernel,
        out_shape=jax.ShapeDtypeStruct((entries, row_width), F32),
        in_specs=[smem(), smem(), smem(), vmem(), vmem()],
        out_specs=vmem(),
    )(count_arr, ent_p, ent_k, image_hat, weighted)

    log_prior = jnp.log1p(class_counts.astype(F32))
    prior = jnp.sum(
        jnp.where(safe_class[:, None] == jnp.arange(col_classes)[None, :], log_prior[None, :], 0.0),
        axis=1,
    )
    scores_c = jnp.dot(cross_c, rotation_response.T, precision=HIGHEST)
    scores = jnp.take(scores_c, rank, axis=0) + prior[:, None]
    scores = jnp.where(inside[:, None], scores, -1e30).reshape(blocksize, LIST, -1)
    inside_pa = inside.reshape(blocksize, LIST)
    top_local = jnp.max(scores, axis=(1, 2))
    total_local = jnp.sum(
        jnp.where(inside_pa[..., None], jnp.exp(scores - top_local[:, None, None]), 0.0), axis=(1, 2)
    )
    gathered = lax.all_gather(jnp.stack([top_local, total_local]), "cls")
    tops = gathered[:, 0]
    totals = gathered[:, 1]
    top_score = jnp.max(tops, axis=0)
    total_sum = jnp.sum(totals * jnp.exp(tops - top_score[None]), axis=0)
    posterior = (
        jnp.where(inside_pa[..., None], jnp.exp(scores - top_score[:, None, None]), 0.0)
        / total_sum[:, None, None]
    )
    evidence = top_score + jnp.log(total_sum)
    post_sum = jnp.sum(posterior, axis=2).reshape(entries)

    rot_re = rotation_response[:, :NANG]
    rot_im = rotation_response[:, NANG:]
    coef_table = jnp.concatenate([rot_re, -rot_im, rot_re * rot_re + rot_im * rot_im], axis=1)
    coef = jnp.dot(posterior.reshape(entries, -1), coef_table, precision=HIGHEST)
    coef_c = jnp.take(coef, order, axis=0)

    numer_acc = pl.pallas_call(
        grad_kernel,
        out_shape=jax.ShapeDtypeStruct(references.shape, F32),
        in_specs=[smem(), smem(), smem(), vmem(), vmem()],
        out_specs=vmem(),
    )(count_arr, ent_p, ent_k, image_hat, coef_c[:, :row_width])

    class_pick = (
        (local_class[None, :] == jnp.arange(col_classes, dtype=jnp.int32)[:, None]) & inside[None, :]
    ).astype(F32)
    volume = jnp.dot(class_pick, coef[:, row_width:], precision=HIGHEST)
    denom_part = jnp.dot(class_pick, post_sum, precision=HIGHEST)
    volume_full = jnp.concatenate([volume, volume], axis=1)
    numer = numer_acc - volume_full[:, None, :] * ref_hat.astype(F32)
    partial = jnp.dot(
        numer.reshape(-1, row_width), inverse, precision=lax.Precision.HIGH
    ).reshape(references.shape)

    outgoing = partial.reshape(dp_count, per_owner, NSHELL, row_width)
    arrived = lax.all_to_all(
        outgoing.astype(jnp.bfloat16), "dp", split_axis=0, concat_axis=0, tiled=True
    )
    summed = jnp.sum(arrived.astype(F32), axis=0)

    dest = pose_slot // blocksize
    dest_hit = dest[None, :] == jnp.arange(dp_count, dtype=jnp.int32)[:, None]
    dest_i = dest_hit.astype(jnp.int32)
    within = jnp.sum((jnp.cumsum(dest_i, axis=1) - dest_i) * dest_i, axis=0)
    sel = dest_hit[:, None, :] & (
        within[None, None, :] == jnp.arange(per_pair, dtype=jnp.int32)[None, :, None]
    )
    send_ev = jnp.sum(jnp.where(sel, evidence[None, None, :], 0.0), axis=2)
    send_pos = jnp.sum(jnp.where(sel, (pose_slot % blocksize).astype(F32)[None, None, :], 0.0), axis=2)
    send_den = denom_part.reshape(dp_count, per_owner)
    small = jnp.concatenate([send_ev, send_pos, send_den], axis=1)
    got = lax.all_to_all(small, "dp", 0, 0, tiled=True)
    got_ev = got[:, :per_pair].reshape(-1)
    got_pos = got[:, per_pair : 2 * per_pair].reshape(-1)
    own_denom = jnp.sum(got[:, 2 * per_pair :], axis=0)
    gradient = summed / (1.0 + own_denom)[:, None, None]
    rows = jnp.arange(blocksize, dtype=F32)
    placed = jnp.sum(jnp.where(got_pos[None, :] == rows[:, None], got_ev[None, :], 0.0), axis=1)
    return (gradient[None], placed)


def solution(mesh):
    return jax.shard_map(
        local,
        mesh=mesh,
        in_specs=(
            P("dp", None, None),
            P("dp"),
            P("cls", None, None),
            P(),
            P(),
            P("dp", None),
            P("cls"),
        ),
        out_specs=(P("cls", "dp", None, None), P("dp")),
        check_vma=False,
    )
```

```python
import math

import jax
import jax.numpy as jnp
from jax import lax
from jax.experimental import pallas as pl
from jax.experimental.pallas import tpu as pltpu
from jax.sharding import PartitionSpec as P

NSHELL = 64
NANG = 256
LIST = 2

HIGHEST = lax.Precision.HIGHEST
F32 = jnp.float32


def angular_tables(points):
    positions = jnp.arange(points, dtype=jnp.int32)
    product = positions[:, None] * positions[None, :] % points
    angles = product.astype(jnp.float32) * (2.0 * math.pi / points)
    cosine = jnp.cos(angles) / math.sqrt(points)
    sine_part = jnp.sin(angles) / math.sqrt(points)
    upper_half = jnp.concatenate([cosine, -sine_part], axis=1)
    lower_half = jnp.concatenate([sine_part, cosine], axis=1)
    return jnp.concatenate([upper_half, lower_half], axis=0)


CHUNK = 512


def cross_kernel(
    count_ref, ent_p_ref, ent_k_ref, image_ref, refs_ref, forward_ref, wrow_ref,
    cross_ref, image_hat_ref, ref_hat_ref, weighted_ref,
):
    forward = forward_ref[...]
    wrow = wrow_ref[...]

    def image_dft(c, carry):
        r = pl.multiple_of(c * CHUNK, CHUNK)
        image_hat_ref[pl.ds(r, CHUNK), :] = jnp.dot(
            image_ref[pl.ds(r, CHUNK), :], forward, preferred_element_type=F32
        ).astype(jnp.bfloat16)
        return carry

    def ref_dft(c, carry):
        r = pl.multiple_of(c * CHUNK, CHUNK)
        hat = jnp.dot(
            refs_ref[pl.ds(r, CHUNK), :], forward, preferred_element_type=F32
        ).astype(jnp.bfloat16)
        ref_hat_ref[pl.ds(r, CHUNK), :] = hat
        weighted_ref[pl.ds(r, CHUNK), :] = (hat.astype(F32) * wrow).astype(jnp.bfloat16)
        return carry

    lax.fori_loop(0, image_ref.shape[0] // CHUNK, image_dft, 0)
    lax.fori_loop(0, refs_ref.shape[0] // CHUNK, ref_dft, 0)
    cross_ref[...] = jnp.zeros_like(cross_ref)

    def body(e, carry):
        rp = pl.multiple_of(ent_p_ref[e] * NSHELL, NSHELL)
        rk = pl.multiple_of(ent_k_ref[e] * NSHELL, NSHELL)
        x = image_hat_ref[pl.ds(rp, NSHELL), :].astype(F32)
        w = weighted_ref[pl.ds(rk, NSHELL), :].astype(F32)
        x_re = x[:, :NANG]
        x_im = x[:, NANG:]
        w_re = w[:, :NANG]
        w_im = w[:, NANG:]
        c_re = jnp.sum(x_re * w_re + x_im * w_im, axis=0, keepdims=True)
        c_im = jnp.sum(x_im * w_re - x_re * w_im, axis=0, keepdims=True)
        cross_ref[pl.ds(e, 1), :] = jnp.concatenate([c_re, c_im], axis=1)
        return carry

    lax.fori_loop(0, count_ref[0], body, 0)


def grad_kernel(
    count_ref, ent_p_ref, ent_k_ref, image_hat_ref, coef_ref, ref_hat_ref, volume_ref,
    out_ref, acc_ref,
):
    def init(k, carry):
        r = pl.multiple_of(k * NSHELL, NSHELL)
        acc_ref[pl.ds(r, NSHELL), :] = -volume_ref[pl.ds(k, 1), :] * ref_hat_ref[
            pl.ds(r, NSHELL), :
        ].astype(F32)
        return carry

    lax.fori_loop(0, volume_ref.shape[0], init, 0)

    def body(e, carry):
        rp = pl.multiple_of(ent_p_ref[e] * NSHELL, NSHELL)
        rk = pl.multiple_of(ent_k_ref[e] * NSHELL, NSHELL)
        x = image_hat_ref[pl.ds(rp, NSHELL), :].astype(F32)
        c = coef_ref[pl.ds(e, 1), :]
        c_re = c[:, :NANG]
        c_im = c[:, NANG:]
        x_re = x[:, :NANG]
        x_im = x[:, NANG:]
        g_re = x_re * c_re - x_im * c_im
        g_im = x_re * c_im + x_im * c_re
        acc_ref[pl.ds(rk, NSHELL), :] = acc_ref[pl.ds(rk, NSHELL), :] + jnp.concatenate(
            [g_re, g_im], axis=1
        )
        return carry

    lax.fori_loop(0, count_ref[0], body, 0)

    def finish(c, carry):
        r = pl.multiple_of(c * CHUNK, CHUNK)
        out_ref[pl.ds(r, CHUNK), :] = acc_ref[pl.ds(r, CHUNK), :].astype(jnp.bfloat16)
        return carry

    lax.fori_loop(0, acc_ref.shape[0] // CHUNK, finish, 0)


def smem():
    return pl.BlockSpec(memory_space=pltpu.SMEM)


def vmem():
    return pl.BlockSpec(memory_space=pltpu.VMEM)


def local(
    images, pose_slot, references, rotation_response, shell_weight, class_lists, class_counts
):
    dp_index = lax.axis_index("dp")
    column = lax.axis_index("cls")
    dp_count = lax.axis_size("dp")
    blocksize = images.shape[0]
    col_classes = references.shape[0]
    per_owner = col_classes // dp_count
    per_pair = blocksize // dp_count
    row_width = 2 * NANG
    entries = blocksize * LIST
    full_table = angular_tables(NANG)
    forward = full_table.astype(jnp.bfloat16)
    inverse = full_table.T

    packed = jnp.concatenate([class_lists, pose_slot[:, None]], axis=1)
    all_packed = lax.all_to_all(
        jnp.broadcast_to(packed[None], (dp_count,) + packed.shape), "dp", 0, 0, tiled=True
    ).reshape(dp_count * blocksize, LIST + 1)
    all_lists = all_packed[:, :LIST]
    slot_hit = jnp.arange(all_lists.shape[0], dtype=jnp.int32)[None, :] == pose_slot[:, None]
    my_lists = jnp.stack(
        [jnp.sum(jnp.where(slot_hit, all_lists[None, :, a], 0), axis=1) for a in range(LIST)],
        axis=1,
    )
    local_class = (my_lists - column * col_classes).reshape(entries)
    inside = (local_class >= 0) & (local_class < col_classes)
    inside_i = inside.astype(jnp.int32)
    count = jnp.sum(inside_i)
    before_in = jnp.cumsum(inside_i) - inside_i
    before_out = jnp.cumsum(1 - inside_i) - (1 - inside_i)
    rank = jnp.where(inside, before_in, count + before_out)
    slots = jnp.arange(entries, dtype=jnp.int32)
    at_rank = rank[None, :] == slots[:, None]
    order = jnp.sum(jnp.where(at_rank, slots[None, :], 0), axis=1)
    safe_class = jnp.clip(local_class, 0, col_classes - 1)
    ent_p = order // LIST
    ent_k = jnp.sum(jnp.where(at_rank, safe_class[None, :], 0), axis=1)
    count_arr = count.reshape(1)

    image_rows = images.shape[0] * NSHELL
    ref_rows = col_classes * NSHELL
    wrow = jnp.tile(shell_weight, CHUNK // NSHELL)[:, None]
    params = pltpu.CompilerParams(vmem_limit_bytes=60 * 1024 * 1024)
    cross_c, image_hat, ref_hat = pl.pallas_call(
        cross_kernel,
        out_shape=(
            jax.ShapeDtypeStruct((entries, row_width), F32),
            jax.ShapeDtypeStruct((image_rows, row_width), jnp.bfloat16),
            jax.ShapeDtypeStruct((ref_rows, row_width), jnp.bfloat16),
        ),
        in_specs=[smem(), smem(), smem(), vmem(), vmem(), vmem(), vmem()],
        out_specs=(vmem(), vmem(), vmem()),
        scratch_shapes=[pltpu.VMEM((ref_rows, row_width), jnp.bfloat16)],
        compiler_params=params,
    )(
        count_arr, ent_p, ent_k, images.reshape(image_rows, row_width),
        references.reshape(ref_rows, row_width), forward, wrow,
    )

    log_prior = jnp.log1p(class_counts.astype(F32))
    prior = jnp.sum(
        jnp.where(safe_class[:, None] == jnp.arange(col_classes)[None, :], log_prior[None, :], 0.0),
        axis=1,
    )
    scores_c = jnp.dot(cross_c, rotation_response.T, precision=HIGHEST)
    scores = jnp.take(scores_c, rank, axis=0) + prior[:, None]
    scores = jnp.where(inside[:, None], scores, -1e30).reshape(blocksize, LIST, -1)
    inside_pa = inside.reshape(blocksize, LIST)
    top_local = jnp.max(scores, axis=(1, 2))
    total_local = jnp.sum(
        jnp.where(inside_pa[..., None], jnp.exp(scores - top_local[:, None, None]), 0.0), axis=(1, 2)
    )
    gathered = lax.all_gather(jnp.stack([top_local, total_local]), "cls")
    tops = gathered[:, 0]
    totals = gathered[:, 1]
    top_score = jnp.max(tops, axis=0)
    total_sum = jnp.sum(totals * jnp.exp(tops - top_score[None]), axis=0)
    posterior = (
        jnp.where(inside_pa[..., None], jnp.exp(scores - top_score[:, None, None]), 0.0)
        / total_sum[:, None, None]
    )
    evidence = top_score + jnp.log(total_sum)
    post_sum = jnp.sum(posterior, axis=2).reshape(entries)

    rot_re = rotation_response[:, :NANG]
    rot_im = rotation_response[:, NANG:]
    coef_table = jnp.concatenate([rot_re, -rot_im, rot_re * rot_re + rot_im * rot_im], axis=1)
    coef = jnp.dot(posterior.reshape(entries, -1), coef_table, precision=HIGHEST)
    coef_c = jnp.take(coef, order, axis=0)

    class_pick = (
        (local_class[None, :] == jnp.arange(col_classes, dtype=jnp.int32)[:, None]) & inside[None, :]
    ).astype(F32)
    volume = jnp.dot(class_pick, coef[:, row_width:], precision=HIGHEST)
    denom_part = jnp.dot(class_pick, post_sum, precision=HIGHEST)
    volume_full = jnp.concatenate([volume, volume], axis=1)
    numer = pl.pallas_call(
        grad_kernel,
        out_shape=jax.ShapeDtypeStruct((ref_rows, row_width), jnp.bfloat16),
        in_specs=[smem(), smem(), smem(), vmem(), vmem(), vmem(), vmem()],
        out_specs=vmem(),
        scratch_shapes=[pltpu.VMEM((ref_rows, row_width), F32)],
        compiler_params=params,
    )(count_arr, ent_p, ent_k, image_hat, coef_c[:, :row_width], ref_hat, volume_full)

    outgoing = numer.reshape(dp_count, per_owner, NSHELL, row_width)
    arrived = lax.all_to_all(outgoing, "dp", split_axis=0, concat_axis=0, tiled=True)
    summed = jnp.sum(arrived.astype(F32), axis=0)
    summed = jnp.dot(
        summed.reshape(-1, row_width), inverse, precision=HIGHEST
    ).reshape(summed.shape)

    dest = pose_slot // blocksize
    dest_hit = dest[None, :] == jnp.arange(dp_count, dtype=jnp.int32)[:, None]
    dest_i = dest_hit.astype(jnp.int32)
    within = jnp.sum((jnp.cumsum(dest_i, axis=1) - dest_i) * dest_i, axis=0)
    sel = dest_hit[:, None, :] & (
        within[None, None, :] == jnp.arange(per_pair, dtype=jnp.int32)[None, :, None]
    )
    send_ev = jnp.sum(jnp.where(sel, evidence[None, None, :], 0.0), axis=2)
    send_pos = jnp.sum(jnp.where(sel, (pose_slot % blocksize).astype(F32)[None, None, :], 0.0), axis=2)
    send_den = denom_part.reshape(dp_count, per_owner)
    small = jnp.concatenate([send_ev, send_pos, send_den], axis=1)
    got = lax.all_to_all(small, "dp", 0, 0, tiled=True)
    got_ev = got[:, :per_pair].reshape(-1)
    got_pos = got[:, per_pair : 2 * per_pair].reshape(-1)
    own_denom = jnp.sum(got[:, 2 * per_pair :], axis=0)
    gradient = summed / (1.0 + own_denom)[:, None, None]
    rows = jnp.arange(blocksize, dtype=F32)
    placed = jnp.sum(jnp.where(got_pos[None, :] == rows[:, None], got_ev[None, :], 0.0), axis=1)
    return (gradient[None], placed)


def solution(mesh):
    return jax.shard_map(
        local,
        mesh=mesh,
        in_specs=(
            P("dp", None, None),
            P("dp"),
            P("cls", None, None),
            P(),
            P(),
            P("dp", None),
            P("cls"),
        ),
        out_specs=(P("cls", "dp", None, None), P("dp")),
        check_vma=False,
    )
```

```python
import math

import jax
import jax.numpy as jnp
from jax import lax
from jax.experimental import pallas as pl
from jax.experimental.pallas import tpu as pltpu
from jax.sharding import PartitionSpec as P

NSHELL = 64
NANG = 256
LIST = 2

HIGHEST = lax.Precision.HIGHEST
F32 = jnp.float32


def angular_tables(points):
    positions = jnp.arange(points, dtype=jnp.int32)
    product = positions[:, None] * positions[None, :] % points
    angles = product.astype(jnp.float32) * (2.0 * math.pi / points)
    cosine = jnp.cos(angles) / math.sqrt(points)
    sine_part = jnp.sin(angles) / math.sqrt(points)
    upper_half = jnp.concatenate([cosine, -sine_part], axis=1)
    lower_half = jnp.concatenate([sine_part, cosine], axis=1)
    return jnp.concatenate([upper_half, lower_half], axis=0)


CHUNK = 512


def cross_kernel(
    count_ref, ent_p_ref, ent_k_ref, image_ref, refs_ref, forward_ref, wrow_ref,
    cross_ref, image_hat_ref, ref_hat_ref, weighted_ref,
):
    forward = forward_ref[...]
    wrow = wrow_ref[...]

    def image_dft(c, carry):
        r = pl.multiple_of(c * CHUNK, CHUNK)
        image_hat_ref[pl.ds(r, CHUNK), :] = jnp.dot(
            image_ref[pl.ds(r, CHUNK), :], forward, preferred_element_type=F32
        ).astype(jnp.bfloat16)
        return carry

    def ref_dft(c, carry):
        r = pl.multiple_of(c * CHUNK, CHUNK)
        hat = jnp.dot(
            refs_ref[pl.ds(r, CHUNK), :], forward, preferred_element_type=F32
        ).astype(jnp.bfloat16)
        ref_hat_ref[pl.ds(r, CHUNK), :] = hat
        weighted_ref[pl.ds(r, CHUNK), :] = (hat.astype(F32) * wrow).astype(jnp.bfloat16)
        return carry

    lax.fori_loop(0, image_ref.shape[0] // CHUNK, image_dft, 0)
    lax.fori_loop(0, refs_ref.shape[0] // CHUNK, ref_dft, 0)
    cross_ref[...] = jnp.zeros_like(cross_ref)

    def body(e, carry):
        rp = pl.multiple_of(ent_p_ref[e] * NSHELL, NSHELL)
        rk = pl.multiple_of(ent_k_ref[e] * NSHELL, NSHELL)
        x = image_hat_ref[pl.ds(rp, NSHELL), :].astype(F32)
        w = weighted_ref[pl.ds(rk, NSHELL), :].astype(F32)
        x_re = x[:, :NANG]
        x_im = x[:, NANG:]
        w_re = w[:, :NANG]
        w_im = w[:, NANG:]
        c_re = jnp.sum(x_re * w_re + x_im * w_im, axis=0, keepdims=True)
        c_im = jnp.sum(x_im * w_re - x_re * w_im, axis=0, keepdims=True)
        cross_ref[pl.ds(e, 1), :] = jnp.concatenate([c_re, c_im], axis=1)
        return carry

    lax.fori_loop(0, count_ref[0], body, 0)


def grad_kernel(
    count_ref, ent_p_ref, ent_k_ref, image_hat_ref, coef_ref, ref_hat_ref, volume_ref,
    out_ref, acc_ref,
):
    def init(k, carry):
        r = pl.multiple_of(k * NSHELL, NSHELL)
        acc_ref[pl.ds(r, NSHELL), :] = -volume_ref[pl.ds(k, 1), :] * ref_hat_ref[
            pl.ds(r, NSHELL), :
        ].astype(F32)
        return carry

    lax.fori_loop(0, volume_ref.shape[0], init, 0)

    def body(e, carry):
        rp = pl.multiple_of(ent_p_ref[e] * NSHELL, NSHELL)
        rk = pl.multiple_of(ent_k_ref[e] * NSHELL, NSHELL)
        x = image_hat_ref[pl.ds(rp, NSHELL), :].astype(F32)
        c = coef_ref[pl.ds(e, 1), :]
        c_re = c[:, :NANG]
        c_im = c[:, NANG:]
        x_re = x[:, :NANG]
        x_im = x[:, NANG:]
        g_re = x_re * c_re - x_im * c_im
        g_im = x_re * c_im + x_im * c_re
        acc_ref[pl.ds(rk, NSHELL), :] = acc_ref[pl.ds(rk, NSHELL), :] + jnp.concatenate(
            [g_re, g_im], axis=1
        )
        return carry

    lax.fori_loop(0, count_ref[0], body, 0)

    def finish(c, carry):
        r = pl.multiple_of(c * CHUNK, CHUNK)
        out_ref[pl.ds(r, CHUNK), :] = acc_ref[pl.ds(r, CHUNK), :].astype(jnp.bfloat16)
        return carry

    lax.fori_loop(0, acc_ref.shape[0] // CHUNK, finish, 0)


def smem():
    return pl.BlockSpec(memory_space=pltpu.SMEM)


def vmem():
    return pl.BlockSpec(memory_space=pltpu.VMEM)


def local(
    images, pose_slot, references, rotation_response, shell_weight, class_lists, class_counts
):
    dp_index = lax.axis_index("dp")
    column = lax.axis_index("cls")
    dp_count = lax.axis_size("dp")
    blocksize = images.shape[0]
    col_classes = references.shape[0]
    per_owner = col_classes // dp_count
    per_pair = blocksize // dp_count
    row_width = 2 * NANG
    entries = blocksize * LIST
    full_table = angular_tables(NANG)
    forward = full_table.astype(jnp.bfloat16)
    inverse = full_table.T

    packed = jnp.concatenate([class_lists, pose_slot[:, None]], axis=1)
    all_packed = lax.all_to_all(
        jnp.broadcast_to(packed[None], (dp_count,) + packed.shape), "dp", 0, 0, tiled=True
    ).reshape(dp_count * blocksize, LIST + 1)
    all_lists = all_packed[:, :LIST]
    slot_hit = jnp.arange(all_lists.shape[0], dtype=jnp.int32)[None, :] == pose_slot[:, None]
    my_lists = jnp.stack(
        [jnp.sum(jnp.where(slot_hit, all_lists[None, :, a], 0), axis=1) for a in range(LIST)],
        axis=1,
    )
    local_class = (my_lists - column * col_classes).reshape(entries)
    inside = (local_class >= 0) & (local_class < col_classes)
    inside_i = inside.astype(jnp.int32)
    count = jnp.sum(inside_i)
    before_in = jnp.cumsum(inside_i) - inside_i
    before_out = jnp.cumsum(1 - inside_i) - (1 - inside_i)
    rank = jnp.where(inside, before_in, count + before_out)
    slots = jnp.arange(entries, dtype=jnp.int32)
    at_rank = rank[None, :] == slots[:, None]
    order = jnp.sum(jnp.where(at_rank, slots[None, :], 0), axis=1)
    safe_class = jnp.clip(local_class, 0, col_classes - 1)
    ent_p = order // LIST
    ent_k = jnp.sum(jnp.where(at_rank, safe_class[None, :], 0), axis=1)
    count_arr = count.reshape(1)

    image_rows = images.shape[0] * NSHELL
    ref_rows = col_classes * NSHELL
    wrow = jnp.tile(shell_weight, CHUNK // NSHELL)[:, None]
    params = pltpu.CompilerParams(vmem_limit_bytes=60 * 1024 * 1024)
    cross_c, image_hat, ref_hat = pl.pallas_call(
        cross_kernel,
        out_shape=(
            jax.ShapeDtypeStruct((entries, row_width), F32),
            jax.ShapeDtypeStruct((image_rows, row_width), jnp.bfloat16),
            jax.ShapeDtypeStruct((ref_rows, row_width), jnp.bfloat16),
        ),
        in_specs=[smem(), smem(), smem(), vmem(), vmem(), vmem(), vmem()],
        out_specs=(vmem(), vmem(), vmem()),
        scratch_shapes=[pltpu.VMEM((ref_rows, row_width), jnp.bfloat16)],
        compiler_params=params,
    )(
        count_arr, ent_p, ent_k, images.reshape(image_rows, row_width),
        references.reshape(ref_rows, row_width), forward, wrow,
    )

    log_prior = jnp.log1p(class_counts.astype(F32))
    prior = jnp.sum(
        jnp.where(safe_class[:, None] == jnp.arange(col_classes)[None, :], log_prior[None, :], 0.0),
        axis=1,
    )
    scores_c = jnp.dot(cross_c, rotation_response.T, precision=HIGHEST)
    scores = jnp.take(scores_c, rank, axis=0) + prior[:, None]
    scores = jnp.where(inside[:, None], scores, -1e30).reshape(blocksize, LIST, -1)
    inside_pa = inside.reshape(blocksize, LIST)
    top_local = jnp.max(scores, axis=(1, 2))
    total_local = jnp.sum(
        jnp.where(inside_pa[..., None], jnp.exp(scores - top_local[:, None, None]), 0.0), axis=(1, 2)
    )
    gathered = lax.all_gather(jnp.stack([top_local, total_local]), "cls")
    tops = gathered[:, 0]
    totals = gathered[:, 1]
    top_score = jnp.max(tops, axis=0)
    total_sum = jnp.sum(totals * jnp.exp(tops - top_score[None]), axis=0)
    posterior = (
        jnp.where(inside_pa[..., None], jnp.exp(scores - top_score[:, None, None]), 0.0)
        / total_sum[:, None, None]
    )
    evidence = top_score + jnp.log(total_sum)
    post_sum = jnp.sum(posterior, axis=2).reshape(entries)

    rot_re = rotation_response[:, :NANG]
    rot_im = rotation_response[:, NANG:]
    coef_table = jnp.concatenate([rot_re, -rot_im, rot_re * rot_re + rot_im * rot_im], axis=1)
    coef = jnp.dot(posterior.reshape(entries, -1), coef_table, precision=HIGHEST)
    coef_c = jnp.take(coef, order, axis=0)

    class_pick = (
        (local_class[None, :] == jnp.arange(col_classes, dtype=jnp.int32)[:, None]) & inside[None, :]
    ).astype(F32)
    volume = jnp.dot(class_pick, coef[:, row_width:], precision=HIGHEST)
    denom_part = jnp.dot(class_pick, post_sum, precision=HIGHEST)
    volume_full = jnp.concatenate([volume, volume], axis=1)
    numer = pl.pallas_call(
        grad_kernel,
        out_shape=jax.ShapeDtypeStruct((ref_rows, row_width), jnp.bfloat16),
        in_specs=[smem(), smem(), smem(), vmem(), vmem(), vmem(), vmem()],
        out_specs=vmem(),
        scratch_shapes=[pltpu.VMEM((ref_rows, row_width), F32)],
        compiler_params=params,
    )(count_arr, ent_p, ent_k, image_hat, coef_c[:, :row_width], ref_hat, volume_full)

    core = dp_index % 2
    by_core = numer.reshape(dp_count // 2, 2, per_owner, NSHELL, row_width)
    keep = lax.dynamic_index_in_dim(by_core, core, axis=1, keepdims=False)
    give = lax.dynamic_index_in_dim(by_core, 1 - core, axis=1, keepdims=False)
    taken = lax.ppermute(give, "dp", perm=[(i, i ^ 1) for i in range(dp_count)])
    pair_sum = (keep.astype(F32) + taken.astype(F32)).astype(jnp.bfloat16)
    groups = [list(range(q, dp_count, 2)) for q in range(2)]
    arrived = lax.all_to_all(
        pair_sum, "dp", split_axis=0, concat_axis=0, tiled=True, axis_index_groups=groups
    )
    summed = jnp.sum(arrived.astype(F32), axis=0)
    summed = jnp.dot(
        summed.reshape(-1, row_width), inverse, precision=HIGHEST
    ).reshape(summed.shape)

    dest = pose_slot // blocksize
    dest_hit = dest[None, :] == jnp.arange(dp_count, dtype=jnp.int32)[:, None]
    dest_i = dest_hit.astype(jnp.int32)
    within = jnp.sum((jnp.cumsum(dest_i, axis=1) - dest_i) * dest_i, axis=0)
    sel = dest_hit[:, None, :] & (
        within[None, None, :] == jnp.arange(per_pair, dtype=jnp.int32)[None, :, None]
    )
    send_ev = jnp.sum(jnp.where(sel, evidence[None, None, :], 0.0), axis=2)
    send_pos = jnp.sum(jnp.where(sel, (pose_slot % blocksize).astype(F32)[None, None, :], 0.0), axis=2)
    send_den = denom_part.reshape(dp_count, per_owner)
    small = jnp.concatenate([send_ev, send_pos, send_den], axis=1)
    got = lax.all_to_all(small, "dp", 0, 0, tiled=True)
    got_ev = got[:, :per_pair].reshape(-1)
    got_pos = got[:, per_pair : 2 * per_pair].reshape(-1)
    own_denom = jnp.sum(got[:, 2 * per_pair :], axis=0)
    gradient = summed / (1.0 + own_denom)[:, None, None]
    rows = jnp.arange(blocksize, dtype=F32)
    placed = jnp.sum(jnp.where(got_pos[None, :] == rows[:, None], got_ev[None, :], 0.0), axis=1)
    return (gradient[None], placed)


def solution(mesh):
    return jax.shard_map(
        local,
        mesh=mesh,
        in_specs=(
            P("dp", None, None),
            P("dp"),
            P("cls", None, None),
            P(),
            P(),
            P("dp", None),
            P("cls"),
        ),
        out_specs=(P("cls", "dp", None, None), P("dp")),
        check_vma=False,
    )
```

```python
import math

import jax
import jax.numpy as jnp
from jax import lax
from jax.experimental import pallas as pl
from jax.experimental.pallas import tpu as pltpu
from jax.sharding import PartitionSpec as P

NSHELL = 64
NANG = 256
LIST = 2

HIGHEST = lax.Precision.HIGHEST
F32 = jnp.float32


def angular_tables(points):
    positions = jnp.arange(points, dtype=jnp.int32)
    product = positions[:, None] * positions[None, :] % points
    angles = product.astype(jnp.float32) * (2.0 * math.pi / points)
    cosine = jnp.cos(angles) / math.sqrt(points)
    sine_part = jnp.sin(angles) / math.sqrt(points)
    upper_half = jnp.concatenate([cosine, -sine_part], axis=1)
    lower_half = jnp.concatenate([sine_part, cosine], axis=1)
    return jnp.concatenate([upper_half, lower_half], axis=0)


CHUNK = 512


ROWS = 1024


def image_dft_kernel(image_ref, forward_ref, out_ref):
    out_ref[...] = jnp.dot(
        image_ref[...], forward_ref[...], preferred_element_type=F32
    ).astype(jnp.bfloat16)


def ref_dft_kernel(refs_ref, forward_ref, wrow_ref, hat_ref, weighted_ref):
    hat = jnp.dot(refs_ref[...], forward_ref[...], preferred_element_type=F32).astype(jnp.bfloat16)
    hat_ref[...] = hat
    weighted_ref[...] = (hat.astype(F32) * wrow_ref[...]).astype(jnp.bfloat16)


def cross_kernel(count_ref, ent_p_ref, ent_k_ref, image_hat_ref, weighted_ref, cross_ref):
    cross_ref[...] = jnp.zeros_like(cross_ref)

    def body(e, carry):
        rp = pl.multiple_of(ent_p_ref[e] * NSHELL, NSHELL)
        rk = pl.multiple_of(ent_k_ref[e] * NSHELL, NSHELL)
        x = image_hat_ref[pl.ds(rp, NSHELL), :].astype(F32)
        w = weighted_ref[pl.ds(rk, NSHELL), :].astype(F32)
        x_re = x[:, :NANG]
        x_im = x[:, NANG:]
        w_re = w[:, :NANG]
        w_im = w[:, NANG:]
        c_re = jnp.sum(x_re * w_re + x_im * w_im, axis=0, keepdims=True)
        c_im = jnp.sum(x_im * w_re - x_re * w_im, axis=0, keepdims=True)
        cross_ref[pl.ds(e, 1), :] = jnp.concatenate([c_re, c_im], axis=1)
        return carry

    lax.fori_loop(0, count_ref[0], body, 0)


def grad_kernel(
    count_ref, ent_p_ref, ent_k_ref, image_hat_ref, coef_ref, ref_hat_ref, volume_ref,
    out_ref, acc_ref,
):
    def init(k, carry):
        r = pl.multiple_of(k * NSHELL, NSHELL)
        acc_ref[pl.ds(r, NSHELL), :] = -volume_ref[pl.ds(k, 1), :] * ref_hat_ref[
            pl.ds(r, NSHELL), :
        ].astype(F32)
        return carry

    lax.fori_loop(0, volume_ref.shape[0], init, 0)

    def body(e, carry):
        rp = pl.multiple_of(ent_p_ref[e] * NSHELL, NSHELL)
        rk = pl.multiple_of(ent_k_ref[e] * NSHELL, NSHELL)
        x = image_hat_ref[pl.ds(rp, NSHELL), :].astype(F32)
        c = coef_ref[pl.ds(e, 1), :]
        c_re = c[:, :NANG]
        c_im = c[:, NANG:]
        x_re = x[:, :NANG]
        x_im = x[:, NANG:]
        g_re = x_re * c_re - x_im * c_im
        g_im = x_re * c_im + x_im * c_re
        acc_ref[pl.ds(rk, NSHELL), :] = acc_ref[pl.ds(rk, NSHELL), :] + jnp.concatenate(
            [g_re, g_im], axis=1
        )
        return carry

    lax.fori_loop(0, count_ref[0], body, 0)

    def finish(c, carry):
        r = pl.multiple_of(c * CHUNK, CHUNK)
        out_ref[pl.ds(r, CHUNK), :] = acc_ref[pl.ds(r, CHUNK), :].astype(jnp.bfloat16)
        return carry

    lax.fori_loop(0, acc_ref.shape[0] // CHUNK, finish, 0)


def smem():
    return pl.BlockSpec(memory_space=pltpu.SMEM)


def vmem():
    return pl.BlockSpec(memory_space=pltpu.VMEM)


def local(
    images, pose_slot, references, rotation_response, shell_weight, class_lists, class_counts
):
    dp_index = lax.axis_index("dp")
    column = lax.axis_index("cls")
    dp_count = lax.axis_size("dp")
    blocksize = images.shape[0]
    col_classes = references.shape[0]
    per_owner = col_classes // dp_count
    per_pair = blocksize // dp_count
    row_width = 2 * NANG
    entries = blocksize * LIST
    full_table = angular_tables(NANG)
    forward = full_table.astype(jnp.bfloat16)
    inverse = full_table.T

    packed = jnp.concatenate([class_lists, pose_slot[:, None]], axis=1)
    all_packed = lax.all_to_all(
        jnp.broadcast_to(packed[None], (dp_count,) + packed.shape), "dp", 0, 0, tiled=True
    ).reshape(dp_count * blocksize, LIST + 1)
    all_lists = all_packed[:, :LIST]
    slot_hit = jnp.arange(all_lists.shape[0], dtype=jnp.int32)[None, :] == pose_slot[:, None]
    my_lists = jnp.stack(
        [jnp.sum(jnp.where(slot_hit, all_lists[None, :, a], 0), axis=1) for a in range(LIST)],
        axis=1,
    )
    local_class = (my_lists - column * col_classes).reshape(entries)
    inside = (local_class >= 0) & (local_class < col_classes)
    inside_i = inside.astype(jnp.int32)
    count = jnp.sum(inside_i)
    before_in = jnp.cumsum(inside_i) - inside_i
    before_out = jnp.cumsum(1 - inside_i) - (1 - inside_i)
    rank = jnp.where(inside, before_in, count + before_out)
    slots = jnp.arange(entries, dtype=jnp.int32)
    at_rank = rank[None, :] == slots[:, None]
    order = jnp.sum(jnp.where(at_rank, slots[None, :], 0), axis=1)
    safe_class = jnp.clip(local_class, 0, col_classes - 1)
    ent_p = order // LIST
    ent_k = jnp.sum(jnp.where(at_rank, safe_class[None, :], 0), axis=1)
    count_arr = count.reshape(1)

    image_rows = images.shape[0] * NSHELL
    ref_rows = col_classes * NSHELL
    wrow = jnp.tile(shell_weight, ROWS // NSHELL)[:, None]
    params = pltpu.CompilerParams(vmem_limit_bytes=60 * 1024 * 1024)
    row_block = pl.BlockSpec((ROWS, row_width), lambda i: (i, 0))
    table_block = pl.BlockSpec((row_width, row_width), lambda i: (0, 0))
    image_hat = pl.pallas_call(
        image_dft_kernel,
        out_shape=jax.ShapeDtypeStruct((image_rows, row_width), jnp.bfloat16),
        grid=(image_rows // ROWS,),
        in_specs=[row_block, table_block],
        out_specs=row_block,
    )(images.reshape(image_rows, row_width), forward)
    ref_hat, weighted = pl.pallas_call(
        ref_dft_kernel,
        out_shape=(
            jax.ShapeDtypeStruct((ref_rows, row_width), jnp.bfloat16),
            jax.ShapeDtypeStruct((ref_rows, row_width), jnp.bfloat16),
        ),
        grid=(ref_rows // ROWS,),
        in_specs=[row_block, table_block, pl.BlockSpec((ROWS, 1), lambda i: (0, 0))],
        out_specs=(row_block, row_block),
    )(references.reshape(ref_rows, row_width), forward, wrow)
    cross_c = pl.pallas_call(
        cross_kernel,
        out_shape=jax.ShapeDtypeStruct((entries, row_width), F32),
        in_specs=[smem(), smem(), smem(), vmem(), vmem()],
        out_specs=vmem(),
        compiler_params=params,
    )(count_arr, ent_p, ent_k, image_hat, weighted)

    log_prior = jnp.log1p(class_counts.astype(F32))
    prior = jnp.sum(
        jnp.where(safe_class[:, None] == jnp.arange(col_classes)[None, :], log_prior[None, :], 0.0),
        axis=1,
    )
    scores_c = jnp.dot(cross_c, rotation_response.T, precision=HIGHEST)
    scores = jnp.take(scores_c, rank, axis=0) + prior[:, None]
    scores = jnp.where(inside[:, None], scores, -1e30).reshape(blocksize, LIST, -1)
    inside_pa = inside.reshape(blocksize, LIST)
    top_local = jnp.max(scores, axis=(1, 2))
    total_local = jnp.sum(
        jnp.where(inside_pa[..., None], jnp.exp(scores - top_local[:, None, None]), 0.0), axis=(1, 2)
    )
    gathered = lax.all_gather(jnp.stack([top_local, total_local]), "cls")
    tops = gathered[:, 0]
    totals = gathered[:, 1]
    top_score = jnp.max(tops, axis=0)
    total_sum = jnp.sum(totals * jnp.exp(tops - top_score[None]), axis=0)
    posterior = (
        jnp.where(inside_pa[..., None], jnp.exp(scores - top_score[:, None, None]), 0.0)
        / total_sum[:, None, None]
    )
    evidence = top_score + jnp.log(total_sum)
    post_sum = jnp.sum(posterior, axis=2).reshape(entries)

    rot_re = rotation_response[:, :NANG]
    rot_im = rotation_response[:, NANG:]
    coef_table = jnp.concatenate([rot_re, -rot_im, rot_re * rot_re + rot_im * rot_im], axis=1)
    coef = jnp.dot(posterior.reshape(entries, -1), coef_table, precision=HIGHEST)
    coef_c = jnp.take(coef, order, axis=0)

    class_pick = (
        (local_class[None, :] == jnp.arange(col_classes, dtype=jnp.int32)[:, None]) & inside[None, :]
    ).astype(F32)
    volume = jnp.dot(class_pick, coef[:, row_width:], precision=HIGHEST)
    denom_part = jnp.dot(class_pick, post_sum, precision=HIGHEST)
    volume_full = jnp.concatenate([volume, volume], axis=1)
    numer = pl.pallas_call(
        grad_kernel,
        out_shape=jax.ShapeDtypeStruct((ref_rows, row_width), jnp.bfloat16),
        in_specs=[smem(), smem(), smem(), vmem(), vmem(), vmem(), vmem()],
        out_specs=vmem(),
        scratch_shapes=[pltpu.VMEM((ref_rows, row_width), F32)],
        compiler_params=params,
    )(count_arr, ent_p, ent_k, image_hat, coef_c[:, :row_width], ref_hat, volume_full)

    core = dp_index % 2
    by_core = numer.reshape(dp_count // 2, 2, per_owner, NSHELL, row_width)
    keep = lax.dynamic_index_in_dim(by_core, core, axis=1, keepdims=False)
    give = lax.dynamic_index_in_dim(by_core, 1 - core, axis=1, keepdims=False)
    taken = lax.ppermute(give, "dp", perm=[(i, i ^ 1) for i in range(dp_count)])
    pair_sum = (keep.astype(F32) + taken.astype(F32)).astype(jnp.bfloat16)
    groups = [list(range(q, dp_count, 2)) for q in range(2)]
    arrived = lax.all_to_all(
        pair_sum, "dp", split_axis=0, concat_axis=0, tiled=True, axis_index_groups=groups
    )
    summed = jnp.sum(arrived.astype(F32), axis=0)
    summed = jnp.dot(
        summed.reshape(-1, row_width), inverse, precision=HIGHEST
    ).reshape(summed.shape)

    dest = pose_slot // blocksize
    dest_hit = dest[None, :] == jnp.arange(dp_count, dtype=jnp.int32)[:, None]
    dest_i = dest_hit.astype(jnp.int32)
    within = jnp.sum((jnp.cumsum(dest_i, axis=1) - dest_i) * dest_i, axis=0)
    sel = dest_hit[:, None, :] & (
        within[None, None, :] == jnp.arange(per_pair, dtype=jnp.int32)[None, :, None]
    )
    send_ev = jnp.sum(jnp.where(sel, evidence[None, None, :], 0.0), axis=2)
    send_pos = jnp.sum(jnp.where(sel, (pose_slot % blocksize).astype(F32)[None, None, :], 0.0), axis=2)
    send_den = denom_part.reshape(dp_count, per_owner)
    small = jnp.concatenate([send_ev, send_pos, send_den], axis=1)
    got = lax.all_to_all(small, "dp", 0, 0, tiled=True)
    got_ev = got[:, :per_pair].reshape(-1)
    got_pos = got[:, per_pair : 2 * per_pair].reshape(-1)
    own_denom = jnp.sum(got[:, 2 * per_pair :], axis=0)
    gradient = summed / (1.0 + own_denom)[:, None, None]
    rows = jnp.arange(blocksize, dtype=F32)
    placed = jnp.sum(jnp.where(got_pos[None, :] == rows[:, None], got_ev[None, :], 0.0), axis=1)
    return (gradient[None], placed)


def solution(mesh):
    return jax.shard_map(
        local,
        mesh=mesh,
        in_specs=(
            P("dp", None, None),
            P("dp"),
            P("cls", None, None),
            P(),
            P(),
            P("dp", None),
            P("cls"),
        ),
        out_specs=(P("cls", "dp", None, None), P("dp")),
        check_vma=False,
    )
```

```python
import math

import jax
import jax.numpy as jnp
from jax import lax
from jax.experimental import pallas as pl
from jax.experimental.pallas import tpu as pltpu
from jax.sharding import PartitionSpec as P

NSHELL = 64
NANG = 256
LIST = 2

HIGHEST = lax.Precision.HIGHEST
F32 = jnp.float32


def angular_tables(points):
    positions = jnp.arange(points, dtype=jnp.int32)
    product = positions[:, None] * positions[None, :] % points
    angles = product.astype(jnp.float32) * (2.0 * math.pi / points)
    cosine = jnp.cos(angles) / math.sqrt(points)
    sine_part = jnp.sin(angles) / math.sqrt(points)
    upper_half = jnp.concatenate([cosine, -sine_part], axis=1)
    lower_half = jnp.concatenate([sine_part, cosine], axis=1)
    return jnp.concatenate([upper_half, lower_half], axis=0)


CHUNK = 512
EXTRA = 16


def cross_kernel(
    count_ref, ent_p_ref, ent_k_ref, image_ref, refs_ref, forward_ref, wrow_ref,
    cross_ref, image_hat_ref, ref_hat_ref, weighted_ref,
):
    forward = forward_ref[...]
    wrow = wrow_ref[...]

    def image_dft(c, carry):
        r = pl.multiple_of(c * CHUNK, CHUNK)
        image_hat_ref[pl.ds(r, CHUNK), :] = jnp.dot(
            image_ref[pl.ds(r, CHUNK), :], forward, preferred_element_type=F32
        ).astype(jnp.bfloat16)
        return carry

    def ref_dft(c, carry):
        r = pl.multiple_of(c * CHUNK, CHUNK)
        hat = jnp.dot(
            refs_ref[pl.ds(r, CHUNK), :], forward, preferred_element_type=F32
        ).astype(jnp.bfloat16)
        ref_hat_ref[pl.ds(r, CHUNK), :] = hat
        weighted_ref[pl.ds(r, CHUNK), :] = (hat.astype(F32) * wrow).astype(jnp.bfloat16)
        return carry

    lax.fori_loop(0, image_ref.shape[0] // CHUNK, image_dft, 0)
    lax.fori_loop(0, refs_ref.shape[0] // CHUNK, ref_dft, 0)
    cross_ref[...] = jnp.zeros_like(cross_ref)

    def body(e, carry):
        rp = pl.multiple_of(ent_p_ref[e] * NSHELL, NSHELL)
        rk = pl.multiple_of(ent_k_ref[e] * NSHELL, NSHELL)
        x = image_hat_ref[pl.ds(rp, NSHELL), :].astype(F32)
        w = weighted_ref[pl.ds(rk, NSHELL), :].astype(F32)
        x_re = x[:, :NANG]
        x_im = x[:, NANG:]
        w_re = w[:, :NANG]
        w_im = w[:, NANG:]
        c_re = jnp.sum(x_re * w_re + x_im * w_im, axis=0, keepdims=True)
        c_im = jnp.sum(x_im * w_re - x_re * w_im, axis=0, keepdims=True)
        cross_ref[pl.ds(e, 1), :] = jnp.concatenate([c_re, c_im], axis=1)
        return carry

    lax.fori_loop(0, count_ref[0], body, 0)


def grad_kernel(
    count_ref, ent_p_ref, ent_k_ref, image_hat_ref, coef_ref, ref_hat_ref, volume_ref,
    out_ref, acc_ref,
):
    def init(k, carry):
        r = pl.multiple_of(k * NSHELL, NSHELL)
        acc_ref[pl.ds(r, NSHELL), :] = -volume_ref[pl.ds(k, 1), :] * ref_hat_ref[
            pl.ds(r, NSHELL), :
        ].astype(F32)
        return carry

    lax.fori_loop(0, volume_ref.shape[0], init, 0)

    def body(e, carry):
        rp = pl.multiple_of(ent_p_ref[e] * NSHELL, NSHELL)
        rk = pl.multiple_of(ent_k_ref[e] * NSHELL, NSHELL)
        x = image_hat_ref[pl.ds(rp, NSHELL), :].astype(F32)
        c = coef_ref[pl.ds(e, 1), :]
        c_re = c[:, :NANG]
        c_im = c[:, NANG:]
        x_re = x[:, :NANG]
        x_im = x[:, NANG:]
        g_re = x_re * c_re - x_im * c_im
        g_im = x_re * c_im + x_im * c_re
        acc_ref[pl.ds(rk, NSHELL), :] = acc_ref[pl.ds(rk, NSHELL), :] + jnp.concatenate(
            [g_re, g_im], axis=1
        )
        return carry

    lax.fori_loop(0, count_ref[0], body, 0)

    def finish(c, carry):
        r = pl.multiple_of(c * CHUNK, CHUNK)
        out_ref[pl.ds(r, CHUNK), :] = acc_ref[pl.ds(r, CHUNK), :].astype(jnp.bfloat16)
        return carry

    lax.fori_loop(0, acc_ref.shape[0] // CHUNK, finish, 0)


def split_pair(x):
    high = x.astype(jnp.bfloat16)
    low = (x - high.astype(F32)).astype(jnp.bfloat16)
    return high, low


def smem():
    return pl.BlockSpec(memory_space=pltpu.SMEM)


def vmem():
    return pl.BlockSpec(memory_space=pltpu.VMEM)


def local(
    images, pose_slot, references, rotation_response, shell_weight, class_lists, class_counts
):
    dp_index = lax.axis_index("dp")
    column = lax.axis_index("cls")
    dp_count = lax.axis_size("dp")
    blocksize = images.shape[0]
    col_classes = references.shape[0]
    per_owner = col_classes // dp_count
    per_pair = blocksize // dp_count
    row_width = 2 * NANG
    entries = blocksize * LIST
    full_table = angular_tables(NANG)
    forward = full_table.astype(jnp.bfloat16)
    inverse = full_table.T

    packed = jnp.concatenate([class_lists, pose_slot[:, None]], axis=1)
    all_packed = lax.all_to_all(
        jnp.broadcast_to(packed[None], (dp_count,) + packed.shape), "dp", 0, 0, tiled=True
    ).reshape(dp_count * blocksize, LIST + 1)
    all_lists = all_packed[:, :LIST]
    slot_hit = jnp.arange(all_lists.shape[0], dtype=jnp.int32)[None, :] == pose_slot[:, None]
    my_lists = jnp.stack(
        [jnp.sum(jnp.where(slot_hit, all_lists[None, :, a], 0), axis=1) for a in range(LIST)],
        axis=1,
    )
    local_class = (my_lists - column * col_classes).reshape(entries)
    inside = (local_class >= 0) & (local_class < col_classes)
    inside_i = inside.astype(jnp.int32)
    count = jnp.sum(inside_i)
    before_in = jnp.cumsum(inside_i) - inside_i
    before_out = jnp.cumsum(1 - inside_i) - (1 - inside_i)
    rank = jnp.where(inside, before_in, count + before_out)
    slots = jnp.arange(entries, dtype=jnp.int32)
    at_rank = rank[None, :] == slots[:, None]
    order = jnp.sum(jnp.where(at_rank, slots[None, :], 0), axis=1)
    safe_class = jnp.clip(local_class, 0, col_classes - 1)
    ent_p = order // LIST
    ent_k = jnp.sum(jnp.where(at_rank, safe_class[None, :], 0), axis=1)
    count_arr = count.reshape(1)

    image_rows = images.shape[0] * NSHELL
    ref_rows = col_classes * NSHELL
    wrow = jnp.tile(shell_weight, CHUNK // NSHELL)[:, None]
    params = pltpu.CompilerParams(vmem_limit_bytes=60 * 1024 * 1024)
    cross_c, image_hat, ref_hat = pl.pallas_call(
        cross_kernel,
        out_shape=(
            jax.ShapeDtypeStruct((entries, row_width), F32),
            jax.ShapeDtypeStruct((image_rows, row_width), jnp.bfloat16),
            jax.ShapeDtypeStruct((ref_rows, row_width), jnp.bfloat16),
        ),
        in_specs=[smem(), smem(), smem(), vmem(), vmem(), vmem(), vmem()],
        out_specs=(vmem(), vmem(), vmem()),
        scratch_shapes=[pltpu.VMEM((ref_rows, row_width), jnp.bfloat16)],
        compiler_params=params,
    )(
        count_arr, ent_p, ent_k, images.reshape(image_rows, row_width),
        references.reshape(ref_rows, row_width), forward, wrow,
    )

    log_prior = jnp.log1p(class_counts.astype(F32))
    prior = jnp.sum(
        jnp.where(safe_class[:, None] == jnp.arange(col_classes)[None, :], log_prior[None, :], 0.0),
        axis=1,
    )
    scores_c = jnp.dot(cross_c, rotation_response.T, precision=HIGHEST)
    scores = jnp.take(scores_c, rank, axis=0) + prior[:, None]
    scores = jnp.where(inside[:, None], scores, -1e30).reshape(blocksize, LIST, -1)
    inside_pa = inside.reshape(blocksize, LIST)
    top_local = jnp.max(scores, axis=(1, 2))
    total_local = jnp.sum(
        jnp.where(inside_pa[..., None], jnp.exp(scores - top_local[:, None, None]), 0.0), axis=(1, 2)
    )
    gathered = lax.all_gather(jnp.stack([top_local, total_local]), "cls")
    tops = gathered[:, 0]
    totals = gathered[:, 1]
    top_score = jnp.max(tops, axis=0)
    total_sum = jnp.sum(totals * jnp.exp(tops - top_score[None]), axis=0)
    posterior = (
        jnp.where(inside_pa[..., None], jnp.exp(scores - top_score[:, None, None]), 0.0)
        / total_sum[:, None, None]
    )
    evidence = top_score + jnp.log(total_sum)
    post_sum = jnp.sum(posterior, axis=2).reshape(entries)

    rot_re = rotation_response[:, :NANG]
    rot_im = rotation_response[:, NANG:]
    coef_table = jnp.concatenate([rot_re, -rot_im, rot_re * rot_re + rot_im * rot_im], axis=1)
    coef = jnp.dot(posterior.reshape(entries, -1), coef_table, precision=HIGHEST)
    coef_c = jnp.take(coef, order, axis=0)

    class_pick = (
        (local_class[None, :] == jnp.arange(col_classes, dtype=jnp.int32)[:, None]) & inside[None, :]
    ).astype(F32)
    volume = jnp.dot(class_pick, coef[:, row_width:], precision=HIGHEST)
    denom_part = jnp.dot(class_pick, post_sum, precision=HIGHEST)
    volume_full = jnp.concatenate([volume, volume], axis=1)
    numer = pl.pallas_call(
        grad_kernel,
        out_shape=jax.ShapeDtypeStruct((ref_rows, row_width), jnp.bfloat16),
        in_specs=[smem(), smem(), smem(), vmem(), vmem(), vmem(), vmem()],
        out_specs=vmem(),
        scratch_shapes=[pltpu.VMEM((ref_rows, row_width), F32)],
        compiler_params=params,
    )(count_arr, ent_p, ent_k, image_hat, coef_c[:, :row_width], ref_hat, volume_full)

    core = dp_index % 2
    dest = pose_slot // blocksize
    dest_hit = dest[None, :] == jnp.arange(dp_count, dtype=jnp.int32)[:, None]
    dest_i = dest_hit.astype(jnp.int32)
    within = jnp.sum((jnp.cumsum(dest_i, axis=1) - dest_i) * dest_i, axis=0)
    sel = dest_hit[:, None, :] & (
        within[None, None, :] == jnp.arange(per_pair, dtype=jnp.int32)[None, :, None]
    )
    send_ev = jnp.sum(jnp.where(sel, evidence[None, None, :], 0.0), axis=2)
    send_pos = jnp.sum(jnp.where(sel, (pose_slot % blocksize).astype(F32)[None, None, :], 0.0), axis=2)
    send_den = denom_part.reshape(dp_count, per_owner)
    ev_hi, ev_lo = split_pair(send_ev)
    den_hi, den_lo = split_pair(send_den)
    small = jnp.concatenate(
        [ev_hi, ev_lo, send_pos.astype(jnp.bfloat16), den_hi, den_lo], axis=1
    )
    slot_w = small.shape[1]
    small_row = lax.dynamic_update_slice(
        jnp.zeros((dp_count, row_width), jnp.bfloat16), small, (0, core * slot_w)
    )
    extra = jnp.zeros((dp_count, EXTRA, row_width), jnp.bfloat16).at[:, 0, :].set(small_row)
    chunk_rows = per_owner * NSHELL
    chunks = jnp.concatenate(
        [numer.reshape(dp_count, chunk_rows, row_width), extra], axis=1
    )

    by_core = chunks.reshape(dp_count // 2, 2, chunk_rows + EXTRA, row_width)
    keep = lax.dynamic_index_in_dim(by_core, core, axis=1, keepdims=False)
    give = lax.dynamic_index_in_dim(by_core, 1 - core, axis=1, keepdims=False)
    taken = lax.ppermute(give, "dp", perm=[(i, i ^ 1) for i in range(dp_count)])
    pair_sum = (keep.astype(F32) + taken.astype(F32)).astype(jnp.bfloat16)
    groups = [list(range(q, dp_count, 2)) for q in range(2)]
    arrived = lax.all_to_all(
        pair_sum, "dp", split_axis=0, concat_axis=0, tiled=True, axis_index_groups=groups
    )
    summed = jnp.sum(arrived[:, :chunk_rows].astype(F32), axis=0)
    summed = jnp.dot(summed, inverse, precision=HIGHEST).reshape(per_owner, NSHELL, row_width)

    got = arrived[:, chunk_rows, : 2 * slot_w].astype(F32).reshape(dp_count, slot_w)
    got_ev = (got[:, :per_pair] + got[:, per_pair : 2 * per_pair]).reshape(-1)
    got_pos = got[:, 2 * per_pair : 3 * per_pair].reshape(-1)
    den_at = 3 * per_pair
    own_denom = jnp.sum(
        got[:, den_at : den_at + per_owner] + got[:, den_at + per_owner : den_at + 2 * per_owner],
        axis=0,
    )
    gradient = summed / (1.0 + own_denom)[:, None, None]
    rows = jnp.arange(blocksize, dtype=F32)
    placed = jnp.sum(jnp.where(got_pos[None, :] == rows[:, None], got_ev[None, :], 0.0), axis=1)
    return (gradient[None], placed)


def solution(mesh):
    return jax.shard_map(
        local,
        mesh=mesh,
        in_specs=(
            P("dp", None, None),
            P("dp"),
            P("cls", None, None),
            P(),
            P(),
            P("dp", None),
            P("cls"),
        ),
        out_specs=(P("cls", "dp", None, None), P("dp")),
        check_vma=False,
    )
```

```python
import math

import jax
import jax.numpy as jnp
from jax import lax
from jax.experimental import pallas as pl
from jax.experimental.pallas import tpu as pltpu
from jax.sharding import PartitionSpec as P

NSHELL = 64
NANG = 256
LIST = 2

HIGHEST = lax.Precision.HIGHEST
F32 = jnp.float32


def angular_tables(points):
    positions = jnp.arange(points, dtype=jnp.int32)
    product = positions[:, None] * positions[None, :] % points
    angles = product.astype(jnp.float32) * (2.0 * math.pi / points)
    cosine = jnp.cos(angles) / math.sqrt(points)
    sine_part = jnp.sin(angles) / math.sqrt(points)
    upper_half = jnp.concatenate([cosine, -sine_part], axis=1)
    lower_half = jnp.concatenate([sine_part, cosine], axis=1)
    return jnp.concatenate([upper_half, lower_half], axis=0)


CHUNK = 512
EXTRA = 16


def cross_kernel(
    count_ref, ent_p_ref, ent_k_ref, image_ref, refs_ref, forward_ref, wrow_ref,
    cross_ref, image_hat_ref, ref_hat_ref, weighted_ref,
):
    forward = forward_ref[...]
    wrow = wrow_ref[...]

    def image_dft(c, carry):
        r = pl.multiple_of(c * CHUNK, CHUNK)
        image_hat_ref[pl.ds(r, CHUNK), :] = jnp.dot(
            image_ref[pl.ds(r, CHUNK), :], forward, preferred_element_type=F32
        ).astype(jnp.bfloat16)
        return carry

    def ref_dft(c, carry):
        r = pl.multiple_of(c * CHUNK, CHUNK)
        hat = jnp.dot(
            refs_ref[pl.ds(r, CHUNK), :], forward, preferred_element_type=F32
        ).astype(jnp.bfloat16)
        ref_hat_ref[pl.ds(r, CHUNK), :] = hat
        weighted_ref[pl.ds(r, CHUNK), :] = (hat.astype(F32) * wrow).astype(jnp.bfloat16)
        return carry

    lax.fori_loop(0, image_ref.shape[0] // CHUNK, image_dft, 0)
    lax.fori_loop(0, refs_ref.shape[0] // CHUNK, ref_dft, 0)
    cross_ref[...] = jnp.zeros_like(cross_ref)

    def body(e, carry):
        rp = pl.multiple_of(ent_p_ref[e] * NSHELL, NSHELL)
        rk = pl.multiple_of(ent_k_ref[e] * NSHELL, NSHELL)
        x = image_hat_ref[pl.ds(rp, NSHELL), :].astype(F32)
        w = weighted_ref[pl.ds(rk, NSHELL), :].astype(F32)
        x_re = x[:, :NANG]
        x_im = x[:, NANG:]
        w_re = w[:, :NANG]
        w_im = w[:, NANG:]
        c_re = jnp.sum(x_re * w_re + x_im * w_im, axis=0, keepdims=True)
        c_im = jnp.sum(x_im * w_re - x_re * w_im, axis=0, keepdims=True)
        cross_ref[pl.ds(e, 1), :] = jnp.concatenate([c_re, c_im], axis=1)
        return carry

    lax.fori_loop(0, count_ref[0], body, 0)


def grad_kernel(
    count_ref, ent_p_ref, ent_k_ref, image_hat_ref, coef_ref, ref_hat_ref, volume_ref,
    out_ref, acc_ref,
):
    def init(k, carry):
        r = pl.multiple_of(k * NSHELL, NSHELL)
        acc_ref[pl.ds(r, NSHELL), :] = -volume_ref[pl.ds(k, 1), :] * ref_hat_ref[
            pl.ds(r, NSHELL), :
        ].astype(F32)
        return carry

    lax.fori_loop(0, volume_ref.shape[0], init, 0)

    def body(e, carry):
        rp = pl.multiple_of(ent_p_ref[e] * NSHELL, NSHELL)
        rk = pl.multiple_of(ent_k_ref[e] * NSHELL, NSHELL)
        x = image_hat_ref[pl.ds(rp, NSHELL), :].astype(F32)
        c = coef_ref[pl.ds(e, 1), :]
        c_re = c[:, :NANG]
        c_im = c[:, NANG:]
        x_re = x[:, :NANG]
        x_im = x[:, NANG:]
        g_re = x_re * c_re - x_im * c_im
        g_im = x_re * c_im + x_im * c_re
        acc_ref[pl.ds(rk, NSHELL), :] = acc_ref[pl.ds(rk, NSHELL), :] + jnp.concatenate(
            [g_re, g_im], axis=1
        )
        return carry

    lax.fori_loop(0, count_ref[0], body, 0)

    def finish(c, carry):
        r = pl.multiple_of(c * CHUNK, CHUNK)
        out_ref[pl.ds(r, CHUNK), :] = acc_ref[pl.ds(r, CHUNK), :].astype(jnp.bfloat16)
        return carry

    lax.fori_loop(0, acc_ref.shape[0] // CHUNK, finish, 0)


def split_pair(x):
    high = x.astype(jnp.bfloat16)
    low = (x - high.astype(F32)).astype(jnp.bfloat16)
    return high, low


def smem():
    return pl.BlockSpec(memory_space=pltpu.SMEM)


def vmem():
    return pl.BlockSpec(memory_space=pltpu.VMEM)


def local(
    images, pose_slot, references, rotation_response, shell_weight, class_lists, class_counts
):
    dp_index = lax.axis_index("dp")
    column = lax.axis_index("cls")
    dp_count = lax.axis_size("dp")
    blocksize = images.shape[0]
    col_classes = references.shape[0]
    per_owner = col_classes // dp_count
    per_pair = blocksize // dp_count
    row_width = 2 * NANG
    entries = blocksize * LIST
    full_table = angular_tables(NANG)
    forward = full_table.astype(jnp.bfloat16)
    inverse = full_table.T

    packed = jnp.concatenate([class_lists, pose_slot[:, None]], axis=1)
    all_packed = lax.all_to_all(
        jnp.broadcast_to(packed[None], (dp_count,) + packed.shape), "dp", 0, 0, tiled=True
    ).reshape(dp_count * blocksize, LIST + 1)
    all_lists = all_packed[:, :LIST]
    slot_hit = jnp.arange(all_lists.shape[0], dtype=jnp.int32)[None, :] == pose_slot[:, None]
    my_lists = jnp.stack(
        [jnp.sum(jnp.where(slot_hit, all_lists[None, :, a], 0), axis=1) for a in range(LIST)],
        axis=1,
    )
    local_class = (my_lists - column * col_classes).reshape(entries)
    inside = (local_class >= 0) & (local_class < col_classes)
    inside_i = inside.astype(jnp.int32)
    count = jnp.sum(inside_i)
    before_in = jnp.cumsum(inside_i) - inside_i
    before_out = jnp.cumsum(1 - inside_i) - (1 - inside_i)
    rank = jnp.where(inside, before_in, count + before_out)
    slots = jnp.arange(entries, dtype=jnp.int32)
    at_rank = rank[None, :] == slots[:, None]
    order = jnp.sum(jnp.where(at_rank, slots[None, :], 0), axis=1)
    safe_class = jnp.clip(local_class, 0, col_classes - 1)
    ent_p = order // LIST
    ent_k = jnp.sum(jnp.where(at_rank, safe_class[None, :], 0), axis=1)
    count_arr = count.reshape(1)

    image_rows = images.shape[0] * NSHELL
    ref_rows = col_classes * NSHELL
    wrow = jnp.tile(shell_weight, CHUNK // NSHELL)[:, None]
    params = pltpu.CompilerParams(vmem_limit_bytes=60 * 1024 * 1024)
    cross_c, image_hat, ref_hat = pl.pallas_call(
        cross_kernel,
        out_shape=(
            jax.ShapeDtypeStruct((entries, row_width), F32),
            jax.ShapeDtypeStruct((image_rows, row_width), jnp.bfloat16),
            jax.ShapeDtypeStruct((ref_rows, row_width), jnp.bfloat16),
        ),
        in_specs=[smem(), smem(), smem(), vmem(), vmem(), vmem(), vmem()],
        out_specs=(vmem(), vmem(), vmem()),
        scratch_shapes=[pltpu.VMEM((ref_rows, row_width), jnp.bfloat16)],
        compiler_params=params,
    )(
        count_arr, ent_p, ent_k, images.reshape(image_rows, row_width),
        references.reshape(ref_rows, row_width), forward, wrow,
    )

    log_prior = jnp.log1p(class_counts.astype(F32))
    prior = jnp.sum(
        jnp.where(safe_class[:, None] == jnp.arange(col_classes)[None, :], log_prior[None, :], 0.0),
        axis=1,
    )
    scores_c = jnp.dot(cross_c, rotation_response.T, precision=HIGHEST)
    scores = jnp.take(scores_c, rank, axis=0) + prior[:, None]
    scores = jnp.where(inside[:, None], scores, -1e30).reshape(blocksize, LIST, -1)
    inside_pa = inside.reshape(blocksize, LIST)
    top_local = jnp.max(scores, axis=(1, 2))
    total_local = jnp.sum(
        jnp.where(inside_pa[..., None], jnp.exp(scores - top_local[:, None, None]), 0.0), axis=(1, 2)
    )
    gathered = lax.all_gather(jnp.stack([top_local, total_local]), "cls")
    tops = gathered[:, 0]
    totals = gathered[:, 1]
    top_score = jnp.max(tops, axis=0)
    total_sum = jnp.sum(totals * jnp.exp(tops - top_score[None]), axis=0)
    posterior = (
        jnp.where(inside_pa[..., None], jnp.exp(scores - top_score[:, None, None]), 0.0)
        / total_sum[:, None, None]
    )
    evidence = top_score + jnp.log(total_sum)
    post_sum = jnp.sum(posterior, axis=2).reshape(entries)

    rot_re = rotation_response[:, :NANG]
    rot_im = rotation_response[:, NANG:]
    coef_table = jnp.concatenate([rot_re, -rot_im, rot_re * rot_re + rot_im * rot_im], axis=1)
    coef = jnp.dot(posterior.reshape(entries, -1), coef_table, precision=HIGHEST)
    coef_c = jnp.take(coef, order, axis=0)

    class_pick = (
        (local_class[None, :] == jnp.arange(col_classes, dtype=jnp.int32)[:, None]) & inside[None, :]
    ).astype(F32)
    volume = jnp.dot(class_pick, coef[:, row_width:], precision=HIGHEST)
    denom_part = jnp.dot(class_pick, post_sum, precision=HIGHEST)
    volume_full = jnp.concatenate([volume, volume], axis=1)
    core = dp_index % 2
    half_rows = ref_rows // 2
    half_classes = col_classes // 2
    ref_by = ref_hat.reshape(dp_count // 2, 2, per_owner * NSHELL, row_width)
    vol_by = volume_full.reshape(dp_count // 2, 2, per_owner, row_width)
    owner_core = (local_class // per_owner) % 2
    within_half = jnp.clip(
        (local_class // (2 * per_owner)) * per_owner + local_class % per_owner, 0, half_classes - 1
    )

    def half_numer(hcore):
        in_half = inside & (owner_core == hcore)
        half_i = in_half.astype(jnp.int32)
        half_count = jnp.sum(half_i)
        half_rank = jnp.where(
            in_half, jnp.cumsum(half_i) - half_i, half_count + jnp.cumsum(1 - half_i) - (1 - half_i)
        )
        hit = half_rank[None, :] == slots[:, None]
        half_order = jnp.sum(jnp.where(hit, slots[None, :], 0), axis=1)
        half_p = half_order // LIST
        half_k = jnp.sum(jnp.where(hit, within_half[None, :], 0), axis=1)
        half_coef = jnp.take(coef[:, :row_width], half_order, axis=0)
        half_refs = lax.dynamic_index_in_dim(ref_by, hcore, 1, False).reshape(half_rows, row_width)
        half_vol = lax.dynamic_index_in_dim(vol_by, hcore, 1, False).reshape(half_classes, row_width)
        return pl.pallas_call(
            grad_kernel,
            out_shape=jax.ShapeDtypeStruct((half_rows, row_width), jnp.bfloat16),
            in_specs=[smem(), smem(), smem(), vmem(), vmem(), vmem(), vmem()],
            out_specs=vmem(),
            scratch_shapes=[pltpu.VMEM((half_rows, row_width), F32)],
            compiler_params=params,
        )(half_count.reshape(1), half_p, half_k, image_hat, half_coef, half_refs, half_vol)

    give_numer = half_numer(1 - core)

    dest = pose_slot // blocksize
    dest_hit = dest[None, :] == jnp.arange(dp_count, dtype=jnp.int32)[:, None]
    dest_i = dest_hit.astype(jnp.int32)
    within = jnp.sum((jnp.cumsum(dest_i, axis=1) - dest_i) * dest_i, axis=0)
    sel = dest_hit[:, None, :] & (
        within[None, None, :] == jnp.arange(per_pair, dtype=jnp.int32)[None, :, None]
    )
    send_ev = jnp.sum(jnp.where(sel, evidence[None, None, :], 0.0), axis=2)
    send_pos = jnp.sum(jnp.where(sel, (pose_slot % blocksize).astype(F32)[None, None, :], 0.0), axis=2)
    send_den = denom_part.reshape(dp_count, per_owner)
    ev_hi, ev_lo = split_pair(send_ev)
    den_hi, den_lo = split_pair(send_den)
    small = jnp.concatenate(
        [ev_hi, ev_lo, send_pos.astype(jnp.bfloat16), den_hi, den_lo], axis=1
    )
    slot_w = small.shape[1]
    small_row = lax.dynamic_update_slice(
        jnp.zeros((dp_count, row_width), jnp.bfloat16), small, (0, core * slot_w)
    )
    extra = jnp.zeros((dp_count, EXTRA, row_width), jnp.bfloat16).at[:, 0, :].set(small_row)
    chunk_rows = per_owner * NSHELL
    extra_by = extra.reshape(dp_count // 2, 2, EXTRA, row_width)
    give = jnp.concatenate(
        [
            give_numer.reshape(dp_count // 2, chunk_rows, row_width),
            lax.dynamic_index_in_dim(extra_by, 1 - core, 1, False),
        ],
        axis=1,
    )
    taken = lax.ppermute(give, "dp", perm=[(i, i ^ 1) for i in range(dp_count)])
    keep_numer = half_numer(core)
    keep = jnp.concatenate(
        [
            keep_numer.reshape(dp_count // 2, chunk_rows, row_width),
            lax.dynamic_index_in_dim(extra_by, core, 1, False),
        ],
        axis=1,
    )
    pair_sum = (keep.astype(F32) + taken.astype(F32)).astype(jnp.bfloat16)
    groups = [list(range(q, dp_count, 2)) for q in range(2)]
    arrived = lax.all_to_all(
        pair_sum, "dp", split_axis=0, concat_axis=0, tiled=True, axis_index_groups=groups
    )
    summed = jnp.sum(arrived[:, :chunk_rows].astype(F32), axis=0)
    summed = jnp.dot(summed, inverse, precision=HIGHEST).reshape(per_owner, NSHELL, row_width)

    got = arrived[:, chunk_rows, : 2 * slot_w].astype(F32).reshape(dp_count, slot_w)
    got_ev = (got[:, :per_pair] + got[:, per_pair : 2 * per_pair]).reshape(-1)
    got_pos = got[:, 2 * per_pair : 3 * per_pair].reshape(-1)
    den_at = 3 * per_pair
    own_denom = jnp.sum(
        got[:, den_at : den_at + per_owner] + got[:, den_at + per_owner : den_at + 2 * per_owner],
        axis=0,
    )
    gradient = summed / (1.0 + own_denom)[:, None, None]
    rows = jnp.arange(blocksize, dtype=F32)
    placed = jnp.sum(jnp.where(got_pos[None, :] == rows[:, None], got_ev[None, :], 0.0), axis=1)
    return (gradient[None], placed)


def solution(mesh):
    return jax.shard_map(
        local,
        mesh=mesh,
        in_specs=(
            P("dp", None, None),
            P("dp"),
            P("cls", None, None),
            P(),
            P(),
            P("dp", None),
            P("cls"),
        ),
        out_specs=(P("cls", "dp", None, None), P("dp")),
        check_vma=False,
    )
```

```python
import math

import jax
import jax.numpy as jnp
from jax import lax
from jax.experimental import pallas as pl
from jax.experimental.pallas import tpu as pltpu
from jax.sharding import PartitionSpec as P

NSHELL = 64
NANG = 256
LIST = 2

HIGHEST = lax.Precision.HIGHEST
F32 = jnp.float32


def angular_tables(points):
    positions = jnp.arange(points, dtype=jnp.int32)
    product = positions[:, None] * positions[None, :] % points
    angles = product.astype(jnp.float32) * (2.0 * math.pi / points)
    cosine = jnp.cos(angles) / math.sqrt(points)
    sine_part = jnp.sin(angles) / math.sqrt(points)
    upper_half = jnp.concatenate([cosine, -sine_part], axis=1)
    lower_half = jnp.concatenate([sine_part, cosine], axis=1)
    return jnp.concatenate([upper_half, lower_half], axis=0)


CHUNK = 512
EXTRA = 16


def cross_kernel(
    count_ref, ent_p_ref, ent_k_ref, image_hbm, refs_hbm, forward_ref, wrow_ref,
    cross_ref, image_hat_hbm, ref_hat_hbm,
    image_buf, refs_buf, hat_buf, ref_hat_buf, weighted_ref, in_sem, out_sem,
):
    n_image = image_buf.shape[0] // CHUNK
    n_ref = refs_buf.shape[0] // CHUNK

    def rows(c):
        return pl.ds(c * CHUNK, CHUNK)

    loads = []
    for c in range(n_ref):
        copy = pltpu.make_async_copy(refs_hbm.at[rows(c)], refs_buf.at[rows(c)], in_sem.at[c])
        copy.start()
        loads.append(copy)
    for c in range(n_image):
        copy = pltpu.make_async_copy(
            image_hbm.at[rows(c)], image_buf.at[rows(c)], in_sem.at[n_ref + c]
        )
        copy.start()
        loads.append(copy)
    forward = forward_ref[...]
    wrow = wrow_ref[...]
    stores = []
    for c in range(n_ref):
        loads[c].wait()
        hat = jnp.dot(refs_buf[rows(c)], forward, preferred_element_type=F32).astype(jnp.bfloat16)
        ref_hat_buf[rows(c)] = hat
        weighted_ref[rows(c)] = (hat.astype(F32) * wrow).astype(jnp.bfloat16)
        copy = pltpu.make_async_copy(ref_hat_buf.at[rows(c)], ref_hat_hbm.at[rows(c)], out_sem.at[c])
        copy.start()
        stores.append(copy)
    for c in range(n_image):
        loads[n_ref + c].wait()
        hat_buf[rows(c)] = jnp.dot(
            image_buf[rows(c)], forward, preferred_element_type=F32
        ).astype(jnp.bfloat16)
        copy = pltpu.make_async_copy(
            hat_buf.at[rows(c)], image_hat_hbm.at[rows(c)], out_sem.at[n_ref + c]
        )
        copy.start()
        stores.append(copy)
    cross_ref[...] = jnp.zeros_like(cross_ref)

    def body(e, carry):
        rp = pl.multiple_of(ent_p_ref[e] * NSHELL, NSHELL)
        rk = pl.multiple_of(ent_k_ref[e] * NSHELL, NSHELL)
        x = hat_buf[pl.ds(rp, NSHELL), :].astype(F32)
        w = weighted_ref[pl.ds(rk, NSHELL), :].astype(F32)
        x_re = x[:, :NANG]
        x_im = x[:, NANG:]
        w_re = w[:, :NANG]
        w_im = w[:, NANG:]
        c_re = jnp.sum(x_re * w_re + x_im * w_im, axis=0, keepdims=True)
        c_im = jnp.sum(x_im * w_re - x_re * w_im, axis=0, keepdims=True)
        cross_ref[pl.ds(e, 1), :] = jnp.concatenate([c_re, c_im], axis=1)
        return carry

    lax.fori_loop(0, count_ref[0], body, 0)
    for copy in stores:
        copy.wait()


def grad_kernel(
    count_ref, ent_p_ref, ent_k_ref, image_hat_ref, coef_ref, ref_hat_ref, volume_ref,
    out_ref, acc_ref,
):
    def init(k, carry):
        r = pl.multiple_of(k * NSHELL, NSHELL)
        acc_ref[pl.ds(r, NSHELL), :] = -volume_ref[pl.ds(k, 1), :] * ref_hat_ref[
            pl.ds(r, NSHELL), :
        ].astype(F32)
        return carry

    lax.fori_loop(0, volume_ref.shape[0], init, 0)

    def body(e, carry):
        rp = pl.multiple_of(ent_p_ref[e] * NSHELL, NSHELL)
        rk = pl.multiple_of(ent_k_ref[e] * NSHELL, NSHELL)
        x = image_hat_ref[pl.ds(rp, NSHELL), :].astype(F32)
        c = coef_ref[pl.ds(e, 1), :]
        c_re = c[:, :NANG]
        c_im = c[:, NANG:]
        x_re = x[:, :NANG]
        x_im = x[:, NANG:]
        g_re = x_re * c_re - x_im * c_im
        g_im = x_re * c_im + x_im * c_re
        acc_ref[pl.ds(rk, NSHELL), :] = acc_ref[pl.ds(rk, NSHELL), :] + jnp.concatenate(
            [g_re, g_im], axis=1
        )
        return carry

    lax.fori_loop(0, count_ref[0], body, 0)

    def finish(c, carry):
        r = pl.multiple_of(c * CHUNK, CHUNK)
        out_ref[pl.ds(r, CHUNK), :] = acc_ref[pl.ds(r, CHUNK), :].astype(jnp.bfloat16)
        return carry

    lax.fori_loop(0, acc_ref.shape[0] // CHUNK, finish, 0)


def split_pair(x):
    high = x.astype(jnp.bfloat16)
    low = (x - high.astype(F32)).astype(jnp.bfloat16)
    return high, low


def smem():
    return pl.BlockSpec(memory_space=pltpu.SMEM)


def vmem():
    return pl.BlockSpec(memory_space=pltpu.VMEM)


def local(
    images, pose_slot, references, rotation_response, shell_weight, class_lists, class_counts
):
    dp_index = lax.axis_index("dp")
    column = lax.axis_index("cls")
    dp_count = lax.axis_size("dp")
    blocksize = images.shape[0]
    col_classes = references.shape[0]
    per_owner = col_classes // dp_count
    per_pair = blocksize // dp_count
    row_width = 2 * NANG
    entries = blocksize * LIST
    full_table = angular_tables(NANG)
    forward = full_table.astype(jnp.bfloat16)
    inverse = full_table.T

    packed = jnp.concatenate([class_lists, pose_slot[:, None]], axis=1)
    all_packed = lax.all_to_all(
        jnp.broadcast_to(packed[None], (dp_count,) + packed.shape), "dp", 0, 0, tiled=True
    ).reshape(dp_count * blocksize, LIST + 1)
    all_lists = all_packed[:, :LIST]
    slot_hit = jnp.arange(all_lists.shape[0], dtype=jnp.int32)[None, :] == pose_slot[:, None]
    my_lists = jnp.stack(
        [jnp.sum(jnp.where(slot_hit, all_lists[None, :, a], 0), axis=1) for a in range(LIST)],
        axis=1,
    )
    local_class = (my_lists - column * col_classes).reshape(entries)
    inside = (local_class >= 0) & (local_class < col_classes)
    inside_i = inside.astype(jnp.int32)
    count = jnp.sum(inside_i)
    before_in = jnp.cumsum(inside_i) - inside_i
    before_out = jnp.cumsum(1 - inside_i) - (1 - inside_i)
    rank = jnp.where(inside, before_in, count + before_out)
    slots = jnp.arange(entries, dtype=jnp.int32)
    at_rank = rank[None, :] == slots[:, None]
    order = jnp.sum(jnp.where(at_rank, slots[None, :], 0), axis=1)
    safe_class = jnp.clip(local_class, 0, col_classes - 1)
    ent_p = order // LIST
    ent_k = jnp.sum(jnp.where(at_rank, safe_class[None, :], 0), axis=1)
    count_arr = count.reshape(1)

    image_rows = images.shape[0] * NSHELL
    ref_rows = col_classes * NSHELL
    wrow = jnp.tile(shell_weight, CHUNK // NSHELL)[:, None]
    params = pltpu.CompilerParams(vmem_limit_bytes=60 * 1024 * 1024)
    anywhere = pl.BlockSpec(memory_space=pl.MemorySpace.ANY)
    cross_c, image_hat, ref_hat = pl.pallas_call(
        cross_kernel,
        out_shape=(
            jax.ShapeDtypeStruct((entries, row_width), F32),
            jax.ShapeDtypeStruct((image_rows, row_width), jnp.bfloat16),
            jax.ShapeDtypeStruct((ref_rows, row_width), jnp.bfloat16),
        ),
        in_specs=[smem(), smem(), smem(), anywhere, anywhere, vmem(), vmem()],
        out_specs=(vmem(), anywhere, anywhere),
        scratch_shapes=[
            pltpu.VMEM((image_rows, row_width), jnp.bfloat16),
            pltpu.VMEM((ref_rows, row_width), jnp.bfloat16),
            pltpu.VMEM((image_rows, row_width), jnp.bfloat16),
            pltpu.VMEM((ref_rows, row_width), jnp.bfloat16),
            pltpu.VMEM((ref_rows, row_width), jnp.bfloat16),
            pltpu.SemaphoreType.DMA(((image_rows + ref_rows) // CHUNK,)),
            pltpu.SemaphoreType.DMA(((image_rows + ref_rows) // CHUNK,)),
        ],
        compiler_params=params,
    )(
        count_arr, ent_p, ent_k, images.reshape(image_rows, row_width),
        references.reshape(ref_rows, row_width), forward, wrow,
    )

    log_prior = jnp.log1p(class_counts.astype(F32))
    prior = jnp.sum(
        jnp.where(safe_class[:, None] == jnp.arange(col_classes)[None, :], log_prior[None, :], 0.0),
        axis=1,
    )
    scores_c = jnp.dot(cross_c, rotation_response.T, precision=HIGHEST)
    scores = jnp.take(scores_c, rank, axis=0) + prior[:, None]
    scores = jnp.where(inside[:, None], scores, -1e30).reshape(blocksize, LIST, -1)
    inside_pa = inside.reshape(blocksize, LIST)
    top_local = jnp.max(scores, axis=(1, 2))
    total_local = jnp.sum(
        jnp.where(inside_pa[..., None], jnp.exp(scores - top_local[:, None, None]), 0.0), axis=(1, 2)
    )
    gathered = lax.all_gather(jnp.stack([top_local, total_local]), "cls")
    tops = gathered[:, 0]
    totals = gathered[:, 1]
    top_score = jnp.max(tops, axis=0)
    total_sum = jnp.sum(totals * jnp.exp(tops - top_score[None]), axis=0)
    posterior = (
        jnp.where(inside_pa[..., None], jnp.exp(scores - top_score[:, None, None]), 0.0)
        / total_sum[:, None, None]
    )
    evidence = top_score + jnp.log(total_sum)
    post_sum = jnp.sum(posterior, axis=2).reshape(entries)

    rot_re = rotation_response[:, :NANG]
    rot_im = rotation_response[:, NANG:]
    coef_table = jnp.concatenate([rot_re, -rot_im, rot_re * rot_re + rot_im * rot_im], axis=1)
    coef = jnp.dot(posterior.reshape(entries, -1), coef_table, precision=HIGHEST)
    coef_c = jnp.take(coef, order, axis=0)

    class_pick = (
        (local_class[None, :] == jnp.arange(col_classes, dtype=jnp.int32)[:, None]) & inside[None, :]
    ).astype(F32)
    volume = jnp.dot(class_pick, coef[:, row_width:], precision=HIGHEST)
    denom_part = jnp.dot(class_pick, post_sum, precision=HIGHEST)
    volume_full = jnp.concatenate([volume, volume], axis=1)
    numer = pl.pallas_call(
        grad_kernel,
        out_shape=jax.ShapeDtypeStruct((ref_rows, row_width), jnp.bfloat16),
        in_specs=[smem(), smem(), smem(), vmem(), vmem(), vmem(), vmem()],
        out_specs=vmem(),
        scratch_shapes=[pltpu.VMEM((ref_rows, row_width), F32)],
        compiler_params=params,
    )(count_arr, ent_p, ent_k, image_hat, coef_c[:, :row_width], ref_hat, volume_full)

    core = dp_index % 2
    dest = pose_slot // blocksize
    dest_hit = dest[None, :] == jnp.arange(dp_count, dtype=jnp.int32)[:, None]
    dest_i = dest_hit.astype(jnp.int32)
    within = jnp.sum((jnp.cumsum(dest_i, axis=1) - dest_i) * dest_i, axis=0)
    sel = dest_hit[:, None, :] & (
        within[None, None, :] == jnp.arange(per_pair, dtype=jnp.int32)[None, :, None]
    )
    send_ev = jnp.sum(jnp.where(sel, evidence[None, None, :], 0.0), axis=2)
    send_pos = jnp.sum(jnp.where(sel, (pose_slot % blocksize).astype(F32)[None, None, :], 0.0), axis=2)
    send_den = denom_part.reshape(dp_count, per_owner)
    ev_hi, ev_lo = split_pair(send_ev)
    den_hi, den_lo = split_pair(send_den)
    small = jnp.concatenate(
        [ev_hi, ev_lo, send_pos.astype(jnp.bfloat16), den_hi, den_lo], axis=1
    )
    slot_w = small.shape[1]
    small_row = lax.dynamic_update_slice(
        jnp.zeros((dp_count, row_width), jnp.bfloat16), small, (0, core * slot_w)
    )
    extra = jnp.zeros((dp_count, EXTRA, row_width), jnp.bfloat16).at[:, 0, :].set(small_row)
    chunk_rows = per_owner * NSHELL
    chunks = jnp.concatenate(
        [numer.reshape(dp_count, chunk_rows, row_width), extra], axis=1
    )

    by_core = chunks.reshape(dp_count // 2, 2, chunk_rows + EXTRA, row_width)
    keep = lax.dynamic_index_in_dim(by_core, core, axis=1, keepdims=False)
    give = lax.dynamic_index_in_dim(by_core, 1 - core, axis=1, keepdims=False)
    taken = lax.ppermute(give, "dp", perm=[(i, i ^ 1) for i in range(dp_count)])
    pair_sum = (keep.astype(F32) + taken.astype(F32)).astype(jnp.bfloat16)
    groups = [list(range(q, dp_count, 2)) for q in range(2)]
    arrived = lax.all_to_all(
        pair_sum, "dp", split_axis=0, concat_axis=0, tiled=True, axis_index_groups=groups
    )
    summed = jnp.sum(arrived[:, :chunk_rows].astype(F32), axis=0)
    summed = jnp.dot(summed, inverse, precision=HIGHEST).reshape(per_owner, NSHELL, row_width)

    got = arrived[:, chunk_rows, : 2 * slot_w].astype(F32).reshape(dp_count, slot_w)
    got_ev = (got[:, :per_pair] + got[:, per_pair : 2 * per_pair]).reshape(-1)
    got_pos = got[:, 2 * per_pair : 3 * per_pair].reshape(-1)
    den_at = 3 * per_pair
    own_denom = jnp.sum(
        got[:, den_at : den_at + per_owner] + got[:, den_at + per_owner : den_at + 2 * per_owner],
        axis=0,
    )
    gradient = summed / (1.0 + own_denom)[:, None, None]
    rows = jnp.arange(blocksize, dtype=F32)
    placed = jnp.sum(jnp.where(got_pos[None, :] == rows[:, None], got_ev[None, :], 0.0), axis=1)
    return (gradient[None], placed)


def solution(mesh):
    return jax.shard_map(
        local,
        mesh=mesh,
        in_specs=(
            P("dp", None, None),
            P("dp"),
            P("cls", None, None),
            P(),
            P(),
            P("dp", None),
            P("cls"),
        ),
        out_specs=(P("cls", "dp", None, None), P("dp")),
        check_vma=False,
    )
```

```python
import math

import jax
import jax.numpy as jnp
from jax import lax
from jax.experimental import pallas as pl
from jax.experimental.pallas import tpu as pltpu
from jax.sharding import PartitionSpec as P

NSHELL = 64
NANG = 256
LIST = 2

HIGHEST = lax.Precision.HIGHEST
F32 = jnp.float32


def angular_tables(points):
    positions = jnp.arange(points, dtype=jnp.int32)
    product = positions[:, None] * positions[None, :] % points
    angles = product.astype(jnp.float32) * (2.0 * math.pi / points)
    cosine = jnp.cos(angles) / math.sqrt(points)
    sine_part = jnp.sin(angles) / math.sqrt(points)
    upper_half = jnp.concatenate([cosine, -sine_part], axis=1)
    lower_half = jnp.concatenate([sine_part, cosine], axis=1)
    return jnp.concatenate([upper_half, lower_half], axis=0)


CHUNK = 512
EXTRA = 16


def cross_kernel(
    count_ref, ent_p_ref, ent_k_ref, image_hbm, refs_hbm, forward_ref, wrow_ref,
    cross_ref, image_hat_hbm, ref_hat_hbm,
    image_buf, refs_buf, hat_buf, ref_hat_buf, weighted_ref, in_sem, out_sem,
):
    n_image = image_buf.shape[0] // CHUNK
    n_ref = refs_buf.shape[0] // CHUNK

    def rows(c):
        return pl.ds(c * CHUNK, CHUNK)

    loads = []
    for c in range(n_ref):
        copy = pltpu.make_async_copy(refs_hbm.at[rows(c)], refs_buf.at[rows(c)], in_sem.at[c])
        copy.start()
        loads.append(copy)
    for c in range(n_image):
        copy = pltpu.make_async_copy(
            image_hbm.at[rows(c)], image_buf.at[rows(c)], in_sem.at[n_ref + c]
        )
        copy.start()
        loads.append(copy)
    forward = forward_ref[...]
    wrow = wrow_ref[...]
    stores = []
    for c in range(n_ref):
        loads[c].wait()
        hat = jnp.dot(refs_buf[rows(c)], forward, preferred_element_type=F32).astype(jnp.bfloat16)
        ref_hat_buf[rows(c)] = hat
        weighted_ref[rows(c)] = (hat.astype(F32) * wrow).astype(jnp.bfloat16)
        copy = pltpu.make_async_copy(ref_hat_buf.at[rows(c)], ref_hat_hbm.at[rows(c)], out_sem.at[c])
        copy.start()
        stores.append(copy)
    for c in range(n_image):
        loads[n_ref + c].wait()
        hat_buf[rows(c)] = jnp.dot(
            image_buf[rows(c)], forward, preferred_element_type=F32
        ).astype(jnp.bfloat16)
        copy = pltpu.make_async_copy(
            hat_buf.at[rows(c)], image_hat_hbm.at[rows(c)], out_sem.at[n_ref + c]
        )
        copy.start()
        stores.append(copy)
    cross_ref[...] = jnp.zeros_like(cross_ref)

    def body(e, carry):
        rp = pl.multiple_of(ent_p_ref[e] * NSHELL, NSHELL)
        rk = pl.multiple_of(ent_k_ref[e] * NSHELL, NSHELL)
        x = hat_buf[pl.ds(rp, NSHELL), :].astype(F32)
        w = weighted_ref[pl.ds(rk, NSHELL), :].astype(F32)
        x_re = x[:, :NANG]
        x_im = x[:, NANG:]
        w_re = w[:, :NANG]
        w_im = w[:, NANG:]
        c_re = jnp.sum(x_re * w_re + x_im * w_im, axis=0, keepdims=True)
        c_im = jnp.sum(x_im * w_re - x_re * w_im, axis=0, keepdims=True)
        cross_ref[pl.ds(e, 1), :] = jnp.concatenate([c_re, c_im], axis=1)
        return carry

    lax.fori_loop(0, count_ref[0], body, 0)
    for copy in stores:
        copy.wait()


def grad_kernel(
    count_ref, ent_p_ref, ent_k_ref, image_hat_hbm, coef_ref, ref_hat_hbm, volume_ref,
    out_hbm, image_buf, ref_buf, acc_ref, out_buf, in_sem, out_sem,
):
    n_image = image_buf.shape[0] // CHUNK
    n_ref = ref_buf.shape[0] // CHUNK
    chunk_classes = CHUNK // NSHELL

    def rows(c):
        return pl.ds(c * CHUNK, CHUNK)

    loads = []
    for c in range(n_ref):
        copy = pltpu.make_async_copy(ref_hat_hbm.at[rows(c)], ref_buf.at[rows(c)], in_sem.at[c])
        copy.start()
        loads.append(copy)
    for c in range(n_image):
        copy = pltpu.make_async_copy(
            image_hat_hbm.at[rows(c)], image_buf.at[rows(c)], in_sem.at[n_ref + c]
        )
        copy.start()
        loads.append(copy)

    for c in range(n_ref):
        loads[c].wait()

        def init(i, carry, c=c):
            k = c * chunk_classes + i
            r = pl.multiple_of(k * NSHELL, NSHELL)
            acc_ref[pl.ds(r, NSHELL), :] = -volume_ref[pl.ds(k, 1), :] * ref_buf[
                pl.ds(r, NSHELL), :
            ].astype(F32)
            return carry

        lax.fori_loop(0, chunk_classes, init, 0)
    for c in range(n_image):
        loads[n_ref + c].wait()

    def body(e, carry):
        rp = pl.multiple_of(ent_p_ref[e] * NSHELL, NSHELL)
        rk = pl.multiple_of(ent_k_ref[e] * NSHELL, NSHELL)
        x = image_buf[pl.ds(rp, NSHELL), :].astype(F32)
        c = coef_ref[pl.ds(e, 1), :]
        c_re = c[:, :NANG]
        c_im = c[:, NANG:]
        x_re = x[:, :NANG]
        x_im = x[:, NANG:]
        g_re = x_re * c_re - x_im * c_im
        g_im = x_re * c_im + x_im * c_re
        acc_ref[pl.ds(rk, NSHELL), :] = acc_ref[pl.ds(rk, NSHELL), :] + jnp.concatenate(
            [g_re, g_im], axis=1
        )
        return carry

    lax.fori_loop(0, count_ref[0], body, 0)

    stores = []
    for c in range(n_ref):
        out_buf[rows(c)] = acc_ref[rows(c)].astype(jnp.bfloat16)
        copy = pltpu.make_async_copy(out_buf.at[rows(c)], out_hbm.at[rows(c)], out_sem.at[c])
        copy.start()
        stores.append(copy)
    for copy in stores:
        copy.wait()


def split_pair(x):
    high = x.astype(jnp.bfloat16)
    low = (x - high.astype(F32)).astype(jnp.bfloat16)
    return high, low


def smem():
    return pl.BlockSpec(memory_space=pltpu.SMEM)


def vmem():
    return pl.BlockSpec(memory_space=pltpu.VMEM)


def local(
    images, pose_slot, references, rotation_response, shell_weight, class_lists, class_counts
):
    dp_index = lax.axis_index("dp")
    column = lax.axis_index("cls")
    dp_count = lax.axis_size("dp")
    blocksize = images.shape[0]
    col_classes = references.shape[0]
    per_owner = col_classes // dp_count
    per_pair = blocksize // dp_count
    row_width = 2 * NANG
    entries = blocksize * LIST
    full_table = angular_tables(NANG)
    forward = full_table.astype(jnp.bfloat16)
    inverse = full_table.T

    packed = jnp.concatenate([class_lists, pose_slot[:, None]], axis=1)
    all_packed = lax.all_to_all(
        jnp.broadcast_to(packed[None], (dp_count,) + packed.shape), "dp", 0, 0, tiled=True
    ).reshape(dp_count * blocksize, LIST + 1)
    all_lists = all_packed[:, :LIST]
    slot_hit = jnp.arange(all_lists.shape[0], dtype=jnp.int32)[None, :] == pose_slot[:, None]
    my_lists = jnp.stack(
        [jnp.sum(jnp.where(slot_hit, all_lists[None, :, a], 0), axis=1) for a in range(LIST)],
        axis=1,
    )
    local_class = (my_lists - column * col_classes).reshape(entries)
    inside = (local_class >= 0) & (local_class < col_classes)
    inside_i = inside.astype(jnp.int32)
    count = jnp.sum(inside_i)
    before_in = jnp.cumsum(inside_i) - inside_i
    before_out = jnp.cumsum(1 - inside_i) - (1 - inside_i)
    rank = jnp.where(inside, before_in, count + before_out)
    slots = jnp.arange(entries, dtype=jnp.int32)
    at_rank = rank[None, :] == slots[:, None]
    order = jnp.sum(jnp.where(at_rank, slots[None, :], 0), axis=1)
    safe_class = jnp.clip(local_class, 0, col_classes - 1)
    ent_p = order // LIST
    ent_k = jnp.sum(jnp.where(at_rank, safe_class[None, :], 0), axis=1)
    count_arr = count.reshape(1)

    image_rows = images.shape[0] * NSHELL
    ref_rows = col_classes * NSHELL
    wrow = jnp.tile(shell_weight, CHUNK // NSHELL)[:, None]
    params = pltpu.CompilerParams(vmem_limit_bytes=60 * 1024 * 1024)
    anywhere = pl.BlockSpec(memory_space=pl.MemorySpace.ANY)
    cross_c, image_hat, ref_hat = pl.pallas_call(
        cross_kernel,
        out_shape=(
            jax.ShapeDtypeStruct((entries, row_width), F32),
            jax.ShapeDtypeStruct((image_rows, row_width), jnp.bfloat16),
            jax.ShapeDtypeStruct((ref_rows, row_width), jnp.bfloat16),
        ),
        in_specs=[smem(), smem(), smem(), anywhere, anywhere, vmem(), vmem()],
        out_specs=(vmem(), anywhere, anywhere),
        scratch_shapes=[
            pltpu.VMEM((image_rows, row_width), jnp.bfloat16),
            pltpu.VMEM((ref_rows, row_width), jnp.bfloat16),
            pltpu.VMEM((image_rows, row_width), jnp.bfloat16),
            pltpu.VMEM((ref_rows, row_width), jnp.bfloat16),
            pltpu.VMEM((ref_rows, row_width), jnp.bfloat16),
            pltpu.SemaphoreType.DMA(((image_rows + ref_rows) // CHUNK,)),
            pltpu.SemaphoreType.DMA(((image_rows + ref_rows) // CHUNK,)),
        ],
        compiler_params=params,
    )(
        count_arr, ent_p, ent_k, images.reshape(image_rows, row_width),
        references.reshape(ref_rows, row_width), forward, wrow,
    )

    log_prior = jnp.log1p(class_counts.astype(F32))
    prior = jnp.sum(
        jnp.where(safe_class[:, None] == jnp.arange(col_classes)[None, :], log_prior[None, :], 0.0),
        axis=1,
    )
    scores_c = jnp.dot(cross_c, rotation_response.T, precision=HIGHEST)
    scores = jnp.take(scores_c, rank, axis=0) + prior[:, None]
    scores = jnp.where(inside[:, None], scores, -1e30).reshape(blocksize, LIST, -1)
    inside_pa = inside.reshape(blocksize, LIST)
    top_local = jnp.max(scores, axis=(1, 2))
    total_local = jnp.sum(
        jnp.where(inside_pa[..., None], jnp.exp(scores - top_local[:, None, None]), 0.0), axis=(1, 2)
    )
    gathered = lax.all_gather(jnp.stack([top_local, total_local]), "cls")
    tops = gathered[:, 0]
    totals = gathered[:, 1]
    top_score = jnp.max(tops, axis=0)
    total_sum = jnp.sum(totals * jnp.exp(tops - top_score[None]), axis=0)
    posterior = (
        jnp.where(inside_pa[..., None], jnp.exp(scores - top_score[:, None, None]), 0.0)
        / total_sum[:, None, None]
    )
    evidence = top_score + jnp.log(total_sum)
    post_sum = jnp.sum(posterior, axis=2).reshape(entries)

    rot_re = rotation_response[:, :NANG]
    rot_im = rotation_response[:, NANG:]
    coef_table = jnp.concatenate([rot_re, -rot_im, rot_re * rot_re + rot_im * rot_im], axis=1)
    coef = jnp.dot(posterior.reshape(entries, -1), coef_table, precision=HIGHEST)
    coef_c = jnp.take(coef, order, axis=0)

    class_pick = (
        (local_class[None, :] == jnp.arange(col_classes, dtype=jnp.int32)[:, None]) & inside[None, :]
    ).astype(F32)
    volume = jnp.dot(class_pick, coef[:, row_width:], precision=HIGHEST)
    denom_part = jnp.dot(class_pick, post_sum, precision=HIGHEST)
    volume_full = jnp.concatenate([volume, volume], axis=1)
    numer = pl.pallas_call(
        grad_kernel,
        out_shape=jax.ShapeDtypeStruct((ref_rows, row_width), jnp.bfloat16),
        in_specs=[smem(), smem(), smem(), anywhere, vmem(), anywhere, vmem()],
        out_specs=anywhere,
        scratch_shapes=[
            pltpu.VMEM((image_rows, row_width), jnp.bfloat16),
            pltpu.VMEM((ref_rows, row_width), jnp.bfloat16),
            pltpu.VMEM((ref_rows, row_width), F32),
            pltpu.VMEM((ref_rows, row_width), jnp.bfloat16),
            pltpu.SemaphoreType.DMA(((image_rows + ref_rows) // CHUNK,)),
            pltpu.SemaphoreType.DMA((ref_rows // CHUNK,)),
        ],
        compiler_params=params,
    )(count_arr, ent_p, ent_k, image_hat, coef_c[:, :row_width], ref_hat, volume_full)

    core = dp_index % 2
    dest = pose_slot // blocksize
    dest_hit = dest[None, :] == jnp.arange(dp_count, dtype=jnp.int32)[:, None]
    dest_i = dest_hit.astype(jnp.int32)
    within = jnp.sum((jnp.cumsum(dest_i, axis=1) - dest_i) * dest_i, axis=0)
    sel = dest_hit[:, None, :] & (
        within[None, None, :] == jnp.arange(per_pair, dtype=jnp.int32)[None, :, None]
    )
    send_ev = jnp.sum(jnp.where(sel, evidence[None, None, :], 0.0), axis=2)
    send_pos = jnp.sum(jnp.where(sel, (pose_slot % blocksize).astype(F32)[None, None, :], 0.0), axis=2)
    send_den = denom_part.reshape(dp_count, per_owner)
    ev_hi, ev_lo = split_pair(send_ev)
    den_hi, den_lo = split_pair(send_den)
    small = jnp.concatenate(
        [ev_hi, ev_lo, send_pos.astype(jnp.bfloat16), den_hi, den_lo], axis=1
    )
    slot_w = small.shape[1]
    small_row = lax.dynamic_update_slice(
        jnp.zeros((dp_count, row_width), jnp.bfloat16), small, (0, core * slot_w)
    )
    extra = jnp.zeros((dp_count, EXTRA, row_width), jnp.bfloat16).at[:, 0, :].set(small_row)
    chunk_rows = per_owner * NSHELL
    chunks = jnp.concatenate(
        [numer.reshape(dp_count, chunk_rows, row_width), extra], axis=1
    )

    by_core = chunks.reshape(dp_count // 2, 2, chunk_rows + EXTRA, row_width)
    keep = lax.dynamic_index_in_dim(by_core, core, axis=1, keepdims=False)
    give = lax.dynamic_index_in_dim(by_core, 1 - core, axis=1, keepdims=False)
    taken = lax.ppermute(give, "dp", perm=[(i, i ^ 1) for i in range(dp_count)])
    pair_sum = (keep.astype(F32) + taken.astype(F32)).astype(jnp.bfloat16)
    groups = [list(range(q, dp_count, 2)) for q in range(2)]
    arrived = lax.all_to_all(
        pair_sum, "dp", split_axis=0, concat_axis=0, tiled=True, axis_index_groups=groups
    )
    summed = jnp.sum(arrived[:, :chunk_rows].astype(F32), axis=0)
    summed = jnp.dot(summed, inverse, precision=HIGHEST).reshape(per_owner, NSHELL, row_width)

    got = arrived[:, chunk_rows, : 2 * slot_w].astype(F32).reshape(dp_count, slot_w)
    got_ev = (got[:, :per_pair] + got[:, per_pair : 2 * per_pair]).reshape(-1)
    got_pos = got[:, 2 * per_pair : 3 * per_pair].reshape(-1)
    den_at = 3 * per_pair
    own_denom = jnp.sum(
        got[:, den_at : den_at + per_owner] + got[:, den_at + per_owner : den_at + 2 * per_owner],
        axis=0,
    )
    gradient = summed / (1.0 + own_denom)[:, None, None]
    rows = jnp.arange(blocksize, dtype=F32)
    placed = jnp.sum(jnp.where(got_pos[None, :] == rows[:, None], got_ev[None, :], 0.0), axis=1)
    return (gradient[None], placed)


def solution(mesh):
    return jax.shard_map(
        local,
        mesh=mesh,
        in_specs=(
            P("dp", None, None),
            P("dp"),
            P("cls", None, None),
            P(),
            P(),
            P("dp", None),
            P("cls"),
        ),
        out_specs=(P("cls", "dp", None, None), P("dp")),
        check_vma=False,
    )
```

```python
import math

import jax
import numpy as np
import jax.numpy as jnp
from jax import lax
from jax.experimental import pallas as pl
from jax.experimental.pallas import tpu as pltpu
from jax.sharding import PartitionSpec as P

NSHELL = 64
NANG = 256
LIST = 2

HIGHEST = lax.Precision.HIGHEST
F32 = jnp.float32


def table_constant(points):
    positions = np.arange(points, dtype=np.int32)
    product = positions[:, None] * positions[None, :] % points
    angles = product.astype(np.float32) * np.float32(2.0 * math.pi / points)
    scale = np.float32(math.sqrt(points))
    cosine = np.cos(angles) / scale
    sine_part = np.sin(angles) / scale
    upper_half = np.concatenate([cosine, -sine_part], axis=1)
    lower_half = np.concatenate([sine_part, cosine], axis=1)
    return np.concatenate([upper_half, lower_half], axis=0).astype(np.float32)


def angular_tables(points):
    positions = jnp.arange(points, dtype=jnp.int32)
    product = positions[:, None] * positions[None, :] % points
    angles = product.astype(jnp.float32) * (2.0 * math.pi / points)
    cosine = jnp.cos(angles) / math.sqrt(points)
    sine_part = jnp.sin(angles) / math.sqrt(points)
    upper_half = jnp.concatenate([cosine, -sine_part], axis=1)
    lower_half = jnp.concatenate([sine_part, cosine], axis=1)
    return jnp.concatenate([upper_half, lower_half], axis=0)


CHUNK = 512
EXTRA = 16


def cross_kernel(
    count_ref, ent_p_ref, ent_k_ref, image_hbm, refs_hbm, forward_ref, wrow_ref,
    cross_ref, image_hat_hbm, ref_hat_hbm,
    image_buf, refs_buf, hat_buf, ref_hat_buf, weighted_ref, in_sem, out_sem,
):
    n_image = image_buf.shape[0] // CHUNK
    n_ref = refs_buf.shape[0] // CHUNK

    def rows(c):
        return pl.ds(c * CHUNK, CHUNK)

    loads = []
    for c in range(n_ref):
        copy = pltpu.make_async_copy(refs_hbm.at[rows(c)], refs_buf.at[rows(c)], in_sem.at[c])
        copy.start()
        loads.append(copy)
    for c in range(n_image):
        copy = pltpu.make_async_copy(
            image_hbm.at[rows(c)], image_buf.at[rows(c)], in_sem.at[n_ref + c]
        )
        copy.start()
        loads.append(copy)
    forward = forward_ref[...]
    wrow = wrow_ref[...][None]
    stores = []
    for c in range(n_ref):
        loads[c].wait()
        hat = jnp.dot(refs_buf[rows(c)], forward, preferred_element_type=F32).astype(jnp.bfloat16)
        ref_hat_buf[rows(c)] = hat
        weighted_ref[rows(c)] = (
            hat.astype(F32).reshape(-1, NSHELL, hat.shape[1]) * wrow
        ).reshape(hat.shape).astype(jnp.bfloat16)
        copy = pltpu.make_async_copy(ref_hat_buf.at[rows(c)], ref_hat_hbm.at[rows(c)], out_sem.at[c])
        copy.start()
        stores.append(copy)
    for c in range(n_image):
        loads[n_ref + c].wait()
        hat_buf[rows(c)] = jnp.dot(
            image_buf[rows(c)], forward, preferred_element_type=F32
        ).astype(jnp.bfloat16)
        copy = pltpu.make_async_copy(
            hat_buf.at[rows(c)], image_hat_hbm.at[rows(c)], out_sem.at[n_ref + c]
        )
        copy.start()
        stores.append(copy)
    cross_ref[...] = jnp.zeros_like(cross_ref)

    def body(e, carry):
        rp = pl.multiple_of(ent_p_ref[e] * NSHELL, NSHELL)
        rk = pl.multiple_of(ent_k_ref[e] * NSHELL, NSHELL)
        x = hat_buf[pl.ds(rp, NSHELL), :].astype(F32)
        w = weighted_ref[pl.ds(rk, NSHELL), :].astype(F32)
        x_re = x[:, :NANG]
        x_im = x[:, NANG:]
        w_re = w[:, :NANG]
        w_im = w[:, NANG:]
        c_re = jnp.sum(x_re * w_re + x_im * w_im, axis=0, keepdims=True)
        c_im = jnp.sum(x_im * w_re - x_re * w_im, axis=0, keepdims=True)
        cross_ref[pl.ds(e, 1), :] = jnp.concatenate([c_re, c_im], axis=1)
        return carry

    lax.fori_loop(0, count_ref[0], body, 0)
    for copy in stores:
        copy.wait()


def grad_kernel(
    count_ref, ent_p_ref, ent_k_ref, image_hat_hbm, coef_ref, ref_hat_hbm, volume_ref,
    out_hbm, image_buf, ref_buf, acc_ref, out_buf, in_sem, out_sem,
):
    n_image = image_buf.shape[0] // CHUNK
    n_ref = ref_buf.shape[0] // CHUNK
    chunk_classes = CHUNK // NSHELL

    def rows(c):
        return pl.ds(c * CHUNK, CHUNK)

    loads = []
    for c in range(n_ref):
        copy = pltpu.make_async_copy(ref_hat_hbm.at[rows(c)], ref_buf.at[rows(c)], in_sem.at[c])
        copy.start()
        loads.append(copy)
    for c in range(n_image):
        copy = pltpu.make_async_copy(
            image_hat_hbm.at[rows(c)], image_buf.at[rows(c)], in_sem.at[n_ref + c]
        )
        copy.start()
        loads.append(copy)

    for c in range(n_ref):
        loads[c].wait()

        def init(i, carry, c=c):
            k = c * chunk_classes + i
            r = pl.multiple_of(k * NSHELL, NSHELL)
            acc_ref[pl.ds(r, NSHELL), :] = -volume_ref[pl.ds(k, 1), :] * ref_buf[
                pl.ds(r, NSHELL), :
            ].astype(F32)
            return carry

        lax.fori_loop(0, chunk_classes, init, 0)
    for c in range(n_image):
        loads[n_ref + c].wait()

    def body(e, carry):
        rp = pl.multiple_of(ent_p_ref[e] * NSHELL, NSHELL)
        rk = pl.multiple_of(ent_k_ref[e] * NSHELL, NSHELL)
        x = image_buf[pl.ds(rp, NSHELL), :].astype(F32)
        c = coef_ref[pl.ds(e, 1), :]
        c_re = c[:, :NANG]
        c_im = c[:, NANG:]
        x_re = x[:, :NANG]
        x_im = x[:, NANG:]
        g_re = x_re * c_re - x_im * c_im
        g_im = x_re * c_im + x_im * c_re
        acc_ref[pl.ds(rk, NSHELL), :] = acc_ref[pl.ds(rk, NSHELL), :] + jnp.concatenate(
            [g_re, g_im], axis=1
        )
        return carry

    lax.fori_loop(0, count_ref[0], body, 0)

    stores = []
    for c in range(n_ref):
        out_buf[rows(c)] = acc_ref[rows(c)].astype(jnp.bfloat16)
        copy = pltpu.make_async_copy(out_buf.at[rows(c)], out_hbm.at[rows(c)], out_sem.at[c])
        copy.start()
        stores.append(copy)
    for copy in stores:
        copy.wait()


def split_pair(x):
    high = x.astype(jnp.bfloat16)
    low = (x - high.astype(F32)).astype(jnp.bfloat16)
    return high, low


def smem():
    return pl.BlockSpec(memory_space=pltpu.SMEM)


def vmem():
    return pl.BlockSpec(memory_space=pltpu.VMEM)


def local(
    images, pose_slot, references, rotation_response, shell_weight, class_lists, class_counts
):
    dp_index = lax.axis_index("dp")
    column = lax.axis_index("cls")
    dp_count = lax.axis_size("dp")
    blocksize = images.shape[0]
    col_classes = references.shape[0]
    per_owner = col_classes // dp_count
    per_pair = blocksize // dp_count
    row_width = 2 * NANG
    entries = blocksize * LIST
    full_table = table_constant(NANG)
    forward = jnp.asarray(full_table).astype(jnp.bfloat16)
    inverse = jnp.asarray(np.ascontiguousarray(full_table.T))

    packed = jnp.concatenate([class_lists, pose_slot[:, None]], axis=1)
    all_packed = lax.all_to_all(
        jnp.broadcast_to(packed[None], (dp_count,) + packed.shape), "dp", 0, 0, tiled=True
    ).reshape(dp_count * blocksize, LIST + 1)
    all_lists = all_packed[:, :LIST]
    slot_hit = jnp.arange(all_lists.shape[0], dtype=jnp.int32)[None, :] == pose_slot[:, None]
    my_lists = jnp.stack(
        [jnp.sum(jnp.where(slot_hit, all_lists[None, :, a], 0), axis=1) for a in range(LIST)],
        axis=1,
    )
    local_class = (my_lists - column * col_classes).reshape(entries)
    inside = (local_class >= 0) & (local_class < col_classes)
    inside_i = inside.astype(jnp.int32)
    count = jnp.sum(inside_i)
    before_in = jnp.cumsum(inside_i) - inside_i
    before_out = jnp.cumsum(1 - inside_i) - (1 - inside_i)
    rank = jnp.where(inside, before_in, count + before_out)
    slots = jnp.arange(entries, dtype=jnp.int32)
    at_rank = rank[None, :] == slots[:, None]
    order = jnp.sum(jnp.where(at_rank, slots[None, :], 0), axis=1)
    safe_class = jnp.clip(local_class, 0, col_classes - 1)
    ent_p = order // LIST
    ent_k = jnp.sum(jnp.where(at_rank, safe_class[None, :], 0), axis=1)
    count_arr = count.reshape(1)

    image_rows = images.shape[0] * NSHELL
    ref_rows = col_classes * NSHELL
    wrow = shell_weight[:, None]
    params = pltpu.CompilerParams(vmem_limit_bytes=60 * 1024 * 1024)
    anywhere = pl.BlockSpec(memory_space=pl.MemorySpace.ANY)
    cross_c, image_hat, ref_hat = pl.pallas_call(
        cross_kernel,
        out_shape=(
            jax.ShapeDtypeStruct((entries, row_width), F32),
            jax.ShapeDtypeStruct((image_rows, row_width), jnp.bfloat16),
            jax.ShapeDtypeStruct((ref_rows, row_width), jnp.bfloat16),
        ),
        in_specs=[smem(), smem(), smem(), anywhere, anywhere, vmem(), vmem()],
        out_specs=(vmem(), anywhere, anywhere),
        scratch_shapes=[
            pltpu.VMEM((image_rows, row_width), jnp.bfloat16),
            pltpu.VMEM((ref_rows, row_width), jnp.bfloat16),
            pltpu.VMEM((image_rows, row_width), jnp.bfloat16),
            pltpu.VMEM((ref_rows, row_width), jnp.bfloat16),
            pltpu.VMEM((ref_rows, row_width), jnp.bfloat16),
            pltpu.SemaphoreType.DMA(((image_rows + ref_rows) // CHUNK,)),
            pltpu.SemaphoreType.DMA(((image_rows + ref_rows) // CHUNK,)),
        ],
        compiler_params=params,
    )(
        count_arr, ent_p, ent_k, images.reshape(image_rows, row_width),
        references.reshape(ref_rows, row_width), forward, wrow,
    )

    log_prior = jnp.log1p(class_counts.astype(F32))
    prior = jnp.sum(
        jnp.where(safe_class[:, None] == jnp.arange(col_classes)[None, :], log_prior[None, :], 0.0),
        axis=1,
    )
    scores_c = jnp.dot(cross_c, rotation_response.T, precision=HIGHEST)
    scores = jnp.take(scores_c, rank, axis=0) + prior[:, None]
    scores = jnp.where(inside[:, None], scores, -1e30).reshape(blocksize, LIST, -1)
    inside_pa = inside.reshape(blocksize, LIST)
    top_local = jnp.max(scores, axis=(1, 2))
    total_local = jnp.sum(
        jnp.where(inside_pa[..., None], jnp.exp(scores - top_local[:, None, None]), 0.0), axis=(1, 2)
    )
    gathered = lax.all_gather(jnp.stack([top_local, total_local]), "cls")
    tops = gathered[:, 0]
    totals = gathered[:, 1]
    top_score = jnp.max(tops, axis=0)
    total_sum = jnp.sum(totals * jnp.exp(tops - top_score[None]), axis=0)
    posterior = (
        jnp.where(inside_pa[..., None], jnp.exp(scores - top_score[:, None, None]), 0.0)
        / total_sum[:, None, None]
    )
    evidence = top_score + jnp.log(total_sum)
    post_sum = jnp.sum(posterior, axis=2).reshape(entries)

    rot_re = rotation_response[:, :NANG]
    rot_im = rotation_response[:, NANG:]
    coef_table = jnp.concatenate([rot_re, -rot_im, rot_re * rot_re + rot_im * rot_im], axis=1)
    coef = jnp.dot(posterior.reshape(entries, -1), coef_table, precision=HIGHEST)
    coef_c = jnp.take(coef, order, axis=0)

    class_pick = (
        (local_class[None, :] == jnp.arange(col_classes, dtype=jnp.int32)[:, None]) & inside[None, :]
    ).astype(F32)
    volume = jnp.dot(class_pick, coef[:, row_width:], precision=HIGHEST)
    denom_part = jnp.dot(class_pick, post_sum, precision=HIGHEST)
    volume_full = jnp.concatenate([volume, volume], axis=1)
    numer = pl.pallas_call(
        grad_kernel,
        out_shape=jax.ShapeDtypeStruct((ref_rows, row_width), jnp.bfloat16),
        in_specs=[smem(), smem(), smem(), anywhere, vmem(), anywhere, vmem()],
        out_specs=anywhere,
        scratch_shapes=[
            pltpu.VMEM((image_rows, row_width), jnp.bfloat16),
            pltpu.VMEM((ref_rows, row_width), jnp.bfloat16),
            pltpu.VMEM((ref_rows, row_width), F32),
            pltpu.VMEM((ref_rows, row_width), jnp.bfloat16),
            pltpu.SemaphoreType.DMA(((image_rows + ref_rows) // CHUNK,)),
            pltpu.SemaphoreType.DMA((ref_rows // CHUNK,)),
        ],
        compiler_params=params,
    )(count_arr, ent_p, ent_k, image_hat, coef_c[:, :row_width], ref_hat, volume_full)

    core = dp_index % 2
    dest = pose_slot // blocksize
    dest_hit = dest[None, :] == jnp.arange(dp_count, dtype=jnp.int32)[:, None]
    dest_i = dest_hit.astype(jnp.int32)
    within = jnp.sum((jnp.cumsum(dest_i, axis=1) - dest_i) * dest_i, axis=0)
    sel = dest_hit[:, None, :] & (
        within[None, None, :] == jnp.arange(per_pair, dtype=jnp.int32)[None, :, None]
    )
    send_ev = jnp.sum(jnp.where(sel, evidence[None, None, :], 0.0), axis=2)
    send_pos = jnp.sum(jnp.where(sel, (pose_slot % blocksize).astype(F32)[None, None, :], 0.0), axis=2)
    send_den = denom_part.reshape(dp_count, per_owner)
    ev_hi, ev_lo = split_pair(send_ev)
    den_hi, den_lo = split_pair(send_den)
    small = jnp.concatenate(
        [ev_hi, ev_lo, send_pos.astype(jnp.bfloat16), den_hi, den_lo], axis=1
    )
    slot_w = small.shape[1]
    small_row = lax.dynamic_update_slice(
        jnp.zeros((dp_count, row_width), jnp.bfloat16), small, (0, core * slot_w)
    )
    extra = jnp.zeros((dp_count, EXTRA, row_width), jnp.bfloat16).at[:, 0, :].set(small_row)
    chunk_rows = per_owner * NSHELL
    chunks = jnp.concatenate(
        [numer.reshape(dp_count, chunk_rows, row_width), extra], axis=1
    )

    by_core = chunks.reshape(dp_count // 2, 2, chunk_rows + EXTRA, row_width)
    keep = lax.dynamic_index_in_dim(by_core, core, axis=1, keepdims=False)
    give = lax.dynamic_index_in_dim(by_core, 1 - core, axis=1, keepdims=False)
    taken = lax.ppermute(give, "dp", perm=[(i, i ^ 1) for i in range(dp_count)])
    pair_sum = (keep.astype(F32) + taken.astype(F32)).astype(jnp.bfloat16)
    groups = [list(range(q, dp_count, 2)) for q in range(2)]
    arrived = lax.all_to_all(
        pair_sum, "dp", split_axis=0, concat_axis=0, tiled=True, axis_index_groups=groups
    )
    summed = jnp.sum(arrived[:, :chunk_rows].astype(F32), axis=0)
    summed = jnp.dot(summed, inverse, precision=HIGHEST).reshape(per_owner, NSHELL, row_width)

    got = arrived[:, chunk_rows, : 2 * slot_w].astype(F32).reshape(dp_count, slot_w)
    got_ev = (got[:, :per_pair] + got[:, per_pair : 2 * per_pair]).reshape(-1)
    got_pos = got[:, 2 * per_pair : 3 * per_pair].reshape(-1)
    den_at = 3 * per_pair
    own_denom = jnp.sum(
        got[:, den_at : den_at + per_owner] + got[:, den_at + per_owner : den_at + 2 * per_owner],
        axis=0,
    )
    gradient = summed / (1.0 + own_denom)[:, None, None]
    rows = jnp.arange(blocksize, dtype=F32)
    placed = jnp.sum(jnp.where(got_pos[None, :] == rows[:, None], got_ev[None, :], 0.0), axis=1)
    return (gradient[None], placed)


def solution(mesh):
    return jax.shard_map(
        local,
        mesh=mesh,
        in_specs=(
            P("dp", None, None),
            P("dp"),
            P("cls", None, None),
            P(),
            P(),
            P("dp", None),
            P("cls"),
        ),
        out_specs=(P("cls", "dp", None, None), P("dp")),
        check_vma=False,
    )
```

```python
import math

import jax
import numpy as np
import jax.numpy as jnp
from jax import lax
from jax.experimental import pallas as pl
from jax.experimental.pallas import tpu as pltpu
from jax.sharding import PartitionSpec as P

NSHELL = 64
NANG = 256
LIST = 2

HIGHEST = lax.Precision.HIGHEST
F32 = jnp.float32


def table_constant(points):
    positions = np.arange(points, dtype=np.int32)
    product = positions[:, None] * positions[None, :] % points
    angles = product.astype(np.float32) * np.float32(2.0 * math.pi / points)
    scale = np.float32(math.sqrt(points))
    cosine = np.cos(angles) / scale
    sine_part = np.sin(angles) / scale
    upper_half = np.concatenate([cosine, -sine_part], axis=1)
    lower_half = np.concatenate([sine_part, cosine], axis=1)
    return np.concatenate([upper_half, lower_half], axis=0).astype(np.float32)


def angular_tables(points):
    positions = jnp.arange(points, dtype=jnp.int32)
    product = positions[:, None] * positions[None, :] % points
    angles = product.astype(jnp.float32) * (2.0 * math.pi / points)
    cosine = jnp.cos(angles) / math.sqrt(points)
    sine_part = jnp.sin(angles) / math.sqrt(points)
    upper_half = jnp.concatenate([cosine, -sine_part], axis=1)
    lower_half = jnp.concatenate([sine_part, cosine], axis=1)
    return jnp.concatenate([upper_half, lower_half], axis=0)


CHUNK = 512
EXTRA = 16


def cross_kernel(
    packed_ref, pose_ref, column_ref, image_hbm, refs_hbm, forward_ref, wrow_ref,
    cross_ref, image_hat_hbm, ref_hat_hbm, count_ref, ent_p_ref, ent_k_ref, ent_e_ref, class_ref,
    image_buf, refs_buf, hat_buf, ref_hat_buf, weighted_ref, in_sem, out_sem,
):
    n_image = image_buf.shape[0] // CHUNK
    n_ref = refs_buf.shape[0] // CHUNK
    n_particle = pose_ref.shape[0]
    n_class = refs_buf.shape[0] // NSHELL

    def rows(c):
        return pl.ds(c * CHUNK, CHUNK)

    loads = []
    for c in range(n_ref):
        copy = pltpu.make_async_copy(refs_hbm.at[rows(c)], refs_buf.at[rows(c)], in_sem.at[c])
        copy.start()
        loads.append(copy)
    for c in range(n_image):
        copy = pltpu.make_async_copy(
            image_hbm.at[rows(c)], image_buf.at[rows(c)], in_sem.at[n_ref + c]
        )
        copy.start()
        loads.append(copy)
    first = column_ref[0] * n_class

    def clear(e, carry):
        ent_p_ref[e] = 0
        ent_k_ref[e] = 0
        ent_e_ref[e] = 0
        return carry

    lax.fori_loop(0, n_particle * LIST, clear, 0)

    def prep(p, cnt):
        slot = pose_ref[p]
        for a in range(LIST):
            k = packed_ref[slot * (LIST + 1) + a] - first
            e = p * LIST + a
            class_ref[e] = k
            ins = jnp.logical_and(k >= 0, k < n_class)

            @pl.when(ins)
            def _():
                ent_p_ref[cnt] = p
                ent_k_ref[cnt] = k
                ent_e_ref[cnt] = e

            cnt = cnt + ins.astype(jnp.int32)
        return cnt

    count_ref[0] = lax.fori_loop(0, n_particle, prep, 0)
    forward = forward_ref[...]
    wrow = wrow_ref[...][None]
    stores = []
    for c in range(n_ref):
        loads[c].wait()
        hat = jnp.dot(refs_buf[rows(c)], forward, preferred_element_type=F32).astype(jnp.bfloat16)
        ref_hat_buf[rows(c)] = hat
        weighted_ref[rows(c)] = (
            hat.astype(F32).reshape(-1, NSHELL, hat.shape[1]) * wrow
        ).reshape(hat.shape).astype(jnp.bfloat16)
        copy = pltpu.make_async_copy(ref_hat_buf.at[rows(c)], ref_hat_hbm.at[rows(c)], out_sem.at[c])
        copy.start()
        stores.append(copy)
    for c in range(n_image):
        loads[n_ref + c].wait()
        hat_buf[rows(c)] = jnp.dot(
            image_buf[rows(c)], forward, preferred_element_type=F32
        ).astype(jnp.bfloat16)
        copy = pltpu.make_async_copy(
            hat_buf.at[rows(c)], image_hat_hbm.at[rows(c)], out_sem.at[n_ref + c]
        )
        copy.start()
        stores.append(copy)
    cross_ref[...] = jnp.zeros_like(cross_ref)

    def body(e, carry):
        rp = pl.multiple_of(ent_p_ref[e] * NSHELL, NSHELL)
        rk = pl.multiple_of(ent_k_ref[e] * NSHELL, NSHELL)
        x = hat_buf[pl.ds(rp, NSHELL), :].astype(F32)
        w = weighted_ref[pl.ds(rk, NSHELL), :].astype(F32)
        x_re = x[:, :NANG]
        x_im = x[:, NANG:]
        w_re = w[:, :NANG]
        w_im = w[:, NANG:]
        c_re = jnp.sum(x_re * w_re + x_im * w_im, axis=0, keepdims=True)
        c_im = jnp.sum(x_im * w_re - x_re * w_im, axis=0, keepdims=True)
        cross_ref[pl.ds(ent_e_ref[e], 1), :] = jnp.concatenate([c_re, c_im], axis=1)
        return carry

    lax.fori_loop(0, count_ref[0], body, 0)
    for copy in stores:
        copy.wait()


def grad_kernel(
    count_ref, ent_p_ref, ent_k_ref, ent_e_ref, image_hat_hbm, coef_ref, ref_hat_hbm, volume_ref,
    out_hbm, image_buf, ref_buf, acc_ref, out_buf, in_sem, out_sem,
):
    n_image = image_buf.shape[0] // CHUNK
    n_ref = ref_buf.shape[0] // CHUNK
    chunk_classes = CHUNK // NSHELL

    def rows(c):
        return pl.ds(c * CHUNK, CHUNK)

    loads = []
    for c in range(n_ref):
        copy = pltpu.make_async_copy(ref_hat_hbm.at[rows(c)], ref_buf.at[rows(c)], in_sem.at[c])
        copy.start()
        loads.append(copy)
    for c in range(n_image):
        copy = pltpu.make_async_copy(
            image_hat_hbm.at[rows(c)], image_buf.at[rows(c)], in_sem.at[n_ref + c]
        )
        copy.start()
        loads.append(copy)

    for c in range(n_ref):
        loads[c].wait()

        def init(i, carry, c=c):
            k = c * chunk_classes + i
            r = pl.multiple_of(k * NSHELL, NSHELL)
            acc_ref[pl.ds(r, NSHELL), :] = -volume_ref[pl.ds(k, 1), :] * ref_buf[
                pl.ds(r, NSHELL), :
            ].astype(F32)
            return carry

        lax.fori_loop(0, chunk_classes, init, 0)
    for c in range(n_image):
        loads[n_ref + c].wait()

    def body(e, carry):
        rp = pl.multiple_of(ent_p_ref[e] * NSHELL, NSHELL)
        rk = pl.multiple_of(ent_k_ref[e] * NSHELL, NSHELL)
        x = image_buf[pl.ds(rp, NSHELL), :].astype(F32)
        c = coef_ref[pl.ds(ent_e_ref[e], 1), :]
        c_re = c[:, :NANG]
        c_im = c[:, NANG:]
        x_re = x[:, :NANG]
        x_im = x[:, NANG:]
        g_re = x_re * c_re - x_im * c_im
        g_im = x_re * c_im + x_im * c_re
        acc_ref[pl.ds(rk, NSHELL), :] = acc_ref[pl.ds(rk, NSHELL), :] + jnp.concatenate(
            [g_re, g_im], axis=1
        )
        return carry

    lax.fori_loop(0, count_ref[0], body, 0)

    stores = []
    for c in range(n_ref):
        out_buf[rows(c)] = acc_ref[rows(c)].astype(jnp.bfloat16)
        copy = pltpu.make_async_copy(out_buf.at[rows(c)], out_hbm.at[rows(c)], out_sem.at[c])
        copy.start()
        stores.append(copy)
    for copy in stores:
        copy.wait()


def split_pair(x):
    high = x.astype(jnp.bfloat16)
    low = (x - high.astype(F32)).astype(jnp.bfloat16)
    return high, low


def smem():
    return pl.BlockSpec(memory_space=pltpu.SMEM)


def vmem():
    return pl.BlockSpec(memory_space=pltpu.VMEM)


def local(
    images, pose_slot, references, rotation_response, shell_weight, class_lists, class_counts
):
    dp_index = lax.axis_index("dp")
    column = lax.axis_index("cls")
    dp_count = lax.axis_size("dp")
    blocksize = images.shape[0]
    col_classes = references.shape[0]
    per_owner = col_classes // dp_count
    per_pair = blocksize // dp_count
    row_width = 2 * NANG
    entries = blocksize * LIST
    full_table = table_constant(NANG)
    forward = jnp.asarray(full_table).astype(jnp.bfloat16)
    inverse = jnp.asarray(np.ascontiguousarray(full_table.T))

    packed = jnp.concatenate([class_lists, pose_slot[:, None]], axis=1)
    all_packed = lax.all_to_all(
        jnp.broadcast_to(packed[None], (dp_count,) + packed.shape), "dp", 0, 0, tiled=True
    ).reshape(dp_count * blocksize, LIST + 1)
    image_rows = images.shape[0] * NSHELL
    ref_rows = col_classes * NSHELL
    wrow = shell_weight[:, None]
    params = pltpu.CompilerParams(vmem_limit_bytes=60 * 1024 * 1024)
    anywhere = pl.BlockSpec(memory_space=pl.MemorySpace.ANY)
    cross_c, image_hat, ref_hat, count_arr, ent_p, ent_k, ent_e, local_class = pl.pallas_call(
        cross_kernel,
        out_shape=(
            jax.ShapeDtypeStruct((entries, row_width), F32),
            jax.ShapeDtypeStruct((image_rows, row_width), jnp.bfloat16),
            jax.ShapeDtypeStruct((ref_rows, row_width), jnp.bfloat16),
            jax.ShapeDtypeStruct((1,), jnp.int32),
            jax.ShapeDtypeStruct((entries,), jnp.int32),
            jax.ShapeDtypeStruct((entries,), jnp.int32),
            jax.ShapeDtypeStruct((entries,), jnp.int32),
            jax.ShapeDtypeStruct((entries,), jnp.int32),
        ),
        in_specs=[smem(), smem(), smem(), anywhere, anywhere, vmem(), vmem()],
        out_specs=(vmem(), anywhere, anywhere, smem(), smem(), smem(), smem(), smem()),
        scratch_shapes=[
            pltpu.VMEM((image_rows, row_width), jnp.bfloat16),
            pltpu.VMEM((ref_rows, row_width), jnp.bfloat16),
            pltpu.VMEM((image_rows, row_width), jnp.bfloat16),
            pltpu.VMEM((ref_rows, row_width), jnp.bfloat16),
            pltpu.VMEM((ref_rows, row_width), jnp.bfloat16),
            pltpu.SemaphoreType.DMA(((image_rows + ref_rows) // CHUNK,)),
            pltpu.SemaphoreType.DMA(((image_rows + ref_rows) // CHUNK,)),
        ],
        compiler_params=params,
    )(
        all_packed.reshape(-1), pose_slot, column.astype(jnp.int32).reshape(1),
        images.reshape(image_rows, row_width), references.reshape(ref_rows, row_width),
        forward, wrow,
    )
    inside = (local_class >= 0) & (local_class < col_classes)
    safe_class = jnp.clip(local_class, 0, col_classes - 1)

    log_prior = jnp.log1p(class_counts.astype(F32))
    prior = jnp.sum(
        jnp.where(safe_class[:, None] == jnp.arange(col_classes)[None, :], log_prior[None, :], 0.0),
        axis=1,
    )
    scores_c = jnp.dot(cross_c, rotation_response.T, precision=HIGHEST)
    scores = scores_c + prior[:, None]
    scores = jnp.where(inside[:, None], scores, -1e30).reshape(blocksize, LIST, -1)
    inside_pa = inside.reshape(blocksize, LIST)
    top_local = jnp.max(scores, axis=(1, 2))
    total_local = jnp.sum(
        jnp.where(inside_pa[..., None], jnp.exp(scores - top_local[:, None, None]), 0.0), axis=(1, 2)
    )
    gathered = lax.all_gather(jnp.stack([top_local, total_local]), "cls")
    tops = gathered[:, 0]
    totals = gathered[:, 1]
    top_score = jnp.max(tops, axis=0)
    total_sum = jnp.sum(totals * jnp.exp(tops - top_score[None]), axis=0)
    posterior = (
        jnp.where(inside_pa[..., None], jnp.exp(scores - top_score[:, None, None]), 0.0)
        / total_sum[:, None, None]
    )
    evidence = top_score + jnp.log(total_sum)
    post_sum = jnp.sum(posterior, axis=2).reshape(entries)

    rot_re = rotation_response[:, :NANG]
    rot_im = rotation_response[:, NANG:]
    coef_table = jnp.concatenate([rot_re, -rot_im, rot_re * rot_re + rot_im * rot_im], axis=1)
    coef = jnp.dot(posterior.reshape(entries, -1), coef_table, precision=HIGHEST)

    class_pick = (
        (local_class[None, :] == jnp.arange(col_classes, dtype=jnp.int32)[:, None]) & inside[None, :]
    ).astype(F32)
    volume = jnp.dot(class_pick, coef[:, row_width:], precision=HIGHEST)
    denom_part = jnp.dot(class_pick, post_sum, precision=HIGHEST)
    volume_full = jnp.concatenate([volume, volume], axis=1)
    numer = pl.pallas_call(
        grad_kernel,
        out_shape=jax.ShapeDtypeStruct((ref_rows, row_width), jnp.bfloat16),
        in_specs=[smem(), smem(), smem(), smem(), anywhere, vmem(), anywhere, vmem()],
        out_specs=anywhere,
        scratch_shapes=[
            pltpu.VMEM((image_rows, row_width), jnp.bfloat16),
            pltpu.VMEM((ref_rows, row_width), jnp.bfloat16),
            pltpu.VMEM((ref_rows, row_width), F32),
            pltpu.VMEM((ref_rows, row_width), jnp.bfloat16),
            pltpu.SemaphoreType.DMA(((image_rows + ref_rows) // CHUNK,)),
            pltpu.SemaphoreType.DMA((ref_rows // CHUNK,)),
        ],
        compiler_params=params,
    )(count_arr, ent_p, ent_k, ent_e, image_hat, coef[:, :row_width], ref_hat, volume_full)

    core = dp_index % 2
    dest = pose_slot // blocksize
    dest_hit = dest[None, :] == jnp.arange(dp_count, dtype=jnp.int32)[:, None]
    dest_i = dest_hit.astype(jnp.int32)
    within = jnp.sum((jnp.cumsum(dest_i, axis=1) - dest_i) * dest_i, axis=0)
    sel = dest_hit[:, None, :] & (
        within[None, None, :] == jnp.arange(per_pair, dtype=jnp.int32)[None, :, None]
    )
    send_ev = jnp.sum(jnp.where(sel, evidence[None, None, :], 0.0), axis=2)
    send_pos = jnp.sum(jnp.where(sel, (pose_slot % blocksize).astype(F32)[None, None, :], 0.0), axis=2)
    send_den = denom_part.reshape(dp_count, per_owner)
    ev_hi, ev_lo = split_pair(send_ev)
    den_hi, den_lo = split_pair(send_den)
    small = jnp.concatenate(
        [ev_hi, ev_lo, send_pos.astype(jnp.bfloat16), den_hi, den_lo], axis=1
    )
    slot_w = small.shape[1]
    small_row = lax.dynamic_update_slice(
        jnp.zeros((dp_count, row_width), jnp.bfloat16), small, (0, core * slot_w)
    )
    extra = jnp.zeros((dp_count, EXTRA, row_width), jnp.bfloat16).at[:, 0, :].set(small_row)
    chunk_rows = per_owner * NSHELL
    chunks = jnp.concatenate(
        [numer.reshape(dp_count, chunk_rows, row_width), extra], axis=1
    )

    by_core = chunks.reshape(dp_count // 2, 2, chunk_rows + EXTRA, row_width)
    keep = lax.dynamic_index_in_dim(by_core, core, axis=1, keepdims=False)
    give = lax.dynamic_index_in_dim(by_core, 1 - core, axis=1, keepdims=False)
    taken = lax.ppermute(give, "dp", perm=[(i, i ^ 1) for i in range(dp_count)])
    pair_sum = (keep.astype(F32) + taken.astype(F32)).astype(jnp.bfloat16)
    groups = [list(range(q, dp_count, 2)) for q in range(2)]
    arrived = lax.all_to_all(
        pair_sum, "dp", split_axis=0, concat_axis=0, tiled=True, axis_index_groups=groups
    )
    summed = jnp.sum(arrived[:, :chunk_rows].astype(F32), axis=0)
    summed = jnp.dot(summed, inverse, precision=HIGHEST).reshape(per_owner, NSHELL, row_width)

    got = arrived[:, chunk_rows, : 2 * slot_w].astype(F32).reshape(dp_count, slot_w)
    got_ev = (got[:, :per_pair] + got[:, per_pair : 2 * per_pair]).reshape(-1)
    got_pos = got[:, 2 * per_pair : 3 * per_pair].reshape(-1)
    den_at = 3 * per_pair
    own_denom = jnp.sum(
        got[:, den_at : den_at + per_owner] + got[:, den_at + per_owner : den_at + 2 * per_owner],
        axis=0,
    )
    gradient = summed / (1.0 + own_denom)[:, None, None]
    rows = jnp.arange(blocksize, dtype=F32)
    placed = jnp.sum(jnp.where(got_pos[None, :] == rows[:, None], got_ev[None, :], 0.0), axis=1)
    return (gradient[None], placed)


def solution(mesh):
    return jax.shard_map(
        local,
        mesh=mesh,
        in_specs=(
            P("dp", None, None),
            P("dp"),
            P("cls", None, None),
            P(),
            P(),
            P("dp", None),
            P("cls"),
        ),
        out_specs=(P("cls", "dp", None, None), P("dp")),
        check_vma=False,
    )
```

```python
import math

import jax
import numpy as np
import jax.numpy as jnp
from jax import lax
from jax.experimental import pallas as pl
from jax.experimental.pallas import tpu as pltpu
from jax.sharding import PartitionSpec as P

NSHELL = 64
NANG = 256
LIST = 2

HIGHEST = lax.Precision.HIGHEST
F32 = jnp.float32


def table_constant(points):
    positions = np.arange(points, dtype=np.int32)
    product = positions[:, None] * positions[None, :] % points
    angles = product.astype(np.float32) * np.float32(2.0 * math.pi / points)
    scale = np.float32(math.sqrt(points))
    cosine = np.cos(angles) / scale
    sine_part = np.sin(angles) / scale
    upper_half = np.concatenate([cosine, -sine_part], axis=1)
    lower_half = np.concatenate([sine_part, cosine], axis=1)
    return np.concatenate([upper_half, lower_half], axis=0).astype(np.float32)


def angular_tables(points):
    positions = jnp.arange(points, dtype=jnp.int32)
    product = positions[:, None] * positions[None, :] % points
    angles = product.astype(jnp.float32) * (2.0 * math.pi / points)
    cosine = jnp.cos(angles) / math.sqrt(points)
    sine_part = jnp.sin(angles) / math.sqrt(points)
    upper_half = jnp.concatenate([cosine, -sine_part], axis=1)
    lower_half = jnp.concatenate([sine_part, cosine], axis=1)
    return jnp.concatenate([upper_half, lower_half], axis=0)


CHUNK = 512
EXTRA = 16


def cross_kernel(
    packed_ref, pose_ref, column_ref, image_hbm, refs_hbm, forward_ref, wrow_ref,
    cross_ref, image_hat_hbm, ref_hat_hbm, count_ref, ent_p_ref, ent_k_ref, ent_e_ref, class_ref,
    image_buf, refs_buf, hat_buf, ref_hat_buf, weighted_ref, in_sem, out_sem,
):
    n_image = image_buf.shape[0] // CHUNK
    n_ref = refs_buf.shape[0] // CHUNK
    n_particle = pose_ref.shape[0]
    n_class = refs_buf.shape[0] // NSHELL

    def rows(c):
        return pl.ds(c * CHUNK, CHUNK)

    loads = []
    for c in range(n_ref):
        copy = pltpu.make_async_copy(refs_hbm.at[rows(c)], refs_buf.at[rows(c)], in_sem.at[c])
        copy.start()
        loads.append(copy)
    for c in range(n_image):
        copy = pltpu.make_async_copy(
            image_hbm.at[rows(c)], image_buf.at[rows(c)], in_sem.at[n_ref + c]
        )
        copy.start()
        loads.append(copy)
    first = column_ref[0] * n_class

    def clear(e, carry):
        ent_p_ref[e] = 0
        ent_k_ref[e] = 0
        ent_e_ref[e] = 0
        return carry

    lax.fori_loop(0, n_particle * LIST, clear, 0)

    def prep(p, cnt):
        slot = pose_ref[p]
        for a in range(LIST):
            block = slot // n_particle
            k = packed_ref[(block * LIST + a) * n_particle + slot - block * n_particle] - first
            e = p * LIST + a
            class_ref[e] = k
            ins = jnp.logical_and(k >= 0, k < n_class)

            @pl.when(ins)
            def _():
                ent_p_ref[cnt] = p
                ent_k_ref[cnt] = k
                ent_e_ref[cnt] = e

            cnt = cnt + ins.astype(jnp.int32)
        return cnt

    count_ref[0] = lax.fori_loop(0, n_particle, prep, 0)
    forward = forward_ref[...]
    wrow = wrow_ref[...][None]
    stores = []
    for c in range(n_ref):
        loads[c].wait()
        hat = jnp.dot(refs_buf[rows(c)], forward, preferred_element_type=F32).astype(jnp.bfloat16)
        ref_hat_buf[rows(c)] = hat
        weighted_ref[rows(c)] = (
            hat.astype(F32).reshape(-1, NSHELL, hat.shape[1]) * wrow
        ).reshape(hat.shape).astype(jnp.bfloat16)
        copy = pltpu.make_async_copy(ref_hat_buf.at[rows(c)], ref_hat_hbm.at[rows(c)], out_sem.at[c])
        copy.start()
        stores.append(copy)
    for c in range(n_image):
        loads[n_ref + c].wait()
        hat_buf[rows(c)] = jnp.dot(
            image_buf[rows(c)], forward, preferred_element_type=F32
        ).astype(jnp.bfloat16)
        copy = pltpu.make_async_copy(
            hat_buf.at[rows(c)], image_hat_hbm.at[rows(c)], out_sem.at[n_ref + c]
        )
        copy.start()
        stores.append(copy)
    cross_ref[...] = jnp.zeros_like(cross_ref)

    def body(e, carry):
        rp = pl.multiple_of(ent_p_ref[e] * NSHELL, NSHELL)
        rk = pl.multiple_of(ent_k_ref[e] * NSHELL, NSHELL)
        x = hat_buf[pl.ds(rp, NSHELL), :].astype(F32)
        w = weighted_ref[pl.ds(rk, NSHELL), :].astype(F32)
        x_re = x[:, :NANG]
        x_im = x[:, NANG:]
        w_re = w[:, :NANG]
        w_im = w[:, NANG:]
        c_re = jnp.sum(x_re * w_re + x_im * w_im, axis=0, keepdims=True)
        c_im = jnp.sum(x_im * w_re - x_re * w_im, axis=0, keepdims=True)
        cross_ref[pl.ds(ent_e_ref[e], 1), :] = jnp.concatenate([c_re, c_im], axis=1)
        return carry

    lax.fori_loop(0, count_ref[0], body, 0)
    for copy in stores:
        copy.wait()


def grad_kernel(
    count_ref, ent_p_ref, ent_k_ref, ent_e_ref, image_hat_hbm, coef_ref, ref_hat_hbm, volume_ref,
    out_hbm, image_buf, ref_buf, acc_ref, out_buf, in_sem, out_sem,
):
    n_image = image_buf.shape[0] // CHUNK
    n_ref = ref_buf.shape[0] // CHUNK
    chunk_classes = CHUNK // NSHELL

    def rows(c):
        return pl.ds(c * CHUNK, CHUNK)

    loads = []
    for c in range(n_ref):
        copy = pltpu.make_async_copy(ref_hat_hbm.at[rows(c)], ref_buf.at[rows(c)], in_sem.at[c])
        copy.start()
        loads.append(copy)
    for c in range(n_image):
        copy = pltpu.make_async_copy(
            image_hat_hbm.at[rows(c)], image_buf.at[rows(c)], in_sem.at[n_ref + c]
        )
        copy.start()
        loads.append(copy)

    for c in range(n_ref):
        loads[c].wait()

        def init(i, carry, c=c):
            k = c * chunk_classes + i
            r = pl.multiple_of(k * NSHELL, NSHELL)
            acc_ref[pl.ds(r, NSHELL), :] = -volume_ref[pl.ds(k, 1), :] * ref_buf[
                pl.ds(r, NSHELL), :
            ].astype(F32)
            return carry

        lax.fori_loop(0, chunk_classes, init, 0)
    for c in range(n_image):
        loads[n_ref + c].wait()

    def body(e, carry):
        rp = pl.multiple_of(ent_p_ref[e] * NSHELL, NSHELL)
        rk = pl.multiple_of(ent_k_ref[e] * NSHELL, NSHELL)
        x = image_buf[pl.ds(rp, NSHELL), :].astype(F32)
        c = coef_ref[pl.ds(ent_e_ref[e], 1), :]
        c_re = c[:, :NANG]
        c_im = c[:, NANG:]
        x_re = x[:, :NANG]
        x_im = x[:, NANG:]
        g_re = x_re * c_re - x_im * c_im
        g_im = x_re * c_im + x_im * c_re
        acc_ref[pl.ds(rk, NSHELL), :] = acc_ref[pl.ds(rk, NSHELL), :] + jnp.concatenate(
            [g_re, g_im], axis=1
        )
        return carry

    lax.fori_loop(0, count_ref[0], body, 0)

    stores = []
    for c in range(n_ref):
        out_buf[rows(c)] = acc_ref[rows(c)].astype(jnp.bfloat16)
        copy = pltpu.make_async_copy(out_buf.at[rows(c)], out_hbm.at[rows(c)], out_sem.at[c])
        copy.start()
        stores.append(copy)
    for copy in stores:
        copy.wait()


def split_pair(x):
    high = x.astype(jnp.bfloat16)
    low = (x - high.astype(F32)).astype(jnp.bfloat16)
    return high, low


def smem():
    return pl.BlockSpec(memory_space=pltpu.SMEM)


def vmem():
    return pl.BlockSpec(memory_space=pltpu.VMEM)


def local(
    images, pose_slot, references, rotation_response, shell_weight, class_lists, class_counts
):
    dp_index = lax.axis_index("dp")
    column = lax.axis_index("cls")
    dp_count = lax.axis_size("dp")
    blocksize = images.shape[0]
    col_classes = references.shape[0]
    per_owner = col_classes // dp_count
    per_pair = blocksize // dp_count
    row_width = 2 * NANG
    entries = blocksize * LIST
    full_table = table_constant(NANG)
    forward = jnp.asarray(full_table).astype(jnp.bfloat16)
    inverse = jnp.asarray(np.ascontiguousarray(full_table.T))

    packed = class_lists.T
    all_packed = lax.all_to_all(
        jnp.broadcast_to(packed[None], (dp_count,) + packed.shape), "dp", 0, 0, tiled=True
    )
    image_rows = images.shape[0] * NSHELL
    ref_rows = col_classes * NSHELL
    wrow = shell_weight[:, None]
    params = pltpu.CompilerParams(vmem_limit_bytes=60 * 1024 * 1024)
    anywhere = pl.BlockSpec(memory_space=pl.MemorySpace.ANY)
    cross_c, image_hat, ref_hat, count_arr, ent_p, ent_k, ent_e, local_class = pl.pallas_call(
        cross_kernel,
        out_shape=(
            jax.ShapeDtypeStruct((entries, row_width), F32),
            jax.ShapeDtypeStruct((image_rows, row_width), jnp.bfloat16),
            jax.ShapeDtypeStruct((ref_rows, row_width), jnp.bfloat16),
            jax.ShapeDtypeStruct((1,), jnp.int32),
            jax.ShapeDtypeStruct((entries,), jnp.int32),
            jax.ShapeDtypeStruct((entries,), jnp.int32),
            jax.ShapeDtypeStruct((entries,), jnp.int32),
            jax.ShapeDtypeStruct((entries,), jnp.int32),
        ),
        in_specs=[smem(), smem(), smem(), anywhere, anywhere, vmem(), vmem()],
        out_specs=(vmem(), anywhere, anywhere, smem(), smem(), smem(), smem(), smem()),
        scratch_shapes=[
            pltpu.VMEM((image_rows, row_width), jnp.bfloat16),
            pltpu.VMEM((ref_rows, row_width), jnp.bfloat16),
            pltpu.VMEM((image_rows, row_width), jnp.bfloat16),
            pltpu.VMEM((ref_rows, row_width), jnp.bfloat16),
            pltpu.VMEM((ref_rows, row_width), jnp.bfloat16),
            pltpu.SemaphoreType.DMA(((image_rows + ref_rows) // CHUNK,)),
            pltpu.SemaphoreType.DMA(((image_rows + ref_rows) // CHUNK,)),
        ],
        compiler_params=params,
    )(
        all_packed.reshape(-1), pose_slot, column.astype(jnp.int32).reshape(1),
        images.reshape(image_rows, row_width), references.reshape(ref_rows, row_width),
        forward, wrow,
    )
    inside = (local_class >= 0) & (local_class < col_classes)
    safe_class = jnp.clip(local_class, 0, col_classes - 1)

    log_prior = jnp.log1p(class_counts.astype(F32))
    prior = jnp.sum(
        jnp.where(safe_class[:, None] == jnp.arange(col_classes)[None, :], log_prior[None, :], 0.0),
        axis=1,
    )
    scores_c = jnp.dot(cross_c, rotation_response.T, precision=HIGHEST)
    scores = scores_c + prior[:, None]
    scores = jnp.where(inside[:, None], scores, -1e30).reshape(blocksize, LIST, -1)
    inside_pa = inside.reshape(blocksize, LIST)
    top_local = jnp.max(scores, axis=(1, 2))
    total_local = jnp.sum(
        jnp.where(inside_pa[..., None], jnp.exp(scores - top_local[:, None, None]), 0.0), axis=(1, 2)
    )
    gathered = lax.all_gather(jnp.stack([top_local, total_local]), "cls")
    tops = gathered[:, 0]
    totals = gathered[:, 1]
    top_score = jnp.max(tops, axis=0)
    total_sum = jnp.sum(totals * jnp.exp(tops - top_score[None]), axis=0)
    posterior = (
        jnp.where(inside_pa[..., None], jnp.exp(scores - top_score[:, None, None]), 0.0)
        / total_sum[:, None, None]
    )
    evidence = top_score + jnp.log(total_sum)
    post_sum = jnp.sum(posterior, axis=2).reshape(entries)

    rot_re = rotation_response[:, :NANG]
    rot_im = rotation_response[:, NANG:]
    coef_table = jnp.concatenate([rot_re, -rot_im, rot_re * rot_re + rot_im * rot_im], axis=1)
    coef = jnp.dot(posterior.reshape(entries, -1), coef_table, precision=HIGHEST)

    class_pick = (
        (local_class[None, :] == jnp.arange(col_classes, dtype=jnp.int32)[:, None]) & inside[None, :]
    ).astype(F32)
    volume = jnp.dot(class_pick, coef[:, row_width:], precision=HIGHEST)
    denom_part = jnp.dot(class_pick, post_sum, precision=HIGHEST)
    volume_full = jnp.concatenate([volume, volume], axis=1)
    numer = pl.pallas_call(
        grad_kernel,
        out_shape=jax.ShapeDtypeStruct((ref_rows, row_width), jnp.bfloat16),
        in_specs=[smem(), smem(), smem(), smem(), anywhere, vmem(), anywhere, vmem()],
        out_specs=anywhere,
        scratch_shapes=[
            pltpu.VMEM((image_rows, row_width), jnp.bfloat16),
            pltpu.VMEM((ref_rows, row_width), jnp.bfloat16),
            pltpu.VMEM((ref_rows, row_width), F32),
            pltpu.VMEM((ref_rows, row_width), jnp.bfloat16),
            pltpu.SemaphoreType.DMA(((image_rows + ref_rows) // CHUNK,)),
            pltpu.SemaphoreType.DMA((ref_rows // CHUNK,)),
        ],
        compiler_params=params,
    )(count_arr, ent_p, ent_k, ent_e, image_hat, coef[:, :row_width], ref_hat, volume_full)

    core = dp_index % 2
    dest = pose_slot // blocksize
    dest_hit = dest[None, :] == jnp.arange(dp_count, dtype=jnp.int32)[:, None]
    dest_i = dest_hit.astype(jnp.int32)
    within = jnp.sum((jnp.cumsum(dest_i, axis=1) - dest_i) * dest_i, axis=0)
    sel = dest_hit[:, None, :] & (
        within[None, None, :] == jnp.arange(per_pair, dtype=jnp.int32)[None, :, None]
    )
    send_ev = jnp.sum(jnp.where(sel, evidence[None, None, :], 0.0), axis=2)
    send_pos = jnp.sum(jnp.where(sel, (pose_slot % blocksize).astype(F32)[None, None, :], 0.0), axis=2)
    send_den = denom_part.reshape(dp_count, per_owner)
    ev_hi, ev_lo = split_pair(send_ev)
    den_hi, den_lo = split_pair(send_den)
    small = jnp.concatenate(
        [ev_hi, ev_lo, send_pos.astype(jnp.bfloat16), den_hi, den_lo], axis=1
    )
    slot_w = small.shape[1]
    small_row = lax.dynamic_update_slice(
        jnp.zeros((dp_count, row_width), jnp.bfloat16), small, (0, core * slot_w)
    )
    extra = jnp.zeros((dp_count, EXTRA, row_width), jnp.bfloat16).at[:, 0, :].set(small_row)
    chunk_rows = per_owner * NSHELL
    chunks = jnp.concatenate(
        [numer.reshape(dp_count, chunk_rows, row_width), extra], axis=1
    )

    by_core = chunks.reshape(dp_count // 2, 2, chunk_rows + EXTRA, row_width)
    keep = lax.dynamic_index_in_dim(by_core, core, axis=1, keepdims=False)
    give = lax.dynamic_index_in_dim(by_core, 1 - core, axis=1, keepdims=False)
    taken = lax.ppermute(give, "dp", perm=[(i, i ^ 1) for i in range(dp_count)])
    pair_sum = (keep.astype(F32) + taken.astype(F32)).astype(jnp.bfloat16)
    groups = [list(range(q, dp_count, 2)) for q in range(2)]
    arrived = lax.all_to_all(
        pair_sum, "dp", split_axis=0, concat_axis=0, tiled=True, axis_index_groups=groups
    )
    summed = jnp.sum(arrived[:, :chunk_rows].astype(F32), axis=0)
    summed = jnp.dot(summed, inverse, precision=HIGHEST).reshape(per_owner, NSHELL, row_width)

    got = arrived[:, chunk_rows, : 2 * slot_w].astype(F32).reshape(dp_count, slot_w)
    got_ev = (got[:, :per_pair] + got[:, per_pair : 2 * per_pair]).reshape(-1)
    got_pos = got[:, 2 * per_pair : 3 * per_pair].reshape(-1)
    den_at = 3 * per_pair
    own_denom = jnp.sum(
        got[:, den_at : den_at + per_owner] + got[:, den_at + per_owner : den_at + 2 * per_owner],
        axis=0,
    )
    gradient = summed / (1.0 + own_denom)[:, None, None]
    rows = jnp.arange(blocksize, dtype=F32)
    placed = jnp.sum(jnp.where(got_pos[None, :] == rows[:, None], got_ev[None, :], 0.0), axis=1)
    return (gradient[None], placed)


def solution(mesh):
    return jax.shard_map(
        local,
        mesh=mesh,
        in_specs=(
            P("dp", None, None),
            P("dp"),
            P("cls", None, None),
            P(),
            P(),
            P("dp", None),
            P("cls"),
        ),
        out_specs=(P("cls", "dp", None, None), P("dp")),
        check_vma=False,
    )
```

```python
import math

import jax
import numpy as np
import jax.numpy as jnp
from jax import lax
from jax.experimental import pallas as pl
from jax.experimental.pallas import tpu as pltpu
from jax.sharding import PartitionSpec as P

NSHELL = 64
NANG = 256
LIST = 2

HIGHEST = lax.Precision.HIGHEST
F32 = jnp.float32


def table_constant(points):
    positions = np.arange(points, dtype=np.int32)
    product = positions[:, None] * positions[None, :] % points
    angles = product.astype(np.float32) * np.float32(2.0 * math.pi / points)
    scale = np.float32(math.sqrt(points))
    cosine = np.cos(angles) / scale
    sine_part = np.sin(angles) / scale
    upper_half = np.concatenate([cosine, -sine_part], axis=1)
    lower_half = np.concatenate([sine_part, cosine], axis=1)
    return np.concatenate([upper_half, lower_half], axis=0).astype(np.float32)


def angular_tables(points):
    positions = jnp.arange(points, dtype=jnp.int32)
    product = positions[:, None] * positions[None, :] % points
    angles = product.astype(jnp.float32) * (2.0 * math.pi / points)
    cosine = jnp.cos(angles) / math.sqrt(points)
    sine_part = jnp.sin(angles) / math.sqrt(points)
    upper_half = jnp.concatenate([cosine, -sine_part], axis=1)
    lower_half = jnp.concatenate([sine_part, cosine], axis=1)
    return jnp.concatenate([upper_half, lower_half], axis=0)


CHUNK = 512
EXTRA = 16


def cross_kernel(
    packed_ref, pose_ref, column_ref, image_hbm, refs_hbm, forward_ref, wrow_ref,
    cross_ref, image_hat_hbm, ref_hat_hbm, count_ref, ent_p_ref, ent_k_ref, ent_e_ref, class_ref,
    image_buf, refs_buf, hat_buf, ref_hat_buf, weighted_ref, in_sem, out_sem,
):
    n_image = image_buf.shape[0] // CHUNK
    n_ref = refs_buf.shape[0] // CHUNK
    n_particle = pose_ref.shape[0]
    n_class = refs_buf.shape[0] // NSHELL

    def rows(c):
        return pl.ds(c * CHUNK, CHUNK)

    loads = []
    for c in range(n_ref):
        copy = pltpu.make_async_copy(refs_hbm.at[rows(c)], refs_buf.at[rows(c)], in_sem.at[c])
        copy.start()
        loads.append(copy)
    for c in range(n_image):
        copy = pltpu.make_async_copy(
            image_hbm.at[rows(c)], image_buf.at[rows(c)], in_sem.at[n_ref + c]
        )
        copy.start()
        loads.append(copy)
    first = column_ref[0] * n_class

    def clear(e, carry):
        ent_p_ref[e] = 0
        ent_k_ref[e] = 0
        ent_e_ref[e] = 0
        return carry

    lax.fori_loop(0, n_particle * LIST, clear, 0)

    def prep(p, cnt):
        slot = pose_ref[p]
        for a in range(LIST):
            block = slot // n_particle
            k = packed_ref[(block * LIST + a) * n_particle + slot - block * n_particle] - first
            e = p * LIST + a
            class_ref[e] = k
            ins = jnp.logical_and(k >= 0, k < n_class)

            @pl.when(ins)
            def _():
                ent_p_ref[cnt] = p
                ent_k_ref[cnt] = k
                ent_e_ref[cnt] = e

            cnt = cnt + ins.astype(jnp.int32)
        return cnt

    count_ref[0] = lax.fori_loop(0, n_particle, prep, 0)
    forward = forward_ref[...]
    wrow = wrow_ref[...][None]
    stores = []
    for c in range(n_ref):
        loads[c].wait()
        hat = jnp.dot(refs_buf[rows(c)], forward, preferred_element_type=F32).astype(jnp.bfloat16)
        ref_hat_buf[rows(c)] = hat
        weighted_ref[rows(c)] = (
            hat.astype(F32).reshape(-1, NSHELL, hat.shape[1]) * wrow
        ).reshape(hat.shape).astype(jnp.bfloat16)
        copy = pltpu.make_async_copy(ref_hat_buf.at[rows(c)], ref_hat_hbm.at[rows(c)], out_sem.at[c])
        copy.start()
        stores.append(copy)
    for c in range(n_image):
        loads[n_ref + c].wait()
        hat_buf[rows(c)] = jnp.dot(
            image_buf[rows(c)], forward, preferred_element_type=F32
        ).astype(jnp.bfloat16)
        copy = pltpu.make_async_copy(
            hat_buf.at[rows(c)], image_hat_hbm.at[rows(c)], out_sem.at[n_ref + c]
        )
        copy.start()
        stores.append(copy)
    cross_ref[...] = jnp.zeros_like(cross_ref)

    def body(e, carry):
        rp = pl.multiple_of(ent_p_ref[e] * NSHELL, NSHELL)
        rk = pl.multiple_of(ent_k_ref[e] * NSHELL, NSHELL)
        x = hat_buf[pl.ds(rp, NSHELL), :].astype(F32)
        w = weighted_ref[pl.ds(rk, NSHELL), :].astype(F32)
        x_re = x[:, :NANG]
        x_im = x[:, NANG:]
        w_re = w[:, :NANG]
        w_im = w[:, NANG:]
        c_re = jnp.sum(x_re * w_re + x_im * w_im, axis=0, keepdims=True)
        c_im = jnp.sum(x_im * w_re - x_re * w_im, axis=0, keepdims=True)
        cross_ref[pl.ds(ent_e_ref[e], 1), :] = jnp.concatenate([c_re, c_im], axis=1)
        return carry

    lax.fori_loop(0, count_ref[0], body, 0)
    for copy in stores:
        copy.wait()


def grad_kernel(
    count_ref, ent_p_ref, ent_k_ref, ent_e_ref, image_hat_hbm, coef_ref, ref_hat_hbm, volume_ref,
    out_hbm, image_buf, ref_buf, acc_ref, out_buf, in_sem, out_sem,
):
    n_image = image_buf.shape[0] // CHUNK
    n_ref = ref_buf.shape[0] // CHUNK
    chunk_classes = CHUNK // NSHELL

    def rows(c):
        return pl.ds(c * CHUNK, CHUNK)

    loads = []
    for c in range(n_ref):
        copy = pltpu.make_async_copy(ref_hat_hbm.at[rows(c)], ref_buf.at[rows(c)], in_sem.at[c])
        copy.start()
        loads.append(copy)
    for c in range(n_image):
        copy = pltpu.make_async_copy(
            image_hat_hbm.at[rows(c)], image_buf.at[rows(c)], in_sem.at[n_ref + c]
        )
        copy.start()
        loads.append(copy)

    for c in range(n_ref):
        loads[c].wait()

        def init(i, carry, c=c):
            k = c * chunk_classes + i
            r = pl.multiple_of(k * NSHELL, NSHELL)
            acc_ref[pl.ds(r, NSHELL), :] = -volume_ref[pl.ds(k, 1), :] * ref_buf[
                pl.ds(r, NSHELL), :
            ].astype(F32)
            return carry

        lax.fori_loop(0, chunk_classes, init, 0)
    for c in range(n_image):
        loads[n_ref + c].wait()

    def body(e, carry):
        rp = pl.multiple_of(ent_p_ref[e] * NSHELL, NSHELL)
        rk = pl.multiple_of(ent_k_ref[e] * NSHELL, NSHELL)
        x = image_buf[pl.ds(rp, NSHELL), :].astype(F32)
        c = coef_ref[pl.ds(ent_e_ref[e], 1), :]
        c_re = c[:, :NANG]
        c_im = c[:, NANG:]
        x_re = x[:, :NANG]
        x_im = x[:, NANG:]
        g_re = x_re * c_re - x_im * c_im
        g_im = x_re * c_im + x_im * c_re
        acc_ref[pl.ds(rk, NSHELL), :] = acc_ref[pl.ds(rk, NSHELL), :] + jnp.concatenate(
            [g_re, g_im], axis=1
        )
        return carry

    lax.fori_loop(0, count_ref[0], body, 0)

    stores = []
    for c in range(n_ref):
        out_buf[rows(c)] = acc_ref[rows(c)].astype(jnp.bfloat16)
        copy = pltpu.make_async_copy(out_buf.at[rows(c)], out_hbm.at[rows(c)], out_sem.at[c])
        copy.start()
        stores.append(copy)
    for copy in stores:
        copy.wait()


def split_pair(x):
    high = x.astype(jnp.bfloat16)
    low = (x - high.astype(F32)).astype(jnp.bfloat16)
    return high, low


def smem():
    return pl.BlockSpec(memory_space=pltpu.SMEM)


def vmem():
    return pl.BlockSpec(memory_space=pltpu.VMEM)


def local(
    images, pose_slot, references, rotation_response, shell_weight, class_lists, class_counts
):
    dp_index = lax.axis_index("dp")
    column = lax.axis_index("cls")
    dp_count = lax.axis_size("dp")
    blocksize = images.shape[0]
    col_classes = references.shape[0]
    per_owner = col_classes // dp_count
    per_pair = blocksize // dp_count
    row_width = 2 * NANG
    entries = blocksize * LIST
    full_table = table_constant(NANG)
    forward = jnp.asarray(full_table).astype(jnp.bfloat16)
    inverse = jnp.asarray(np.ascontiguousarray(full_table.T))

    packed = class_lists.T
    all_packed = lax.all_to_all(
        jnp.broadcast_to(packed[None], (dp_count,) + packed.shape), "dp", 0, 0, tiled=True
    )
    image_rows = images.shape[0] * NSHELL
    ref_rows = col_classes * NSHELL
    wrow = shell_weight[:, None]
    params = pltpu.CompilerParams(vmem_limit_bytes=60 * 1024 * 1024)
    anywhere = pl.BlockSpec(memory_space=pl.MemorySpace.ANY)
    cross_c, image_hat, ref_hat, count_arr, ent_p, ent_k, ent_e, local_class = pl.pallas_call(
        cross_kernel,
        out_shape=(
            jax.ShapeDtypeStruct((entries, row_width), F32),
            jax.ShapeDtypeStruct((image_rows, row_width), jnp.bfloat16),
            jax.ShapeDtypeStruct((ref_rows, row_width), jnp.bfloat16),
            jax.ShapeDtypeStruct((1,), jnp.int32),
            jax.ShapeDtypeStruct((entries,), jnp.int32),
            jax.ShapeDtypeStruct((entries,), jnp.int32),
            jax.ShapeDtypeStruct((entries,), jnp.int32),
            jax.ShapeDtypeStruct((entries,), jnp.int32),
        ),
        in_specs=[smem(), smem(), smem(), anywhere, anywhere, vmem(), vmem()],
        out_specs=(vmem(), anywhere, anywhere, smem(), smem(), smem(), smem(), smem()),
        scratch_shapes=[
            pltpu.VMEM((image_rows, row_width), jnp.bfloat16),
            pltpu.VMEM((ref_rows, row_width), jnp.bfloat16),
            pltpu.VMEM((image_rows, row_width), jnp.bfloat16),
            pltpu.VMEM((ref_rows, row_width), jnp.bfloat16),
            pltpu.VMEM((ref_rows, row_width), jnp.bfloat16),
            pltpu.SemaphoreType.DMA(((image_rows + ref_rows) // CHUNK,)),
            pltpu.SemaphoreType.DMA(((image_rows + ref_rows) // CHUNK,)),
        ],
        compiler_params=params,
    )(
        all_packed.reshape(-1), pose_slot, column.astype(jnp.int32).reshape(1),
        images.reshape(image_rows, row_width), references.reshape(ref_rows, row_width),
        forward, wrow,
    )
    inside = (local_class >= 0) & (local_class < col_classes)
    safe_class = jnp.clip(local_class, 0, col_classes - 1)

    log_prior = jnp.log1p(class_counts.astype(F32))
    prior = jnp.sum(
        jnp.where(safe_class[:, None] == jnp.arange(col_classes)[None, :], log_prior[None, :], 0.0),
        axis=1,
    )
    scores_c = jnp.dot(cross_c, rotation_response.T, precision=HIGHEST)
    scores = scores_c + prior[:, None]
    scores = jnp.where(inside[:, None], scores, -1e30).reshape(blocksize, LIST, -1)
    inside_pa = inside.reshape(blocksize, LIST)
    top_local = jnp.max(scores, axis=(1, 2))
    total_local = jnp.sum(
        jnp.where(inside_pa[..., None], jnp.exp(scores - top_local[:, None, None]), 0.0), axis=(1, 2)
    )
    mine = jnp.stack([top_local, total_local])
    slots_cls = jnp.arange(lax.axis_size("cls"), dtype=jnp.int32)
    gathered = lax.psum(
        jnp.where((slots_cls == column)[:, None, None], mine[None], 0.0), "cls"
    )
    tops = gathered[:, 0]
    totals = gathered[:, 1]
    top_score = jnp.max(tops, axis=0)
    total_sum = jnp.sum(totals * jnp.exp(tops - top_score[None]), axis=0)
    posterior = (
        jnp.where(inside_pa[..., None], jnp.exp(scores - top_score[:, None, None]), 0.0)
        / total_sum[:, None, None]
    )
    evidence = top_score + jnp.log(total_sum)
    post_sum = jnp.sum(posterior, axis=2).reshape(entries)

    rot_re = rotation_response[:, :NANG]
    rot_im = rotation_response[:, NANG:]
    coef_table = jnp.concatenate([rot_re, -rot_im, rot_re * rot_re + rot_im * rot_im], axis=1)
    coef = jnp.dot(posterior.reshape(entries, -1), coef_table, precision=HIGHEST)

    class_pick = (
        (local_class[None, :] == jnp.arange(col_classes, dtype=jnp.int32)[:, None]) & inside[None, :]
    ).astype(F32)
    volume = jnp.dot(class_pick, coef[:, row_width:], precision=HIGHEST)
    denom_part = jnp.dot(class_pick, post_sum, precision=HIGHEST)
    volume_full = jnp.concatenate([volume, volume], axis=1)
    numer = pl.pallas_call(
        grad_kernel,
        out_shape=jax.ShapeDtypeStruct((ref_rows, row_width), jnp.bfloat16),
        in_specs=[smem(), smem(), smem(), smem(), anywhere, vmem(), anywhere, vmem()],
        out_specs=anywhere,
        scratch_shapes=[
            pltpu.VMEM((image_rows, row_width), jnp.bfloat16),
            pltpu.VMEM((ref_rows, row_width), jnp.bfloat16),
            pltpu.VMEM((ref_rows, row_width), F32),
            pltpu.VMEM((ref_rows, row_width), jnp.bfloat16),
            pltpu.SemaphoreType.DMA(((image_rows + ref_rows) // CHUNK,)),
            pltpu.SemaphoreType.DMA((ref_rows // CHUNK,)),
        ],
        compiler_params=params,
    )(count_arr, ent_p, ent_k, ent_e, image_hat, coef[:, :row_width], ref_hat, volume_full)

    core = dp_index % 2
    dest = pose_slot // blocksize
    dest_hit = dest[None, :] == jnp.arange(dp_count, dtype=jnp.int32)[:, None]
    dest_i = dest_hit.astype(jnp.int32)
    within = jnp.sum((jnp.cumsum(dest_i, axis=1) - dest_i) * dest_i, axis=0)
    sel = dest_hit[:, None, :] & (
        within[None, None, :] == jnp.arange(per_pair, dtype=jnp.int32)[None, :, None]
    )
    send_ev = jnp.sum(jnp.where(sel, evidence[None, None, :], 0.0), axis=2)
    send_pos = jnp.sum(jnp.where(sel, (pose_slot % blocksize).astype(F32)[None, None, :], 0.0), axis=2)
    send_den = denom_part.reshape(dp_count, per_owner)
    ev_hi, ev_lo = split_pair(send_ev)
    den_hi, den_lo = split_pair(send_den)
    small = jnp.concatenate(
        [ev_hi, ev_lo, send_pos.astype(jnp.bfloat16), den_hi, den_lo], axis=1
    )
    slot_w = small.shape[1]
    small_row = lax.dynamic_update_slice(
        jnp.zeros((dp_count, row_width), jnp.bfloat16), small, (0, core * slot_w)
    )
    extra = jnp.zeros((dp_count, EXTRA, row_width), jnp.bfloat16).at[:, 0, :].set(small_row)
    chunk_rows = per_owner * NSHELL
    chunks = jnp.concatenate(
        [numer.reshape(dp_count, chunk_rows, row_width), extra], axis=1
    )

    by_core = chunks.reshape(dp_count // 2, 2, chunk_rows + EXTRA, row_width)
    keep = lax.dynamic_index_in_dim(by_core, core, axis=1, keepdims=False)
    give = lax.dynamic_index_in_dim(by_core, 1 - core, axis=1, keepdims=False)
    taken = lax.ppermute(give, "dp", perm=[(i, i ^ 1) for i in range(dp_count)])
    pair_sum = (keep.astype(F32) + taken.astype(F32)).astype(jnp.bfloat16)
    groups = [list(range(q, dp_count, 2)) for q in range(2)]
    arrived = lax.all_to_all(
        pair_sum, "dp", split_axis=0, concat_axis=0, tiled=True, axis_index_groups=groups
    )
    summed = jnp.sum(arrived[:, :chunk_rows].astype(F32), axis=0)
    summed = jnp.dot(summed, inverse, precision=HIGHEST).reshape(per_owner, NSHELL, row_width)

    got = arrived[:, chunk_rows, : 2 * slot_w].astype(F32).reshape(dp_count, slot_w)
    got_ev = (got[:, :per_pair] + got[:, per_pair : 2 * per_pair]).reshape(-1)
    got_pos = got[:, 2 * per_pair : 3 * per_pair].reshape(-1)
    den_at = 3 * per_pair
    own_denom = jnp.sum(
        got[:, den_at : den_at + per_owner] + got[:, den_at + per_owner : den_at + 2 * per_owner],
        axis=0,
    )
    gradient = summed / (1.0 + own_denom)[:, None, None]
    rows = jnp.arange(blocksize, dtype=F32)
    placed = jnp.sum(jnp.where(got_pos[None, :] == rows[:, None], got_ev[None, :], 0.0), axis=1)
    return (gradient[None], placed)


def solution(mesh):
    return jax.shard_map(
        local,
        mesh=mesh,
        in_specs=(
            P("dp", None, None),
            P("dp"),
            P("cls", None, None),
            P(),
            P(),
            P("dp", None),
            P("cls"),
        ),
        out_specs=(P("cls", "dp", None, None), P("dp")),
        check_vma=False,
    )
```

```python
import math

import jax
import numpy as np
import jax.numpy as jnp
from jax import lax
from jax.experimental import pallas as pl
from jax.experimental.pallas import tpu as pltpu
from jax.sharding import PartitionSpec as P

NSHELL = 64
NANG = 256
LIST = 2

HIGHEST = lax.Precision.HIGHEST
F32 = jnp.float32


def table_constant(points):
    positions = np.arange(points, dtype=np.int32)
    product = positions[:, None] * positions[None, :] % points
    angles = product.astype(np.float32) * np.float32(2.0 * math.pi / points)
    scale = np.float32(math.sqrt(points))
    cosine = np.cos(angles) / scale
    sine_part = np.sin(angles) / scale
    upper_half = np.concatenate([cosine, -sine_part], axis=1)
    lower_half = np.concatenate([sine_part, cosine], axis=1)
    return np.concatenate([upper_half, lower_half], axis=0).astype(np.float32)


def angular_tables(points):
    positions = jnp.arange(points, dtype=jnp.int32)
    product = positions[:, None] * positions[None, :] % points
    angles = product.astype(jnp.float32) * (2.0 * math.pi / points)
    cosine = jnp.cos(angles) / math.sqrt(points)
    sine_part = jnp.sin(angles) / math.sqrt(points)
    upper_half = jnp.concatenate([cosine, -sine_part], axis=1)
    lower_half = jnp.concatenate([sine_part, cosine], axis=1)
    return jnp.concatenate([upper_half, lower_half], axis=0)


CHUNK = 512
EXTRA = 16


def cross_kernel(
    packed_ref, pose_ref, column_ref, image_hbm, refs_hbm, forward_ref, wrow_ref,
    cross_ref, image_hat_hbm, ref_hat_hbm, count_ref, ent_p_ref, ent_k_ref, ent_e_ref, class_ref,
    image_buf, refs_buf, hat_buf, ref_hat_buf, weighted_ref, in_sem, out_sem,
):
    n_image = image_buf.shape[0] // CHUNK
    n_ref = refs_buf.shape[0] // CHUNK
    n_particle = pose_ref.shape[0]
    n_class = refs_buf.shape[0] // NSHELL

    def rows(c):
        return pl.ds(c * CHUNK, CHUNK)

    loads = []
    for c in range(n_ref):
        copy = pltpu.make_async_copy(refs_hbm.at[rows(c)], refs_buf.at[rows(c)], in_sem.at[c])
        copy.start()
        loads.append(copy)
    for c in range(n_image):
        copy = pltpu.make_async_copy(
            image_hbm.at[rows(c)], image_buf.at[rows(c)], in_sem.at[n_ref + c]
        )
        copy.start()
        loads.append(copy)
    first = column_ref[0] * n_class

    def prep(p, cnt):
        slot = pose_ref[p]
        block = slot // n_particle
        for a in range(LIST):
            k = packed_ref[(block * LIST + a) * n_particle + slot - block * n_particle] - first
            e = p * LIST + a
            class_ref[e] = k
            ins = jnp.logical_and(k >= 0, k < n_class)
            ent_p_ref[cnt] = p
            ent_k_ref[cnt] = k
            ent_e_ref[cnt] = e
            cnt = cnt + ins.astype(jnp.int32)
        return cnt

    count_ref[0] = lax.fori_loop(0, n_particle, prep, 0)
    forward = forward_ref[...]
    wrow = wrow_ref[...][None]
    stores = []
    for c in range(n_ref):
        loads[c].wait()
        hat = jnp.dot(refs_buf[rows(c)], forward, preferred_element_type=F32).astype(jnp.bfloat16)
        ref_hat_buf[rows(c)] = hat
        weighted_ref[rows(c)] = (
            hat.astype(F32).reshape(-1, NSHELL, hat.shape[1]) * wrow
        ).reshape(hat.shape).astype(jnp.bfloat16)
        copy = pltpu.make_async_copy(ref_hat_buf.at[rows(c)], ref_hat_hbm.at[rows(c)], out_sem.at[c])
        copy.start()
        stores.append(copy)
    for c in range(n_image):
        loads[n_ref + c].wait()
        hat_buf[rows(c)] = jnp.dot(
            image_buf[rows(c)], forward, preferred_element_type=F32
        ).astype(jnp.bfloat16)
        copy = pltpu.make_async_copy(
            hat_buf.at[rows(c)], image_hat_hbm.at[rows(c)], out_sem.at[n_ref + c]
        )
        copy.start()
        stores.append(copy)
    cross_ref[...] = jnp.zeros_like(cross_ref)

    def body(e, carry):
        rp = pl.multiple_of(ent_p_ref[e] * NSHELL, NSHELL)
        rk = pl.multiple_of(ent_k_ref[e] * NSHELL, NSHELL)
        x = hat_buf[pl.ds(rp, NSHELL), :].astype(F32)
        w = weighted_ref[pl.ds(rk, NSHELL), :].astype(F32)
        x_re = x[:, :NANG]
        x_im = x[:, NANG:]
        w_re = w[:, :NANG]
        w_im = w[:, NANG:]
        c_re = jnp.sum(x_re * w_re + x_im * w_im, axis=0, keepdims=True)
        c_im = jnp.sum(x_im * w_re - x_re * w_im, axis=0, keepdims=True)
        cross_ref[pl.ds(ent_e_ref[e], 1), :] = jnp.concatenate([c_re, c_im], axis=1)
        return carry

    lax.fori_loop(0, count_ref[0], body, 0)
    for copy in stores:
        copy.wait()


def grad_kernel(
    count_ref, ent_p_ref, ent_k_ref, ent_e_ref, image_hat_hbm, coef_ref, ref_hat_hbm, volume_ref,
    out_hbm, image_buf, ref_buf, acc_ref, out_buf, in_sem, out_sem,
):
    n_image = image_buf.shape[0] // CHUNK
    n_ref = ref_buf.shape[0] // CHUNK
    chunk_classes = CHUNK // NSHELL

    def rows(c):
        return pl.ds(c * CHUNK, CHUNK)

    loads = []
    for c in range(n_ref):
        copy = pltpu.make_async_copy(ref_hat_hbm.at[rows(c)], ref_buf.at[rows(c)], in_sem.at[c])
        copy.start()
        loads.append(copy)
    for c in range(n_image):
        copy = pltpu.make_async_copy(
            image_hat_hbm.at[rows(c)], image_buf.at[rows(c)], in_sem.at[n_ref + c]
        )
        copy.start()
        loads.append(copy)

    for c in range(n_ref):
        loads[c].wait()

        def init(i, carry, c=c):
            k = c * chunk_classes + i
            r = pl.multiple_of(k * NSHELL, NSHELL)
            acc_ref[pl.ds(r, NSHELL), :] = -volume_ref[pl.ds(k, 1), :] * ref_buf[
                pl.ds(r, NSHELL), :
            ].astype(F32)
            return carry

        lax.fori_loop(0, chunk_classes, init, 0)
    for c in range(n_image):
        loads[n_ref + c].wait()

    def body(e, carry):
        rp = pl.multiple_of(ent_p_ref[e] * NSHELL, NSHELL)
        rk = pl.multiple_of(ent_k_ref[e] * NSHELL, NSHELL)
        x = image_buf[pl.ds(rp, NSHELL), :].astype(F32)
        c = coef_ref[pl.ds(ent_e_ref[e], 1), :]
        c_re = c[:, :NANG]
        c_im = c[:, NANG:]
        x_re = x[:, :NANG]
        x_im = x[:, NANG:]
        g_re = x_re * c_re - x_im * c_im
        g_im = x_re * c_im + x_im * c_re
        acc_ref[pl.ds(rk, NSHELL), :] = acc_ref[pl.ds(rk, NSHELL), :] + jnp.concatenate(
            [g_re, g_im], axis=1
        )
        return carry

    lax.fori_loop(0, count_ref[0], body, 0)

    stores = []
    for c in range(n_ref):
        out_buf[rows(c)] = acc_ref[rows(c)].astype(jnp.bfloat16)
        copy = pltpu.make_async_copy(out_buf.at[rows(c)], out_hbm.at[rows(c)], out_sem.at[c])
        copy.start()
        stores.append(copy)
    for copy in stores:
        copy.wait()


def split_pair(x):
    high = x.astype(jnp.bfloat16)
    low = (x - high.astype(F32)).astype(jnp.bfloat16)
    return high, low


def smem():
    return pl.BlockSpec(memory_space=pltpu.SMEM)


def vmem():
    return pl.BlockSpec(memory_space=pltpu.VMEM)


def local(
    images, pose_slot, references, rotation_response, shell_weight, class_lists, class_counts
):
    dp_index = lax.axis_index("dp")
    column = lax.axis_index("cls")
    dp_count = lax.axis_size("dp")
    blocksize = images.shape[0]
    col_classes = references.shape[0]
    per_owner = col_classes // dp_count
    per_pair = blocksize // dp_count
    row_width = 2 * NANG
    entries = blocksize * LIST
    full_table = table_constant(NANG)
    forward = jnp.asarray(full_table).astype(jnp.bfloat16)
    inverse = jnp.asarray(np.ascontiguousarray(full_table.T))

    packed = class_lists.T
    all_packed = lax.all_to_all(
        jnp.broadcast_to(packed[None], (dp_count,) + packed.shape), "dp", 0, 0, tiled=True
    )
    image_rows = images.shape[0] * NSHELL
    ref_rows = col_classes * NSHELL
    wrow = shell_weight[:, None]
    params = pltpu.CompilerParams(vmem_limit_bytes=60 * 1024 * 1024)
    anywhere = pl.BlockSpec(memory_space=pl.MemorySpace.ANY)
    cross_c, image_hat, ref_hat, count_arr, ent_p, ent_k, ent_e, local_class = pl.pallas_call(
        cross_kernel,
        out_shape=(
            jax.ShapeDtypeStruct((entries, row_width), F32),
            jax.ShapeDtypeStruct((image_rows, row_width), jnp.bfloat16),
            jax.ShapeDtypeStruct((ref_rows, row_width), jnp.bfloat16),
            jax.ShapeDtypeStruct((1,), jnp.int32),
            jax.ShapeDtypeStruct((entries,), jnp.int32),
            jax.ShapeDtypeStruct((entries,), jnp.int32),
            jax.ShapeDtypeStruct((entries,), jnp.int32),
            jax.ShapeDtypeStruct((entries,), jnp.int32),
        ),
        in_specs=[smem(), smem(), smem(), anywhere, anywhere, vmem(), vmem()],
        out_specs=(vmem(), anywhere, anywhere, smem(), smem(), smem(), smem(), smem()),
        scratch_shapes=[
            pltpu.VMEM((image_rows, row_width), jnp.bfloat16),
            pltpu.VMEM((ref_rows, row_width), jnp.bfloat16),
            pltpu.VMEM((image_rows, row_width), jnp.bfloat16),
            pltpu.VMEM((ref_rows, row_width), jnp.bfloat16),
            pltpu.VMEM((ref_rows, row_width), jnp.bfloat16),
            pltpu.SemaphoreType.DMA(((image_rows + ref_rows) // CHUNK,)),
            pltpu.SemaphoreType.DMA(((image_rows + ref_rows) // CHUNK,)),
        ],
        compiler_params=params,
    )(
        all_packed.reshape(-1), pose_slot, column.astype(jnp.int32).reshape(1),
        images.reshape(image_rows, row_width), references.reshape(ref_rows, row_width),
        forward, wrow,
    )
    inside = (local_class >= 0) & (local_class < col_classes)
    safe_class = jnp.clip(local_class, 0, col_classes - 1)

    log_prior = jnp.log1p(class_counts.astype(F32))
    prior = jnp.sum(
        jnp.where(safe_class[:, None] == jnp.arange(col_classes)[None, :], log_prior[None, :], 0.0),
        axis=1,
    )
    scores_c = jnp.dot(cross_c, rotation_response.T, precision=HIGHEST)
    scores = scores_c + prior[:, None]
    scores = jnp.where(inside[:, None], scores, -1e30).reshape(blocksize, LIST, -1)
    inside_pa = inside.reshape(blocksize, LIST)
    top_local = jnp.max(scores, axis=(1, 2))
    total_local = jnp.sum(
        jnp.where(inside_pa[..., None], jnp.exp(scores - top_local[:, None, None]), 0.0), axis=(1, 2)
    )
    gathered = lax.all_gather(jnp.stack([top_local, total_local]), "cls")
    tops = gathered[:, 0]
    totals = gathered[:, 1]
    top_score = jnp.max(tops, axis=0)
    total_sum = jnp.sum(totals * jnp.exp(tops - top_score[None]), axis=0)
    posterior = (
        jnp.where(inside_pa[..., None], jnp.exp(scores - top_score[:, None, None]), 0.0)
        / total_sum[:, None, None]
    )
    evidence = top_score + jnp.log(total_sum)
    post_sum = jnp.sum(posterior, axis=2).reshape(entries)

    rot_re = rotation_response[:, :NANG]
    rot_im = rotation_response[:, NANG:]
    coef_table = jnp.concatenate([rot_re, -rot_im, rot_re * rot_re + rot_im * rot_im], axis=1)
    coef = jnp.dot(posterior.reshape(entries, -1), coef_table, precision=HIGHEST)

    class_pick = (
        (local_class[None, :] == jnp.arange(col_classes, dtype=jnp.int32)[:, None]) & inside[None, :]
    ).astype(F32)
    volume = jnp.dot(class_pick, coef[:, row_width:], precision=HIGHEST)
    denom_part = jnp.dot(class_pick, post_sum, precision=HIGHEST)
    volume_full = jnp.concatenate([volume, volume], axis=1)
    numer = pl.pallas_call(
        grad_kernel,
        out_shape=jax.ShapeDtypeStruct((ref_rows, row_width), jnp.bfloat16),
        in_specs=[smem(), smem(), smem(), smem(), anywhere, vmem(), anywhere, vmem()],
        out_specs=anywhere,
        scratch_shapes=[
            pltpu.VMEM((image_rows, row_width), jnp.bfloat16),
            pltpu.VMEM((ref_rows, row_width), jnp.bfloat16),
            pltpu.VMEM((ref_rows, row_width), F32),
            pltpu.VMEM((ref_rows, row_width), jnp.bfloat16),
            pltpu.SemaphoreType.DMA(((image_rows + ref_rows) // CHUNK,)),
            pltpu.SemaphoreType.DMA((ref_rows // CHUNK,)),
        ],
        compiler_params=params,
    )(count_arr, ent_p, ent_k, ent_e, image_hat, coef[:, :row_width], ref_hat, volume_full)

    core = dp_index % 2
    dest = pose_slot // blocksize
    dest_hit = dest[None, :] == jnp.arange(dp_count, dtype=jnp.int32)[:, None]
    dest_i = dest_hit.astype(jnp.int32)
    within = jnp.sum((jnp.cumsum(dest_i, axis=1) - dest_i) * dest_i, axis=0)
    sel = dest_hit[:, None, :] & (
        within[None, None, :] == jnp.arange(per_pair, dtype=jnp.int32)[None, :, None]
    )
    send_ev = jnp.sum(jnp.where(sel, evidence[None, None, :], 0.0), axis=2)
    send_pos = jnp.sum(jnp.where(sel, (pose_slot % blocksize).astype(F32)[None, None, :], 0.0), axis=2)
    send_den = denom_part.reshape(dp_count, per_owner)
    ev_hi, ev_lo = split_pair(send_ev)
    den_hi, den_lo = split_pair(send_den)
    small = jnp.concatenate(
        [ev_hi, ev_lo, send_pos.astype(jnp.bfloat16), den_hi, den_lo], axis=1
    )
    slot_w = small.shape[1]
    small_row = lax.dynamic_update_slice(
        jnp.zeros((dp_count, row_width), jnp.bfloat16), small, (0, core * slot_w)
    )
    extra = jnp.zeros((dp_count, EXTRA, row_width), jnp.bfloat16).at[:, 0, :].set(small_row)
    chunk_rows = per_owner * NSHELL
    chunks = jnp.concatenate(
        [numer.reshape(dp_count, chunk_rows, row_width), extra], axis=1
    )

    by_core = chunks.reshape(dp_count // 2, 2, chunk_rows + EXTRA, row_width)
    keep = lax.dynamic_index_in_dim(by_core, core, axis=1, keepdims=False)
    give = lax.dynamic_index_in_dim(by_core, 1 - core, axis=1, keepdims=False)
    taken = lax.ppermute(give, "dp", perm=[(i, i ^ 1) for i in range(dp_count)])
    pair_sum = (keep.astype(F32) + taken.astype(F32)).astype(jnp.bfloat16)
    groups = [list(range(q, dp_count, 2)) for q in range(2)]
    arrived = lax.all_to_all(
        pair_sum, "dp", split_axis=0, concat_axis=0, tiled=True, axis_index_groups=groups
    )
    summed = jnp.sum(arrived[:, :chunk_rows].astype(F32), axis=0)
    summed = jnp.dot(summed, inverse, precision=HIGHEST).reshape(per_owner, NSHELL, row_width)

    got = arrived[:, chunk_rows, : 2 * slot_w].astype(F32).reshape(dp_count, slot_w)
    got_ev = (got[:, :per_pair] + got[:, per_pair : 2 * per_pair]).reshape(-1)
    got_pos = got[:, 2 * per_pair : 3 * per_pair].reshape(-1)
    den_at = 3 * per_pair
    own_denom = jnp.sum(
        got[:, den_at : den_at + per_owner] + got[:, den_at + per_owner : den_at + 2 * per_owner],
        axis=0,
    )
    gradient = summed / (1.0 + own_denom)[:, None, None]
    rows = jnp.arange(blocksize, dtype=F32)
    placed = jnp.sum(jnp.where(got_pos[None, :] == rows[:, None], got_ev[None, :], 0.0), axis=1)
    return (gradient[None], placed)


def solution(mesh):
    return jax.shard_map(
        local,
        mesh=mesh,
        in_specs=(
            P("dp", None, None),
            P("dp"),
            P("cls", None, None),
            P(),
            P(),
            P("dp", None),
            P("cls"),
        ),
        out_specs=(P("cls", "dp", None, None), P("dp")),
        check_vma=False,
    )
```

```python
import math

import jax
import numpy as np
import jax.numpy as jnp
from jax import lax
from jax.experimental import pallas as pl
from jax.experimental.pallas import tpu as pltpu
from jax.sharding import PartitionSpec as P

NSHELL = 64
NANG = 256
LIST = 2

HIGHEST = lax.Precision.HIGHEST
F32 = jnp.float32


def table_constant(points):
    positions = np.arange(points, dtype=np.int32)
    product = positions[:, None] * positions[None, :] % points
    angles = product.astype(np.float32) * np.float32(2.0 * math.pi / points)
    scale = np.float32(math.sqrt(points))
    cosine = np.cos(angles) / scale
    sine_part = np.sin(angles) / scale
    upper_half = np.concatenate([cosine, -sine_part], axis=1)
    lower_half = np.concatenate([sine_part, cosine], axis=1)
    return np.concatenate([upper_half, lower_half], axis=0).astype(np.float32)


def angular_tables(points):
    positions = jnp.arange(points, dtype=jnp.int32)
    product = positions[:, None] * positions[None, :] % points
    angles = product.astype(jnp.float32) * (2.0 * math.pi / points)
    cosine = jnp.cos(angles) / math.sqrt(points)
    sine_part = jnp.sin(angles) / math.sqrt(points)
    upper_half = jnp.concatenate([cosine, -sine_part], axis=1)
    lower_half = jnp.concatenate([sine_part, cosine], axis=1)
    return jnp.concatenate([upper_half, lower_half], axis=0)


CHUNK = 512
EXTRA = 16


def cross_kernel(
    packed_ref, pose_ref, column_ref, image_hbm, refs_hbm, forward_ref, wrow_ref,
    cross_ref, image_hat_hbm, ref_hat_hbm, count_ref, ent_p_ref, ent_k_ref, ent_e_ref, class_ref,
    image_buf, refs_buf, hat_buf, ref_hat_buf, weighted_ref, in_sem, out_sem,
):
    n_image = image_buf.shape[0] // CHUNK
    n_ref = refs_buf.shape[0] // CHUNK
    n_particle = pose_ref.shape[0]
    n_class = refs_buf.shape[0] // NSHELL

    def rows(c):
        return pl.ds(c * CHUNK, CHUNK)

    loads = []
    for c in range(n_ref):
        copy = pltpu.make_async_copy(refs_hbm.at[rows(c)], refs_buf.at[rows(c)], in_sem.at[c])
        copy.start()
        loads.append(copy)
    for c in range(n_image):
        copy = pltpu.make_async_copy(
            image_hbm.at[rows(c)], image_buf.at[rows(c)], in_sem.at[n_ref + c]
        )
        copy.start()
        loads.append(copy)
    first = column_ref[0] * n_class

    def prep(p, cnt):
        slot = pose_ref[p]
        block = slot // n_particle
        for a in range(LIST):
            k = packed_ref[(block * LIST + a) * n_particle + slot - block * n_particle] - first
            e = p * LIST + a
            class_ref[e] = k
            ins = jnp.logical_and(k >= 0, k < n_class)
            ent_p_ref[cnt] = p
            ent_k_ref[cnt] = k
            ent_e_ref[cnt] = e
            cnt = cnt + ins.astype(jnp.int32)
        return cnt

    count_ref[0] = lax.fori_loop(0, n_particle, prep, 0)
    forward = forward_ref[...]
    wrow = wrow_ref[...][None]
    stores = []
    for c in range(n_ref):
        loads[c].wait()
        hat = jnp.dot(refs_buf[rows(c)], forward, preferred_element_type=F32).astype(jnp.bfloat16)
        ref_hat_buf[rows(c)] = hat
        weighted_ref[rows(c)] = (
            hat.astype(F32).reshape(-1, NSHELL, hat.shape[1]) * wrow
        ).reshape(hat.shape).astype(jnp.bfloat16)
        copy = pltpu.make_async_copy(ref_hat_buf.at[rows(c)], ref_hat_hbm.at[rows(c)], out_sem.at[c])
        copy.start()
        stores.append(copy)
    for c in range(n_image):
        loads[n_ref + c].wait()
        hat_buf[rows(c)] = jnp.dot(
            image_buf[rows(c)], forward, preferred_element_type=F32
        ).astype(jnp.bfloat16)
        copy = pltpu.make_async_copy(
            hat_buf.at[rows(c)], image_hat_hbm.at[rows(c)], out_sem.at[n_ref + c]
        )
        copy.start()
        stores.append(copy)
    cross_ref[...] = jnp.zeros_like(cross_ref)

    def body(e, carry):
        rp = pl.multiple_of(ent_p_ref[e] * NSHELL, NSHELL)
        rk = pl.multiple_of(ent_k_ref[e] * NSHELL, NSHELL)
        x = hat_buf[pl.ds(rp, NSHELL), :].astype(F32)
        w = weighted_ref[pl.ds(rk, NSHELL), :].astype(F32)
        x_re = x[:, :NANG]
        x_im = x[:, NANG:]
        w_re = w[:, :NANG]
        w_im = w[:, NANG:]
        c_re = jnp.sum(x_re * w_re + x_im * w_im, axis=0, keepdims=True)
        c_im = jnp.sum(x_im * w_re - x_re * w_im, axis=0, keepdims=True)
        cross_ref[pl.ds(ent_e_ref[e], 1), :] = jnp.concatenate([c_re, c_im], axis=1)
        return carry

    lax.fori_loop(0, count_ref[0], body, 0)
    for copy in stores:
        copy.wait()


def grad_kernel(
    count_ref, ent_p_ref, ent_k_ref, ent_e_ref, image_hat_hbm, coef_ref, ref_hat_hbm, volume_ref,
    out_hbm, image_buf, ref_buf, acc_ref, out_buf, in_sem, out_sem,
):
    n_image = image_buf.shape[0] // CHUNK
    n_ref = ref_buf.shape[0] // CHUNK
    chunk_classes = CHUNK // NSHELL

    def rows(c):
        return pl.ds(c * CHUNK, CHUNK)

    loads = []
    for c in range(n_ref):
        copy = pltpu.make_async_copy(ref_hat_hbm.at[rows(c)], ref_buf.at[rows(c)], in_sem.at[c])
        copy.start()
        loads.append(copy)
    for c in range(n_image):
        copy = pltpu.make_async_copy(
            image_hat_hbm.at[rows(c)], image_buf.at[rows(c)], in_sem.at[n_ref + c]
        )
        copy.start()
        loads.append(copy)

    acc_ref[...] = jnp.zeros_like(acc_ref)
    for c in range(n_image):
        loads[n_ref + c].wait()

    def body(e, carry):
        rp = pl.multiple_of(ent_p_ref[e] * NSHELL, NSHELL)
        rk = pl.multiple_of(ent_k_ref[e] * NSHELL, NSHELL)
        x = image_buf[pl.ds(rp, NSHELL), :].astype(F32)
        c = coef_ref[pl.ds(ent_e_ref[e], 1), :]
        c_re = c[:, :NANG]
        c_im = c[:, NANG:]
        x_re = x[:, :NANG]
        x_im = x[:, NANG:]
        g_re = x_re * c_re - x_im * c_im
        g_im = x_re * c_im + x_im * c_re
        acc_ref[pl.ds(rk, NSHELL), :] = acc_ref[pl.ds(rk, NSHELL), :] + jnp.concatenate(
            [g_re, g_im], axis=1
        )
        return carry

    lax.fori_loop(0, count_ref[0], body, 0)

    stores = []
    for c in range(n_ref):
        loads[c].wait()
        vol = volume_ref[pl.ds(c * chunk_classes, chunk_classes), :][:, None, :]
        ref_part = ref_buf[rows(c)].astype(F32).reshape(chunk_classes, NSHELL, -1)
        acc_part = acc_ref[rows(c)].reshape(chunk_classes, NSHELL, -1)
        out_buf[rows(c)] = (acc_part - vol * ref_part).reshape(CHUNK, -1).astype(jnp.bfloat16)
        copy = pltpu.make_async_copy(out_buf.at[rows(c)], out_hbm.at[rows(c)], out_sem.at[c])
        copy.start()
        stores.append(copy)
    for copy in stores:
        copy.wait()


def split_pair(x):
    high = x.astype(jnp.bfloat16)
    low = (x - high.astype(F32)).astype(jnp.bfloat16)
    return high, low


def smem():
    return pl.BlockSpec(memory_space=pltpu.SMEM)


def vmem():
    return pl.BlockSpec(memory_space=pltpu.VMEM)


def local(
    images, pose_slot, references, rotation_response, shell_weight, class_lists, class_counts
):
    dp_index = lax.axis_index("dp")
    column = lax.axis_index("cls")
    dp_count = lax.axis_size("dp")
    blocksize = images.shape[0]
    col_classes = references.shape[0]
    per_owner = col_classes // dp_count
    per_pair = blocksize // dp_count
    row_width = 2 * NANG
    entries = blocksize * LIST
    full_table = table_constant(NANG)
    forward = jnp.asarray(full_table).astype(jnp.bfloat16)
    inverse = jnp.asarray(np.ascontiguousarray(full_table.T))

    packed = class_lists.T
    all_packed = lax.all_to_all(
        jnp.broadcast_to(packed[None], (dp_count,) + packed.shape), "dp", 0, 0, tiled=True
    )
    image_rows = images.shape[0] * NSHELL
    ref_rows = col_classes * NSHELL
    wrow = shell_weight[:, None]
    params = pltpu.CompilerParams(vmem_limit_bytes=60 * 1024 * 1024)
    anywhere = pl.BlockSpec(memory_space=pl.MemorySpace.ANY)
    cross_c, image_hat, ref_hat, count_arr, ent_p, ent_k, ent_e, local_class = pl.pallas_call(
        cross_kernel,
        out_shape=(
            jax.ShapeDtypeStruct((entries, row_width), F32),
            jax.ShapeDtypeStruct((image_rows, row_width), jnp.bfloat16),
            jax.ShapeDtypeStruct((ref_rows, row_width), jnp.bfloat16),
            jax.ShapeDtypeStruct((1,), jnp.int32),
            jax.ShapeDtypeStruct((entries,), jnp.int32),
            jax.ShapeDtypeStruct((entries,), jnp.int32),
            jax.ShapeDtypeStruct((entries,), jnp.int32),
            jax.ShapeDtypeStruct((entries,), jnp.int32),
        ),
        in_specs=[smem(), smem(), smem(), anywhere, anywhere, vmem(), vmem()],
        out_specs=(vmem(), anywhere, anywhere, smem(), smem(), smem(), smem(), smem()),
        scratch_shapes=[
            pltpu.VMEM((image_rows, row_width), jnp.bfloat16),
            pltpu.VMEM((ref_rows, row_width), jnp.bfloat16),
            pltpu.VMEM((image_rows, row_width), jnp.bfloat16),
            pltpu.VMEM((ref_rows, row_width), jnp.bfloat16),
            pltpu.VMEM((ref_rows, row_width), jnp.bfloat16),
            pltpu.SemaphoreType.DMA(((image_rows + ref_rows) // CHUNK,)),
            pltpu.SemaphoreType.DMA(((image_rows + ref_rows) // CHUNK,)),
        ],
        compiler_params=params,
    )(
        all_packed.reshape(-1), pose_slot, column.astype(jnp.int32).reshape(1),
        images.reshape(image_rows, row_width), references.reshape(ref_rows, row_width),
        forward, wrow,
    )
    inside = (local_class >= 0) & (local_class < col_classes)
    safe_class = jnp.clip(local_class, 0, col_classes - 1)

    log_prior = jnp.log1p(class_counts.astype(F32))
    prior = jnp.sum(
        jnp.where(safe_class[:, None] == jnp.arange(col_classes)[None, :], log_prior[None, :], 0.0),
        axis=1,
    )
    scores_c = jnp.dot(cross_c, rotation_response.T, precision=HIGHEST)
    scores = scores_c + prior[:, None]
    scores = jnp.where(inside[:, None], scores, -1e30).reshape(blocksize, LIST, -1)
    inside_pa = inside.reshape(blocksize, LIST)
    top_local = jnp.max(scores, axis=(1, 2))
    total_local = jnp.sum(
        jnp.where(inside_pa[..., None], jnp.exp(scores - top_local[:, None, None]), 0.0), axis=(1, 2)
    )
    gathered = lax.all_gather(jnp.stack([top_local, total_local]), "cls")
    tops = gathered[:, 0]
    totals = gathered[:, 1]
    top_score = jnp.max(tops, axis=0)
    total_sum = jnp.sum(totals * jnp.exp(tops - top_score[None]), axis=0)
    posterior = (
        jnp.where(inside_pa[..., None], jnp.exp(scores - top_score[:, None, None]), 0.0)
        / total_sum[:, None, None]
    )
    evidence = top_score + jnp.log(total_sum)
    post_sum = jnp.sum(posterior, axis=2).reshape(entries)

    rot_re = rotation_response[:, :NANG]
    rot_im = rotation_response[:, NANG:]
    coef_table = jnp.concatenate([rot_re, -rot_im, rot_re * rot_re + rot_im * rot_im], axis=1)
    coef = jnp.dot(posterior.reshape(entries, -1), coef_table, precision=HIGHEST)

    class_pick = (
        (local_class[None, :] == jnp.arange(col_classes, dtype=jnp.int32)[:, None]) & inside[None, :]
    ).astype(F32)
    volume = jnp.dot(class_pick, coef[:, row_width:], precision=HIGHEST)
    denom_part = jnp.dot(class_pick, post_sum, precision=HIGHEST)
    volume_full = jnp.concatenate([volume, volume], axis=1)
    numer = pl.pallas_call(
        grad_kernel,
        out_shape=jax.ShapeDtypeStruct((ref_rows, row_width), jnp.bfloat16),
        in_specs=[smem(), smem(), smem(), smem(), anywhere, vmem(), anywhere, vmem()],
        out_specs=anywhere,
        scratch_shapes=[
            pltpu.VMEM((image_rows, row_width), jnp.bfloat16),
            pltpu.VMEM((ref_rows, row_width), jnp.bfloat16),
            pltpu.VMEM((ref_rows, row_width), F32),
            pltpu.VMEM((ref_rows, row_width), jnp.bfloat16),
            pltpu.SemaphoreType.DMA(((image_rows + ref_rows) // CHUNK,)),
            pltpu.SemaphoreType.DMA((ref_rows // CHUNK,)),
        ],
        compiler_params=params,
    )(count_arr, ent_p, ent_k, ent_e, image_hat, coef[:, :row_width], ref_hat, volume_full)

    core = dp_index % 2
    dest = pose_slot // blocksize
    dest_hit = dest[None, :] == jnp.arange(dp_count, dtype=jnp.int32)[:, None]
    dest_i = dest_hit.astype(jnp.int32)
    within = jnp.sum((jnp.cumsum(dest_i, axis=1) - dest_i) * dest_i, axis=0)
    sel = dest_hit[:, None, :] & (
        within[None, None, :] == jnp.arange(per_pair, dtype=jnp.int32)[None, :, None]
    )
    send_ev = jnp.sum(jnp.where(sel, evidence[None, None, :], 0.0), axis=2)
    send_pos = jnp.sum(jnp.where(sel, (pose_slot % blocksize).astype(F32)[None, None, :], 0.0), axis=2)
    send_den = denom_part.reshape(dp_count, per_owner)
    ev_hi, ev_lo = split_pair(send_ev)
    den_hi, den_lo = split_pair(send_den)
    small = jnp.concatenate(
        [ev_hi, ev_lo, send_pos.astype(jnp.bfloat16), den_hi, den_lo], axis=1
    )
    slot_w = small.shape[1]
    small_row = lax.dynamic_update_slice(
        jnp.zeros((dp_count, row_width), jnp.bfloat16), small, (0, core * slot_w)
    )
    extra = jnp.zeros((dp_count, EXTRA, row_width), jnp.bfloat16).at[:, 0, :].set(small_row)
    chunk_rows = per_owner * NSHELL
    chunks = jnp.concatenate(
        [numer.reshape(dp_count, chunk_rows, row_width), extra], axis=1
    )

    by_core = chunks.reshape(dp_count // 2, 2, chunk_rows + EXTRA, row_width)
    keep = lax.dynamic_index_in_dim(by_core, core, axis=1, keepdims=False)
    give = lax.dynamic_index_in_dim(by_core, 1 - core, axis=1, keepdims=False)
    taken = lax.ppermute(give, "dp", perm=[(i, i ^ 1) for i in range(dp_count)])
    pair_sum = (keep.astype(F32) + taken.astype(F32)).astype(jnp.bfloat16)
    groups = [list(range(q, dp_count, 2)) for q in range(2)]
    arrived = lax.all_to_all(
        pair_sum, "dp", split_axis=0, concat_axis=0, tiled=True, axis_index_groups=groups
    )
    summed = jnp.sum(arrived[:, :chunk_rows].astype(F32), axis=0)
    summed = jnp.dot(summed, inverse, precision=HIGHEST).reshape(per_owner, NSHELL, row_width)

    got = arrived[:, chunk_rows, : 2 * slot_w].astype(F32).reshape(dp_count, slot_w)
    got_ev = (got[:, :per_pair] + got[:, per_pair : 2 * per_pair]).reshape(-1)
    got_pos = got[:, 2 * per_pair : 3 * per_pair].reshape(-1)
    den_at = 3 * per_pair
    own_denom = jnp.sum(
        got[:, den_at : den_at + per_owner] + got[:, den_at + per_owner : den_at + 2 * per_owner],
        axis=0,
    )
    gradient = summed / (1.0 + own_denom)[:, None, None]
    rows = jnp.arange(blocksize, dtype=F32)
    placed = jnp.sum(jnp.where(got_pos[None, :] == rows[:, None], got_ev[None, :], 0.0), axis=1)
    return (gradient[None], placed)


def solution(mesh):
    return jax.shard_map(
        local,
        mesh=mesh,
        in_specs=(
            P("dp", None, None),
            P("dp"),
            P("cls", None, None),
            P(),
            P(),
            P("dp", None),
            P("cls"),
        ),
        out_specs=(P("cls", "dp", None, None), P("dp")),
        check_vma=False,
    )
```

```python
import math

import jax
import numpy as np
import jax.numpy as jnp
from jax import lax
from jax.experimental import pallas as pl
from jax.experimental.pallas import tpu as pltpu
from jax.sharding import PartitionSpec as P

NSHELL = 64
NANG = 256
LIST = 2

HIGHEST = lax.Precision.HIGHEST
F32 = jnp.float32


def table_constant(points):
    positions = np.arange(points, dtype=np.int32)
    product = positions[:, None] * positions[None, :] % points
    angles = product.astype(np.float32) * np.float32(2.0 * math.pi / points)
    scale = np.float32(math.sqrt(points))
    cosine = np.cos(angles) / scale
    sine_part = np.sin(angles) / scale
    upper_half = np.concatenate([cosine, -sine_part], axis=1)
    lower_half = np.concatenate([sine_part, cosine], axis=1)
    return np.concatenate([upper_half, lower_half], axis=0).astype(np.float32)


def angular_tables(points):
    positions = jnp.arange(points, dtype=jnp.int32)
    product = positions[:, None] * positions[None, :] % points
    angles = product.astype(jnp.float32) * (2.0 * math.pi / points)
    cosine = jnp.cos(angles) / math.sqrt(points)
    sine_part = jnp.sin(angles) / math.sqrt(points)
    upper_half = jnp.concatenate([cosine, -sine_part], axis=1)
    lower_half = jnp.concatenate([sine_part, cosine], axis=1)
    return jnp.concatenate([upper_half, lower_half], axis=0)


CHUNK = 512
EXTRA = 16


def cross_kernel(
    packed_ref, pose_ref, column_ref, image_hbm, refs_hbm, forward_ref, wrow_ref,
    cross_ref, image_hat_hbm, ref_hat_hbm, count_ref, ent_p_ref, ent_k_ref, ent_e_ref, class_ref,
    image_buf, refs_buf, hat_buf, ref_hat_buf, weighted_ref, in_sem, out_sem,
):
    n_image = image_buf.shape[0] // CHUNK
    n_ref = refs_buf.shape[0] // CHUNK
    n_particle = pose_ref.shape[0]
    n_class = refs_buf.shape[0] // NSHELL

    def rows(c):
        return pl.ds(c * CHUNK, CHUNK)

    loads = []
    for c in range(n_ref):
        copy = pltpu.make_async_copy(refs_hbm.at[rows(c)], refs_buf.at[rows(c)], in_sem.at[c])
        copy.start()
        loads.append(copy)
    for c in range(n_image):
        copy = pltpu.make_async_copy(
            image_hbm.at[rows(c)], image_buf.at[rows(c)], in_sem.at[n_ref + c]
        )
        copy.start()
        loads.append(copy)
    first = column_ref[0] * n_class

    def prep(p, cnt):
        slot = pose_ref[p]
        block = slot // n_particle
        for a in range(LIST):
            k = packed_ref[(block * LIST + a) * n_particle + slot - block * n_particle] - first
            e = p * LIST + a
            class_ref[e] = k
            ins = jnp.logical_and(k >= 0, k < n_class)
            ent_p_ref[cnt] = p
            ent_k_ref[cnt] = k
            ent_e_ref[cnt] = e
            cnt = cnt + ins.astype(jnp.int32)
        return cnt

    count_ref[0] = lax.fori_loop(0, n_particle, prep, 0)
    forward = forward_ref[...]
    wrow = wrow_ref[...][None]
    stores = []
    for c in range(n_ref):
        loads[c].wait()
        hat = jnp.dot(refs_buf[rows(c)], forward, preferred_element_type=F32).astype(jnp.bfloat16)
        ref_hat_buf[rows(c)] = hat
        weighted_ref[rows(c)] = (
            hat.astype(F32).reshape(-1, NSHELL, hat.shape[1]) * wrow
        ).reshape(hat.shape).astype(jnp.bfloat16)
        copy = pltpu.make_async_copy(ref_hat_buf.at[rows(c)], ref_hat_hbm.at[rows(c)], out_sem.at[c])
        copy.start()
        stores.append(copy)
    for c in range(n_image):
        loads[n_ref + c].wait()
        hat_buf[rows(c)] = jnp.dot(
            image_buf[rows(c)], forward, preferred_element_type=F32
        ).astype(jnp.bfloat16)
        copy = pltpu.make_async_copy(
            hat_buf.at[rows(c)], image_hat_hbm.at[rows(c)], out_sem.at[n_ref + c]
        )
        copy.start()
        stores.append(copy)
    cross_ref[...] = jnp.zeros_like(cross_ref)

    def body(e, carry):
        rp = pl.multiple_of(ent_p_ref[e] * NSHELL, NSHELL)
        rk = pl.multiple_of(ent_k_ref[e] * NSHELL, NSHELL)
        x = hat_buf[pl.ds(rp, NSHELL), :].astype(F32)
        w = weighted_ref[pl.ds(rk, NSHELL), :].astype(F32)
        x_re = x[:, :NANG]
        x_im = x[:, NANG:]
        w_re = w[:, :NANG]
        w_im = w[:, NANG:]
        c_re = jnp.sum(x_re * w_re + x_im * w_im, axis=0, keepdims=True)
        c_im = jnp.sum(x_im * w_re - x_re * w_im, axis=0, keepdims=True)
        cross_ref[pl.ds(ent_e_ref[e], 1), :] = jnp.concatenate([c_re, c_im], axis=1)
        return carry

    lax.fori_loop(0, count_ref[0], body, 0)
    for copy in stores:
        copy.wait()


def grad_kernel(
    count_ref, ent_p_ref, ent_k_ref, ent_e_ref, image_hat_hbm, coef_ref, ref_hat_hbm, volume_ref,
    out_hbm, image_buf, ref_buf, acc_ref, out_buf, in_sem, out_sem,
):
    n_image = image_buf.shape[0] // CHUNK
    n_ref = ref_buf.shape[0] // CHUNK
    chunk_classes = CHUNK // NSHELL

    def rows(c):
        return pl.ds(c * CHUNK, CHUNK)

    loads = []
    for c in range(n_ref):
        copy = pltpu.make_async_copy(ref_hat_hbm.at[rows(c)], ref_buf.at[rows(c)], in_sem.at[c])
        copy.start()
        loads.append(copy)
    for c in range(n_image):
        copy = pltpu.make_async_copy(
            image_hat_hbm.at[rows(c)], image_buf.at[rows(c)], in_sem.at[n_ref + c]
        )
        copy.start()
        loads.append(copy)

    acc_ref[...] = jnp.zeros_like(acc_ref)
    for c in range(n_image):
        loads[n_ref + c].wait()

    def body(e, carry):
        rp = pl.multiple_of(ent_p_ref[e] * NSHELL, NSHELL)
        rk = pl.multiple_of(ent_k_ref[e] * NSHELL, NSHELL)
        x = image_buf[pl.ds(rp, NSHELL), :].astype(F32)
        c = coef_ref[pl.ds(ent_e_ref[e], 1), pl.ds(0, 2 * NANG)]
        c_re = c[:, :NANG]
        c_im = c[:, NANG:]
        x_re = x[:, :NANG]
        x_im = x[:, NANG:]
        g_re = x_re * c_re - x_im * c_im
        g_im = x_re * c_im + x_im * c_re
        acc_ref[pl.ds(rk, NSHELL), :] = acc_ref[pl.ds(rk, NSHELL), :] + jnp.concatenate(
            [g_re, g_im], axis=1
        )
        return carry

    lax.fori_loop(0, count_ref[0], body, 0)

    stores = []
    for c in range(n_ref):
        loads[c].wait()
        vol_half = volume_ref[pl.ds(c * chunk_classes, chunk_classes), :]
        vol = jnp.concatenate([vol_half, vol_half], axis=1)[:, None, :]
        ref_part = ref_buf[rows(c)].astype(F32).reshape(chunk_classes, NSHELL, -1)
        acc_part = acc_ref[rows(c)].reshape(chunk_classes, NSHELL, -1)
        out_buf[rows(c)] = (acc_part - vol * ref_part).reshape(CHUNK, -1).astype(jnp.bfloat16)
        copy = pltpu.make_async_copy(out_buf.at[rows(c)], out_hbm.at[rows(c)], out_sem.at[c])
        copy.start()
        stores.append(copy)
    for copy in stores:
        copy.wait()


def split_pair(x):
    high = x.astype(jnp.bfloat16)
    low = (x - high.astype(F32)).astype(jnp.bfloat16)
    return high, low


def smem():
    return pl.BlockSpec(memory_space=pltpu.SMEM)


def vmem():
    return pl.BlockSpec(memory_space=pltpu.VMEM)


def local(
    images, pose_slot, references, rotation_response, shell_weight, class_lists, class_counts
):
    dp_index = lax.axis_index("dp")
    column = lax.axis_index("cls")
    dp_count = lax.axis_size("dp")
    blocksize = images.shape[0]
    col_classes = references.shape[0]
    per_owner = col_classes // dp_count
    per_pair = blocksize // dp_count
    row_width = 2 * NANG
    entries = blocksize * LIST
    full_table = table_constant(NANG)
    forward = jnp.asarray(full_table).astype(jnp.bfloat16)
    inverse = jnp.asarray(np.ascontiguousarray(full_table.T))

    packed = class_lists.T
    all_packed = lax.all_to_all(
        jnp.broadcast_to(packed[None], (dp_count,) + packed.shape), "dp", 0, 0, tiled=True
    )
    image_rows = images.shape[0] * NSHELL
    ref_rows = col_classes * NSHELL
    wrow = shell_weight[:, None]
    params = pltpu.CompilerParams(vmem_limit_bytes=60 * 1024 * 1024)
    anywhere = pl.BlockSpec(memory_space=pl.MemorySpace.ANY)
    cross_c, image_hat, ref_hat, count_arr, ent_p, ent_k, ent_e, local_class = pl.pallas_call(
        cross_kernel,
        out_shape=(
            jax.ShapeDtypeStruct((entries, row_width), F32),
            jax.ShapeDtypeStruct((image_rows, row_width), jnp.bfloat16),
            jax.ShapeDtypeStruct((ref_rows, row_width), jnp.bfloat16),
            jax.ShapeDtypeStruct((1,), jnp.int32),
            jax.ShapeDtypeStruct((entries,), jnp.int32),
            jax.ShapeDtypeStruct((entries,), jnp.int32),
            jax.ShapeDtypeStruct((entries,), jnp.int32),
            jax.ShapeDtypeStruct((entries,), jnp.int32),
        ),
        in_specs=[smem(), smem(), smem(), anywhere, anywhere, vmem(), vmem()],
        out_specs=(vmem(), anywhere, anywhere, smem(), smem(), smem(), smem(), smem()),
        scratch_shapes=[
            pltpu.VMEM((image_rows, row_width), jnp.bfloat16),
            pltpu.VMEM((ref_rows, row_width), jnp.bfloat16),
            pltpu.VMEM((image_rows, row_width), jnp.bfloat16),
            pltpu.VMEM((ref_rows, row_width), jnp.bfloat16),
            pltpu.VMEM((ref_rows, row_width), jnp.bfloat16),
            pltpu.SemaphoreType.DMA(((image_rows + ref_rows) // CHUNK,)),
            pltpu.SemaphoreType.DMA(((image_rows + ref_rows) // CHUNK,)),
        ],
        compiler_params=params,
    )(
        all_packed.reshape(-1), pose_slot, column.astype(jnp.int32).reshape(1),
        images.reshape(image_rows, row_width), references.reshape(ref_rows, row_width),
        forward, wrow,
    )
    inside = (local_class >= 0) & (local_class < col_classes)
    safe_class = jnp.clip(local_class, 0, col_classes - 1)

    log_prior = jnp.log1p(class_counts.astype(F32))
    prior = jnp.sum(
        jnp.where(safe_class[:, None] == jnp.arange(col_classes)[None, :], log_prior[None, :], 0.0),
        axis=1,
    )
    scores_c = jnp.dot(cross_c, rotation_response.T, precision=HIGHEST)
    scores = scores_c + prior[:, None]
    scores = jnp.where(inside[:, None], scores, -1e30).reshape(blocksize, LIST, -1)
    inside_pa = inside.reshape(blocksize, LIST)
    top_local = jnp.max(scores, axis=(1, 2))
    total_local = jnp.sum(
        jnp.where(inside_pa[..., None], jnp.exp(scores - top_local[:, None, None]), 0.0), axis=(1, 2)
    )
    gathered = lax.all_gather(jnp.stack([top_local, total_local]), "cls")
    tops = gathered[:, 0]
    totals = gathered[:, 1]
    top_score = jnp.max(tops, axis=0)
    total_sum = jnp.sum(totals * jnp.exp(tops - top_score[None]), axis=0)
    posterior = (
        jnp.where(inside_pa[..., None], jnp.exp(scores - top_score[:, None, None]), 0.0)
        / total_sum[:, None, None]
    )
    evidence = top_score + jnp.log(total_sum)
    post_sum = jnp.sum(posterior, axis=2).reshape(entries)

    rot_re = rotation_response[:, :NANG]
    rot_im = rotation_response[:, NANG:]
    coef_table = jnp.concatenate([rot_re, -rot_im, rot_re * rot_re + rot_im * rot_im], axis=1)
    coef = jnp.dot(posterior.reshape(entries, -1), coef_table, precision=HIGHEST)

    class_pick = (
        (local_class[None, :] == jnp.arange(col_classes, dtype=jnp.int32)[:, None]) & inside[None, :]
    ).astype(F32)
    volume = jnp.dot(class_pick, coef[:, row_width:], precision=HIGHEST)
    denom_part = jnp.dot(class_pick, post_sum, precision=HIGHEST)
    numer = pl.pallas_call(
        grad_kernel,
        out_shape=jax.ShapeDtypeStruct((ref_rows, row_width), jnp.bfloat16),
        in_specs=[smem(), smem(), smem(), smem(), anywhere, vmem(), anywhere, vmem()],
        out_specs=anywhere,
        scratch_shapes=[
            pltpu.VMEM((image_rows, row_width), jnp.bfloat16),
            pltpu.VMEM((ref_rows, row_width), jnp.bfloat16),
            pltpu.VMEM((ref_rows, row_width), F32),
            pltpu.VMEM((ref_rows, row_width), jnp.bfloat16),
            pltpu.SemaphoreType.DMA(((image_rows + ref_rows) // CHUNK,)),
            pltpu.SemaphoreType.DMA((ref_rows // CHUNK,)),
        ],
        compiler_params=params,
    )(count_arr, ent_p, ent_k, ent_e, image_hat, coef, ref_hat, volume)

    core = dp_index % 2
    dest = pose_slot // blocksize
    dest_hit = dest[None, :] == jnp.arange(dp_count, dtype=jnp.int32)[:, None]
    dest_i = dest_hit.astype(jnp.int32)
    within = jnp.sum((jnp.cumsum(dest_i, axis=1) - dest_i) * dest_i, axis=0)
    sel = dest_hit[:, None, :] & (
        within[None, None, :] == jnp.arange(per_pair, dtype=jnp.int32)[None, :, None]
    )
    send_ev = jnp.sum(jnp.where(sel, evidence[None, None, :], 0.0), axis=2)
    send_pos = jnp.sum(jnp.where(sel, (pose_slot % blocksize).astype(F32)[None, None, :], 0.0), axis=2)
    send_den = denom_part.reshape(dp_count, per_owner)
    ev_hi, ev_lo = split_pair(send_ev)
    den_hi, den_lo = split_pair(send_den)
    small = jnp.concatenate(
        [ev_hi, ev_lo, send_pos.astype(jnp.bfloat16), den_hi, den_lo], axis=1
    )
    slot_w = small.shape[1]
    small_row = lax.dynamic_update_slice(
        jnp.zeros((dp_count, row_width), jnp.bfloat16), small, (0, core * slot_w)
    )
    extra = jnp.zeros((dp_count, EXTRA, row_width), jnp.bfloat16).at[:, 0, :].set(small_row)
    chunk_rows = per_owner * NSHELL
    chunks = jnp.concatenate(
        [numer.reshape(dp_count, chunk_rows, row_width), extra], axis=1
    )

    by_core = chunks.reshape(dp_count // 2, 2, chunk_rows + EXTRA, row_width)
    keep = lax.dynamic_index_in_dim(by_core, core, axis=1, keepdims=False)
    give = lax.dynamic_index_in_dim(by_core, 1 - core, axis=1, keepdims=False)
    taken = lax.ppermute(give, "dp", perm=[(i, i ^ 1) for i in range(dp_count)])
    pair_sum = (keep.astype(F32) + taken.astype(F32)).astype(jnp.bfloat16)
    groups = [list(range(q, dp_count, 2)) for q in range(2)]
    arrived = lax.all_to_all(
        pair_sum, "dp", split_axis=0, concat_axis=0, tiled=True, axis_index_groups=groups
    )
    summed = jnp.sum(arrived[:, :chunk_rows].astype(F32), axis=0)
    summed = jnp.dot(summed, inverse, precision=HIGHEST).reshape(per_owner, NSHELL, row_width)

    got = arrived[:, chunk_rows, : 2 * slot_w].astype(F32).reshape(dp_count, slot_w)
    got_ev = (got[:, :per_pair] + got[:, per_pair : 2 * per_pair]).reshape(-1)
    got_pos = got[:, 2 * per_pair : 3 * per_pair].reshape(-1)
    den_at = 3 * per_pair
    own_denom = jnp.sum(
        got[:, den_at : den_at + per_owner] + got[:, den_at + per_owner : den_at + 2 * per_owner],
        axis=0,
    )
    gradient = summed / (1.0 + own_denom)[:, None, None]
    rows = jnp.arange(blocksize, dtype=F32)
    placed = jnp.sum(jnp.where(got_pos[None, :] == rows[:, None], got_ev[None, :], 0.0), axis=1)
    return (gradient[None], placed)


def solution(mesh):
    return jax.shard_map(
        local,
        mesh=mesh,
        in_specs=(
            P("dp", None, None),
            P("dp"),
            P("cls", None, None),
            P(),
            P(),
            P("dp", None),
            P("cls"),
        ),
        out_specs=(P("cls", "dp", None, None), P("dp")),
        check_vma=False,
    )
```

```python
import math

import jax
import numpy as np
import jax.numpy as jnp
from jax import lax
from jax.experimental import pallas as pl
from jax.experimental.pallas import tpu as pltpu
from jax.sharding import PartitionSpec as P

NSHELL = 64
NANG = 256
LIST = 2

HIGHEST = lax.Precision.HIGHEST
F32 = jnp.float32


def table_constant(points):
    positions = np.arange(points, dtype=np.int32)
    product = positions[:, None] * positions[None, :] % points
    angles = product.astype(np.float32) * np.float32(2.0 * math.pi / points)
    scale = np.float32(math.sqrt(points))
    cosine = np.cos(angles) / scale
    sine_part = np.sin(angles) / scale
    upper_half = np.concatenate([cosine, -sine_part], axis=1)
    lower_half = np.concatenate([sine_part, cosine], axis=1)
    return np.concatenate([upper_half, lower_half], axis=0).astype(np.float32)


def angular_tables(points):
    positions = jnp.arange(points, dtype=jnp.int32)
    product = positions[:, None] * positions[None, :] % points
    angles = product.astype(jnp.float32) * (2.0 * math.pi / points)
    cosine = jnp.cos(angles) / math.sqrt(points)
    sine_part = jnp.sin(angles) / math.sqrt(points)
    upper_half = jnp.concatenate([cosine, -sine_part], axis=1)
    lower_half = jnp.concatenate([sine_part, cosine], axis=1)
    return jnp.concatenate([upper_half, lower_half], axis=0)


CHUNK = 512
EXTRA = 16


def cross_kernel(
    packed_ref, pose_ref, column_ref, image_hbm, refs_hbm, forward_ref, wrow_ref,
    cross_ref, image_hat_hbm, ref_hat_hbm, count_ref, ent_p_ref, ent_k_ref, ent_e_ref, class_ref,
    image_buf, refs_buf, hat_buf, ref_hat_buf, weighted_ref, in_sem, out_sem,
):
    n_image = image_buf.shape[0] // CHUNK
    n_ref = refs_buf.shape[0] // CHUNK
    n_particle = pose_ref.shape[0]
    n_class = refs_buf.shape[0] // NSHELL

    def rows(c):
        return pl.ds(c * CHUNK, CHUNK)

    loads = []
    for c in range(n_ref):
        copy = pltpu.make_async_copy(refs_hbm.at[rows(c)], refs_buf.at[rows(c)], in_sem.at[c])
        copy.start()
        loads.append(copy)
    for c in range(n_image):
        copy = pltpu.make_async_copy(
            image_hbm.at[rows(c)], image_buf.at[rows(c)], in_sem.at[n_ref + c]
        )
        copy.start()
        loads.append(copy)
    first = column_ref[0] * n_class

    def prep(p, cnt):
        slot = pose_ref[p]
        block = slot // n_particle
        for a in range(LIST):
            k = packed_ref[(block * LIST + a) * n_particle + slot - block * n_particle] - first
            e = p * LIST + a
            class_ref[e] = k
            ins = jnp.logical_and(k >= 0, k < n_class)
            ent_p_ref[cnt] = p
            ent_k_ref[cnt] = k
            ent_e_ref[cnt] = e
            cnt = cnt + ins.astype(jnp.int32)
        return cnt

    count_ref[0] = lax.fori_loop(0, n_particle, prep, 0)
    forward = forward_ref[...]
    wrow = wrow_ref[...][None]
    stores = []
    for c in range(n_ref):
        loads[c].wait()
        hat = jnp.dot(refs_buf[rows(c)], forward, preferred_element_type=F32).astype(jnp.bfloat16)
        ref_hat_buf[rows(c)] = hat
        weighted_ref[rows(c)] = (
            hat.astype(F32).reshape(-1, NSHELL, hat.shape[1]) * wrow
        ).reshape(hat.shape).astype(jnp.bfloat16)
        copy = pltpu.make_async_copy(ref_hat_buf.at[rows(c)], ref_hat_hbm.at[rows(c)], out_sem.at[c])
        copy.start()
        stores.append(copy)
    for c in range(n_image):
        loads[n_ref + c].wait()
        hat_buf[rows(c)] = jnp.dot(
            image_buf[rows(c)], forward, preferred_element_type=F32
        ).astype(jnp.bfloat16)
        copy = pltpu.make_async_copy(
            hat_buf.at[rows(c)], image_hat_hbm.at[rows(c)], out_sem.at[n_ref + c]
        )
        copy.start()
        stores.append(copy)
    cross_ref[...] = jnp.zeros_like(cross_ref)

    def body(e, carry):
        rp = pl.multiple_of(ent_p_ref[e] * NSHELL, NSHELL)
        rk = pl.multiple_of(ent_k_ref[e] * NSHELL, NSHELL)
        x = hat_buf[pl.ds(rp, NSHELL), :].astype(F32)
        w = weighted_ref[pl.ds(rk, NSHELL), :].astype(F32)
        x_re = x[:, :NANG]
        x_im = x[:, NANG:]
        w_re = w[:, :NANG]
        w_im = w[:, NANG:]
        c_re = jnp.sum(x_re * w_re + x_im * w_im, axis=0, keepdims=True)
        c_im = jnp.sum(x_im * w_re - x_re * w_im, axis=0, keepdims=True)
        cross_ref[pl.ds(ent_e_ref[e], 1), :] = jnp.concatenate([c_re, c_im], axis=1)
        return carry

    lax.fori_loop(0, count_ref[0], body, 0)
    for copy in stores:
        copy.wait()


def grad_kernel(
    count_ref, ent_p_ref, ent_k_ref, ent_e_ref, core_ref, image_hat_hbm, coef_ref, ref_hat_hbm,
    volume_ref, extra_ref, give_hbm, keep_hbm, image_buf, ref_buf, acc_ref, out_buf, in_sem, out_sem,
):
    n_image = image_buf.shape[0] // CHUNK
    n_ref = ref_buf.shape[0] // CHUNK
    chunk_classes = CHUNK // NSHELL

    def rows(c):
        return pl.ds(c * CHUNK, CHUNK)

    loads = []
    for c in range(n_ref):
        copy = pltpu.make_async_copy(ref_hat_hbm.at[rows(c)], ref_buf.at[rows(c)], in_sem.at[c])
        copy.start()
        loads.append(copy)
    for c in range(n_image):
        copy = pltpu.make_async_copy(
            image_hat_hbm.at[rows(c)], image_buf.at[rows(c)], in_sem.at[n_ref + c]
        )
        copy.start()
        loads.append(copy)

    acc_ref[...] = jnp.zeros_like(acc_ref)
    for c in range(n_image):
        loads[n_ref + c].wait()

    def body(e, carry):
        rp = pl.multiple_of(ent_p_ref[e] * NSHELL, NSHELL)
        rk = pl.multiple_of(ent_k_ref[e] * NSHELL, NSHELL)
        x = image_buf[pl.ds(rp, NSHELL), :].astype(F32)
        c = coef_ref[pl.ds(ent_e_ref[e], 1), pl.ds(0, 2 * NANG)]
        c_re = c[:, :NANG]
        c_im = c[:, NANG:]
        x_re = x[:, :NANG]
        x_im = x[:, NANG:]
        g_re = x_re * c_re - x_im * c_im
        g_im = x_re * c_im + x_im * c_re
        acc_ref[pl.ds(rk, NSHELL), :] = acc_ref[pl.ds(rk, NSHELL), :] + jnp.concatenate(
            [g_re, g_im], axis=1
        )
        return carry

    lax.fori_loop(0, count_ref[0], body, 0)

    for c in range(n_ref):
        loads[c].wait()
    core = core_ref[0]
    owner_rows = 2 * NSHELL
    n_chip = give_hbm.shape[0]
    stores = []
    for i in range(n_chip):
        for h, target in enumerate((give_hbm, keep_hbm)):
            owner = 2 * i + (1 - core if h == 0 else core)
            r = pl.multiple_of(owner * owner_rows, owner_rows)
            vol_half = volume_ref[owner]
            vol = jnp.concatenate([vol_half, vol_half], axis=1)[:, None, :]
            ref_part = ref_buf[pl.ds(r, owner_rows), :].astype(F32).reshape(2, NSHELL, -1)
            acc_part = acc_ref[pl.ds(r, owner_rows), :].reshape(2, NSHELL, -1)
            out_buf[pl.ds(r, owner_rows), :] = (
                (acc_part - vol * ref_part).reshape(owner_rows, -1).astype(jnp.bfloat16)
            )
            slot = 2 * i + h
            copy = pltpu.make_async_copy(
                out_buf.at[pl.ds(r, owner_rows)], target.at[i, pl.ds(0, owner_rows)], out_sem.at[slot]
            )
            copy.start()
            stores.append(copy)
            copy = pltpu.make_async_copy(
                extra_ref.at[owner], target.at[i, pl.ds(owner_rows, EXTRA)],
                out_sem.at[2 * n_chip + slot],
            )
            copy.start()
            stores.append(copy)
    for copy in stores:
        copy.wait()


def split_pair(x):
    high = x.astype(jnp.bfloat16)
    low = (x - high.astype(F32)).astype(jnp.bfloat16)
    return high, low


def smem():
    return pl.BlockSpec(memory_space=pltpu.SMEM)


def vmem():
    return pl.BlockSpec(memory_space=pltpu.VMEM)


def local(
    images, pose_slot, references, rotation_response, shell_weight, class_lists, class_counts
):
    dp_index = lax.axis_index("dp")
    column = lax.axis_index("cls")
    dp_count = lax.axis_size("dp")
    blocksize = images.shape[0]
    col_classes = references.shape[0]
    per_owner = col_classes // dp_count
    per_pair = blocksize // dp_count
    row_width = 2 * NANG
    entries = blocksize * LIST
    full_table = table_constant(NANG)
    forward = jnp.asarray(full_table).astype(jnp.bfloat16)
    inverse = jnp.asarray(np.ascontiguousarray(full_table.T))

    packed = class_lists.T
    all_packed = lax.all_to_all(
        jnp.broadcast_to(packed[None], (dp_count,) + packed.shape), "dp", 0, 0, tiled=True
    )
    image_rows = images.shape[0] * NSHELL
    ref_rows = col_classes * NSHELL
    wrow = shell_weight[:, None]
    params = pltpu.CompilerParams(vmem_limit_bytes=60 * 1024 * 1024)
    anywhere = pl.BlockSpec(memory_space=pl.MemorySpace.ANY)
    cross_c, image_hat, ref_hat, count_arr, ent_p, ent_k, ent_e, local_class = pl.pallas_call(
        cross_kernel,
        out_shape=(
            jax.ShapeDtypeStruct((entries, row_width), F32),
            jax.ShapeDtypeStruct((image_rows, row_width), jnp.bfloat16),
            jax.ShapeDtypeStruct((ref_rows, row_width), jnp.bfloat16),
            jax.ShapeDtypeStruct((1,), jnp.int32),
            jax.ShapeDtypeStruct((entries,), jnp.int32),
            jax.ShapeDtypeStruct((entries,), jnp.int32),
            jax.ShapeDtypeStruct((entries,), jnp.int32),
            jax.ShapeDtypeStruct((entries,), jnp.int32),
        ),
        in_specs=[smem(), smem(), smem(), anywhere, anywhere, vmem(), vmem()],
        out_specs=(vmem(), anywhere, anywhere, smem(), smem(), smem(), smem(), smem()),
        scratch_shapes=[
            pltpu.VMEM((image_rows, row_width), jnp.bfloat16),
            pltpu.VMEM((ref_rows, row_width), jnp.bfloat16),
            pltpu.VMEM((image_rows, row_width), jnp.bfloat16),
            pltpu.VMEM((ref_rows, row_width), jnp.bfloat16),
            pltpu.VMEM((ref_rows, row_width), jnp.bfloat16),
            pltpu.SemaphoreType.DMA(((image_rows + ref_rows) // CHUNK,)),
            pltpu.SemaphoreType.DMA(((image_rows + ref_rows) // CHUNK,)),
        ],
        compiler_params=params,
    )(
        all_packed.reshape(-1), pose_slot, column.astype(jnp.int32).reshape(1),
        images.reshape(image_rows, row_width), references.reshape(ref_rows, row_width),
        forward, wrow,
    )
    inside = (local_class >= 0) & (local_class < col_classes)
    safe_class = jnp.clip(local_class, 0, col_classes - 1)

    log_prior = jnp.log1p(class_counts.astype(F32))
    prior = jnp.sum(
        jnp.where(safe_class[:, None] == jnp.arange(col_classes)[None, :], log_prior[None, :], 0.0),
        axis=1,
    )
    scores_c = jnp.dot(cross_c, rotation_response.T, precision=HIGHEST)
    scores = scores_c + prior[:, None]
    scores = jnp.where(inside[:, None], scores, -1e30).reshape(blocksize, LIST, -1)
    inside_pa = inside.reshape(blocksize, LIST)
    top_local = jnp.max(scores, axis=(1, 2))
    total_local = jnp.sum(
        jnp.where(inside_pa[..., None], jnp.exp(scores - top_local[:, None, None]), 0.0), axis=(1, 2)
    )
    gathered = lax.all_gather(jnp.stack([top_local, total_local]), "cls")
    tops = gathered[:, 0]
    totals = gathered[:, 1]
    top_score = jnp.max(tops, axis=0)
    total_sum = jnp.sum(totals * jnp.exp(tops - top_score[None]), axis=0)
    posterior = (
        jnp.where(inside_pa[..., None], jnp.exp(scores - top_score[:, None, None]), 0.0)
        / total_sum[:, None, None]
    )
    evidence = top_score + jnp.log(total_sum)
    post_sum = jnp.sum(posterior, axis=2).reshape(entries)

    rot_re = rotation_response[:, :NANG]
    rot_im = rotation_response[:, NANG:]
    coef_table = jnp.concatenate([rot_re, -rot_im, rot_re * rot_re + rot_im * rot_im], axis=1)
    coef = jnp.dot(posterior.reshape(entries, -1), coef_table, precision=HIGHEST)

    class_pick = (
        (local_class[None, :] == jnp.arange(col_classes, dtype=jnp.int32)[:, None]) & inside[None, :]
    ).astype(F32)
    volume = jnp.dot(class_pick, coef[:, row_width:], precision=HIGHEST)
    denom_part = jnp.dot(class_pick, post_sum, precision=HIGHEST)
    core = dp_index % 2
    dest = pose_slot // blocksize
    dest_hit = dest[None, :] == jnp.arange(dp_count, dtype=jnp.int32)[:, None]
    dest_i = dest_hit.astype(jnp.int32)
    within = jnp.sum((jnp.cumsum(dest_i, axis=1) - dest_i) * dest_i, axis=0)
    sel = dest_hit[:, None, :] & (
        within[None, None, :] == jnp.arange(per_pair, dtype=jnp.int32)[None, :, None]
    )
    send_ev = jnp.sum(jnp.where(sel, evidence[None, None, :], 0.0), axis=2)
    send_pos = jnp.sum(jnp.where(sel, (pose_slot % blocksize).astype(F32)[None, None, :], 0.0), axis=2)
    send_den = denom_part.reshape(dp_count, per_owner)
    ev_hi, ev_lo = split_pair(send_ev)
    den_hi, den_lo = split_pair(send_den)
    small = jnp.concatenate(
        [ev_hi, ev_lo, send_pos.astype(jnp.bfloat16), den_hi, den_lo], axis=1
    )
    slot_w = small.shape[1]
    small_row = lax.dynamic_update_slice(
        jnp.zeros((dp_count, row_width), jnp.bfloat16), small, (0, core * slot_w)
    )
    extra = jnp.zeros((dp_count, EXTRA, row_width), jnp.bfloat16).at[:, 0, :].set(small_row)
    chunk_rows = per_owner * NSHELL
    half_shape = jax.ShapeDtypeStruct((dp_count // 2, chunk_rows + EXTRA, row_width), jnp.bfloat16)
    give, keep = pl.pallas_call(
        grad_kernel,
        out_shape=(half_shape, half_shape),
        in_specs=[smem(), smem(), smem(), smem(), smem(), anywhere, vmem(), anywhere, vmem(), vmem()],
        out_specs=(anywhere, anywhere),
        scratch_shapes=[
            pltpu.VMEM((image_rows, row_width), jnp.bfloat16),
            pltpu.VMEM((ref_rows, row_width), jnp.bfloat16),
            pltpu.VMEM((ref_rows, row_width), F32),
            pltpu.VMEM((ref_rows, row_width), jnp.bfloat16),
            pltpu.SemaphoreType.DMA(((image_rows + ref_rows) // CHUNK,)),
            pltpu.SemaphoreType.DMA((2 * dp_count,)),
        ],
        compiler_params=params,
    )(
        count_arr, ent_p, ent_k, ent_e, core.astype(jnp.int32).reshape(1), image_hat, coef,
        ref_hat, volume.reshape(dp_count, per_owner, -1), extra,
    )

    taken = lax.ppermute(give, "dp", perm=[(i, i ^ 1) for i in range(dp_count)])
    pair_sum = (keep.astype(F32) + taken.astype(F32)).astype(jnp.bfloat16)
    groups = [list(range(q, dp_count, 2)) for q in range(2)]
    arrived = lax.all_to_all(
        pair_sum, "dp", split_axis=0, concat_axis=0, tiled=True, axis_index_groups=groups
    )
    summed = jnp.sum(arrived[:, :chunk_rows].astype(F32), axis=0)
    summed = jnp.dot(summed, inverse, precision=HIGHEST).reshape(per_owner, NSHELL, row_width)

    got = arrived[:, chunk_rows, : 2 * slot_w].astype(F32).reshape(dp_count, slot_w)
    got_ev = (got[:, :per_pair] + got[:, per_pair : 2 * per_pair]).reshape(-1)
    got_pos = got[:, 2 * per_pair : 3 * per_pair].reshape(-1)
    den_at = 3 * per_pair
    own_denom = jnp.sum(
        got[:, den_at : den_at + per_owner] + got[:, den_at + per_owner : den_at + 2 * per_owner],
        axis=0,
    )
    gradient = summed / (1.0 + own_denom)[:, None, None]
    rows = jnp.arange(blocksize, dtype=F32)
    placed = jnp.sum(jnp.where(got_pos[None, :] == rows[:, None], got_ev[None, :], 0.0), axis=1)
    return (gradient[None], placed)


def solution(mesh):
    return jax.shard_map(
        local,
        mesh=mesh,
        in_specs=(
            P("dp", None, None),
            P("dp"),
            P("cls", None, None),
            P(),
            P(),
            P("dp", None),
            P("cls"),
        ),
        out_specs=(P("cls", "dp", None, None), P("dp")),
        check_vma=False,
    )
```

```python
import math

import jax
import numpy as np
import jax.numpy as jnp
from jax import lax
from jax.experimental import pallas as pl
from jax.experimental.pallas import tpu as pltpu
from jax.sharding import PartitionSpec as P

NSHELL = 64
NANG = 256
LIST = 2

HIGHEST = lax.Precision.HIGHEST
F32 = jnp.float32


def table_constant(points):
    positions = np.arange(points, dtype=np.int32)
    product = positions[:, None] * positions[None, :] % points
    angles = product.astype(np.float32) * np.float32(2.0 * math.pi / points)
    scale = np.float32(math.sqrt(points))
    cosine = np.cos(angles) / scale
    sine_part = np.sin(angles) / scale
    upper_half = np.concatenate([cosine, -sine_part], axis=1)
    lower_half = np.concatenate([sine_part, cosine], axis=1)
    return np.concatenate([upper_half, lower_half], axis=0).astype(np.float32)


def angular_tables(points):
    positions = jnp.arange(points, dtype=jnp.int32)
    product = positions[:, None] * positions[None, :] % points
    angles = product.astype(jnp.float32) * (2.0 * math.pi / points)
    cosine = jnp.cos(angles) / math.sqrt(points)
    sine_part = jnp.sin(angles) / math.sqrt(points)
    upper_half = jnp.concatenate([cosine, -sine_part], axis=1)
    lower_half = jnp.concatenate([sine_part, cosine], axis=1)
    return jnp.concatenate([upper_half, lower_half], axis=0)


CHUNK = 512
EXTRA = 16


def cross_kernel(
    packed_ref, pose_ref, column_ref, image_hbm, refs_hbm, forward_ref, wrow_ref,
    cross_ref, image_hat_hbm, ref_hat_hbm, count_ref, ent_p_ref, ent_k_ref, ent_e_ref, class_ref,
    image_buf, refs_buf, hat_buf, ref_hat_buf, weighted_ref, in_sem, out_sem,
):
    n_image = image_buf.shape[0] // CHUNK
    n_ref = refs_buf.shape[0] // CHUNK
    n_particle = pose_ref.shape[0]
    n_class = refs_buf.shape[0] // NSHELL

    def rows(c):
        return pl.ds(c * CHUNK, CHUNK)

    loads = []
    for c in range(n_ref):
        copy = pltpu.make_async_copy(refs_hbm.at[rows(c)], refs_buf.at[rows(c)], in_sem.at[c])
        copy.start()
        loads.append(copy)
    for c in range(n_image):
        copy = pltpu.make_async_copy(
            image_hbm.at[rows(c)], image_buf.at[rows(c)], in_sem.at[n_ref + c]
        )
        copy.start()
        loads.append(copy)
    first = column_ref[0] * n_class

    def prep(p, cnt):
        slot = pose_ref[p]
        block = slot // n_particle
        for a in range(LIST):
            k = packed_ref[(block * LIST + a) * n_particle + slot - block * n_particle] - first
            e = p * LIST + a
            class_ref[e] = k
            ins = jnp.logical_and(k >= 0, k < n_class)
            ent_p_ref[cnt] = p
            ent_k_ref[cnt] = k
            ent_e_ref[cnt] = e
            cnt = cnt + ins.astype(jnp.int32)
        return cnt

    count_ref[0] = lax.fori_loop(0, n_particle, prep, 0)
    forward = forward_ref[...]
    wrow = wrow_ref[...][None]
    stores = []
    for c in range(n_ref):
        loads[c].wait()
        hat = jnp.dot(refs_buf[rows(c)], forward, preferred_element_type=F32).astype(jnp.bfloat16)
        ref_hat_buf[rows(c)] = hat
        weighted_ref[rows(c)] = (
            hat.astype(F32).reshape(-1, NSHELL, hat.shape[1]) * wrow
        ).reshape(hat.shape).astype(jnp.bfloat16)
        copy = pltpu.make_async_copy(ref_hat_buf.at[rows(c)], ref_hat_hbm.at[rows(c)], out_sem.at[c])
        copy.start()
        stores.append(copy)
    for c in range(n_image):
        loads[n_ref + c].wait()
        hat_buf[rows(c)] = jnp.dot(
            image_buf[rows(c)], forward, preferred_element_type=F32
        ).astype(jnp.bfloat16)
        copy = pltpu.make_async_copy(
            hat_buf.at[rows(c)], image_hat_hbm.at[rows(c)], out_sem.at[n_ref + c]
        )
        copy.start()
        stores.append(copy)
    cross_ref[...] = jnp.zeros_like(cross_ref)

    def body(e, carry):
        rp = pl.multiple_of(ent_p_ref[e] * NSHELL, NSHELL)
        rk = pl.multiple_of(ent_k_ref[e] * NSHELL, NSHELL)
        x = hat_buf[pl.ds(rp, NSHELL), :].astype(F32)
        w = weighted_ref[pl.ds(rk, NSHELL), :].astype(F32)
        x_re = x[:, :NANG]
        x_im = x[:, NANG:]
        w_re = w[:, :NANG]
        w_im = w[:, NANG:]
        c_re = jnp.sum(x_re * w_re + x_im * w_im, axis=0, keepdims=True)
        c_im = jnp.sum(x_im * w_re - x_re * w_im, axis=0, keepdims=True)
        cross_ref[pl.ds(ent_e_ref[e], 1), :] = jnp.concatenate([c_re, c_im], axis=1)
        return carry

    lax.fori_loop(0, count_ref[0], body, 0)
    for copy in stores:
        copy.wait()


def grad_kernel(
    count_ref, ent_p_ref, ent_k_ref, ent_e_ref, core_ref, image_hat_hbm, coef_ref, ref_hat_hbm,
    volume_ref, extra_ref, give_hbm, keep_hbm, image_buf, ref_buf, acc_ref, out_buf, in_sem, out_sem,
):
    n_image = image_buf.shape[0] // CHUNK
    n_ref = ref_buf.shape[0] // CHUNK
    chunk_classes = CHUNK // NSHELL

    def rows(c):
        return pl.ds(c * CHUNK, CHUNK)

    loads = []
    for c in range(n_ref):
        copy = pltpu.make_async_copy(ref_hat_hbm.at[rows(c)], ref_buf.at[rows(c)], in_sem.at[c])
        copy.start()
        loads.append(copy)
    for c in range(n_image):
        copy = pltpu.make_async_copy(
            image_hat_hbm.at[rows(c)], image_buf.at[rows(c)], in_sem.at[n_ref + c]
        )
        copy.start()
        loads.append(copy)

    acc_ref[...] = jnp.zeros_like(acc_ref)
    for c in range(n_image):
        loads[n_ref + c].wait()

    def body(e, carry):
        rp = pl.multiple_of(ent_p_ref[e] * NSHELL, NSHELL)
        rk = pl.multiple_of(ent_k_ref[e] * NSHELL, NSHELL)
        x = image_buf[pl.ds(rp, NSHELL), :].astype(F32)
        c = coef_ref[pl.ds(ent_e_ref[e], 1), pl.ds(0, 2 * NANG)]
        c_re = c[:, :NANG]
        c_im = c[:, NANG:]
        x_re = x[:, :NANG]
        x_im = x[:, NANG:]
        g_re = x_re * c_re - x_im * c_im
        g_im = x_re * c_im + x_im * c_re
        acc_ref[pl.ds(rk, NSHELL), :] = acc_ref[pl.ds(rk, NSHELL), :] + jnp.concatenate(
            [g_re, g_im], axis=1
        )
        return carry

    lax.fori_loop(0, count_ref[0], body, 0)

    for c in range(n_ref):
        loads[c].wait()
    core = core_ref[0]
    owner_rows = 2 * NSHELL
    chips_per_chunk = CHUNK // (2 * owner_rows)
    stores = []
    for c in range(n_ref):
        vol_half = volume_ref[pl.ds(c * chunk_classes, chunk_classes), :]
        vol = jnp.concatenate([vol_half, vol_half], axis=1)[:, None, :]
        ref_part = ref_buf[rows(c)].astype(F32).reshape(chunk_classes, NSHELL, -1)
        acc_part = acc_ref[rows(c)].reshape(chunk_classes, NSHELL, -1)
        out_buf[rows(c)] = (acc_part - vol * ref_part).reshape(CHUNK, -1).astype(jnp.bfloat16)
        for j in range(chips_per_chunk):
            i = c * chips_per_chunk + j
            for h, target in enumerate((give_hbm, keep_hbm)):
                owner = 2 * i + (1 - core if h == 0 else core)
                r = pl.multiple_of(owner * owner_rows, owner_rows)
                slot = 2 * i + h
                copy = pltpu.make_async_copy(
                    out_buf.at[pl.ds(r, owner_rows)], target.at[i, pl.ds(0, owner_rows)],
                    out_sem.at[slot],
                )
                copy.start()
                stores.append(copy)
                copy = pltpu.make_async_copy(
                    extra_ref.at[owner], target.at[i, pl.ds(owner_rows, EXTRA)],
                    out_sem.at[2 * give_hbm.shape[0] + slot],
                )
                copy.start()
                stores.append(copy)
    for copy in stores:
        copy.wait()


def split_pair(x):
    high = x.astype(jnp.bfloat16)
    low = (x - high.astype(F32)).astype(jnp.bfloat16)
    return high, low


def smem():
    return pl.BlockSpec(memory_space=pltpu.SMEM)


def vmem():
    return pl.BlockSpec(memory_space=pltpu.VMEM)


def local(
    images, pose_slot, references, rotation_response, shell_weight, class_lists, class_counts
):
    dp_index = lax.axis_index("dp")
    column = lax.axis_index("cls")
    dp_count = lax.axis_size("dp")
    blocksize = images.shape[0]
    col_classes = references.shape[0]
    per_owner = col_classes // dp_count
    per_pair = blocksize // dp_count
    row_width = 2 * NANG
    entries = blocksize * LIST
    full_table = table_constant(NANG)
    forward = jnp.asarray(full_table).astype(jnp.bfloat16)
    inverse = jnp.asarray(np.ascontiguousarray(full_table.T))

    packed = class_lists.T
    all_packed = lax.all_to_all(
        jnp.broadcast_to(packed[None], (dp_count,) + packed.shape), "dp", 0, 0, tiled=True
    )
    image_rows = images.shape[0] * NSHELL
    ref_rows = col_classes * NSHELL
    wrow = shell_weight[:, None]
    params = pltpu.CompilerParams(vmem_limit_bytes=60 * 1024 * 1024)
    anywhere = pl.BlockSpec(memory_space=pl.MemorySpace.ANY)
    cross_c, image_hat, ref_hat, count_arr, ent_p, ent_k, ent_e, local_class = pl.pallas_call(
        cross_kernel,
        out_shape=(
            jax.ShapeDtypeStruct((entries, row_width), F32),
            jax.ShapeDtypeStruct((image_rows, row_width), jnp.bfloat16),
            jax.ShapeDtypeStruct((ref_rows, row_width), jnp.bfloat16),
            jax.ShapeDtypeStruct((1,), jnp.int32),
            jax.ShapeDtypeStruct((entries,), jnp.int32),
            jax.ShapeDtypeStruct((entries,), jnp.int32),
            jax.ShapeDtypeStruct((entries,), jnp.int32),
            jax.ShapeDtypeStruct((entries,), jnp.int32),
        ),
        in_specs=[smem(), smem(), smem(), anywhere, anywhere, vmem(), vmem()],
        out_specs=(vmem(), anywhere, anywhere, smem(), smem(), smem(), smem(), smem()),
        scratch_shapes=[
            pltpu.VMEM((image_rows, row_width), jnp.bfloat16),
            pltpu.VMEM((ref_rows, row_width), jnp.bfloat16),
            pltpu.VMEM((image_rows, row_width), jnp.bfloat16),
            pltpu.VMEM((ref_rows, row_width), jnp.bfloat16),
            pltpu.VMEM((ref_rows, row_width), jnp.bfloat16),
            pltpu.SemaphoreType.DMA(((image_rows + ref_rows) // CHUNK,)),
            pltpu.SemaphoreType.DMA(((image_rows + ref_rows) // CHUNK,)),
        ],
        compiler_params=params,
    )(
        all_packed.reshape(-1), pose_slot, column.astype(jnp.int32).reshape(1),
        images.reshape(image_rows, row_width), references.reshape(ref_rows, row_width),
        forward, wrow,
    )
    inside = (local_class >= 0) & (local_class < col_classes)
    safe_class = jnp.clip(local_class, 0, col_classes - 1)

    log_prior = jnp.log1p(class_counts.astype(F32))
    prior = jnp.sum(
        jnp.where(safe_class[:, None] == jnp.arange(col_classes)[None, :], log_prior[None, :], 0.0),
        axis=1,
    )
    scores_c = jnp.dot(cross_c, rotation_response.T, precision=HIGHEST)
    scores = scores_c + prior[:, None]
    scores = jnp.where(inside[:, None], scores, -1e30).reshape(blocksize, LIST, -1)
    inside_pa = inside.reshape(blocksize, LIST)
    top_local = jnp.max(scores, axis=(1, 2))
    total_local = jnp.sum(
        jnp.where(inside_pa[..., None], jnp.exp(scores - top_local[:, None, None]), 0.0), axis=(1, 2)
    )
    gathered = lax.all_gather(jnp.stack([top_local, total_local]), "cls")
    tops = gathered[:, 0]
    totals = gathered[:, 1]
    top_score = jnp.max(tops, axis=0)
    total_sum = jnp.sum(totals * jnp.exp(tops - top_score[None]), axis=0)
    posterior = (
        jnp.where(inside_pa[..., None], jnp.exp(scores - top_score[:, None, None]), 0.0)
        / total_sum[:, None, None]
    )
    evidence = top_score + jnp.log(total_sum)
    post_sum = jnp.sum(posterior, axis=2).reshape(entries)

    rot_re = rotation_response[:, :NANG]
    rot_im = rotation_response[:, NANG:]
    coef_table = jnp.concatenate([rot_re, -rot_im, rot_re * rot_re + rot_im * rot_im], axis=1)
    coef = jnp.dot(posterior.reshape(entries, -1), coef_table, precision=HIGHEST)

    class_pick = (
        (local_class[None, :] == jnp.arange(col_classes, dtype=jnp.int32)[:, None]) & inside[None, :]
    ).astype(F32)
    volume = jnp.dot(class_pick, coef[:, row_width:], precision=HIGHEST)
    denom_part = jnp.dot(class_pick, post_sum, precision=HIGHEST)
    core = dp_index % 2
    dest = pose_slot // blocksize
    dest_hit = dest[None, :] == jnp.arange(dp_count, dtype=jnp.int32)[:, None]
    dest_i = dest_hit.astype(jnp.int32)
    within = jnp.sum((jnp.cumsum(dest_i, axis=1) - dest_i) * dest_i, axis=0)
    sel = dest_hit[:, None, :] & (
        within[None, None, :] == jnp.arange(per_pair, dtype=jnp.int32)[None, :, None]
    )
    send_ev = jnp.sum(jnp.where(sel, evidence[None, None, :], 0.0), axis=2)
    send_pos = jnp.sum(jnp.where(sel, (pose_slot % blocksize).astype(F32)[None, None, :], 0.0), axis=2)
    send_den = denom_part.reshape(dp_count, per_owner)
    ev_hi, ev_lo = split_pair(send_ev)
    den_hi, den_lo = split_pair(send_den)
    small = jnp.concatenate(
        [ev_hi, ev_lo, send_pos.astype(jnp.bfloat16), den_hi, den_lo], axis=1
    )
    slot_w = small.shape[1]
    small_row = lax.dynamic_update_slice(
        jnp.zeros((dp_count, row_width), jnp.bfloat16), small, (0, core * slot_w)
    )
    extra = jnp.zeros((dp_count, EXTRA, row_width), jnp.bfloat16).at[:, 0, :].set(small_row)
    chunk_rows = per_owner * NSHELL
    half_shape = jax.ShapeDtypeStruct((dp_count // 2, chunk_rows + EXTRA, row_width), jnp.bfloat16)
    give, keep = pl.pallas_call(
        grad_kernel,
        out_shape=(half_shape, half_shape),
        in_specs=[smem(), smem(), smem(), smem(), smem(), anywhere, vmem(), anywhere, vmem(), vmem()],
        out_specs=(anywhere, anywhere),
        scratch_shapes=[
            pltpu.VMEM((image_rows, row_width), jnp.bfloat16),
            pltpu.VMEM((ref_rows, row_width), jnp.bfloat16),
            pltpu.VMEM((ref_rows, row_width), F32),
            pltpu.VMEM((ref_rows, row_width), jnp.bfloat16),
            pltpu.SemaphoreType.DMA(((image_rows + ref_rows) // CHUNK,)),
            pltpu.SemaphoreType.DMA((2 * dp_count,)),
        ],
        compiler_params=params,
    )(
        count_arr, ent_p, ent_k, ent_e, core.astype(jnp.int32).reshape(1), image_hat, coef,
        ref_hat, volume, extra,
    )

    taken = lax.ppermute(give, "dp", perm=[(i, i ^ 1) for i in range(dp_count)])
    pair_sum = (keep.astype(F32) + taken.astype(F32)).astype(jnp.bfloat16)
    groups = [list(range(q, dp_count, 2)) for q in range(2)]
    arrived = lax.all_to_all(
        pair_sum, "dp", split_axis=0, concat_axis=0, tiled=True, axis_index_groups=groups
    )
    summed = jnp.sum(arrived[:, :chunk_rows].astype(F32), axis=0)
    summed = jnp.dot(summed, inverse, precision=HIGHEST).reshape(per_owner, NSHELL, row_width)

    got = arrived[:, chunk_rows, : 2 * slot_w].astype(F32).reshape(dp_count, slot_w)
    got_ev = (got[:, :per_pair] + got[:, per_pair : 2 * per_pair]).reshape(-1)
    got_pos = got[:, 2 * per_pair : 3 * per_pair].reshape(-1)
    den_at = 3 * per_pair
    own_denom = jnp.sum(
        got[:, den_at : den_at + per_owner] + got[:, den_at + per_owner : den_at + 2 * per_owner],
        axis=0,
    )
    gradient = summed / (1.0 + own_denom)[:, None, None]
    rows = jnp.arange(blocksize, dtype=F32)
    placed = jnp.sum(jnp.where(got_pos[None, :] == rows[:, None], got_ev[None, :], 0.0), axis=1)
    return (gradient[None], placed)


def solution(mesh):
    return jax.shard_map(
        local,
        mesh=mesh,
        in_specs=(
            P("dp", None, None),
            P("dp"),
            P("cls", None, None),
            P(),
            P(),
            P("dp", None),
            P("cls"),
        ),
        out_specs=(P("cls", "dp", None, None), P("dp")),
        check_vma=False,
    )
```

```python
import math

import jax
import numpy as np
import jax.numpy as jnp
from jax import lax
from jax.experimental import pallas as pl
from jax.experimental.pallas import tpu as pltpu
from jax.sharding import PartitionSpec as P

NSHELL = 64
NANG = 256
LIST = 2

HIGHEST = lax.Precision.HIGHEST
F32 = jnp.float32


def table_constant(points):
    positions = np.arange(points, dtype=np.int32)
    product = positions[:, None] * positions[None, :] % points
    angles = product.astype(np.float32) * np.float32(2.0 * math.pi / points)
    scale = np.float32(math.sqrt(points))
    cosine = np.cos(angles) / scale
    sine_part = np.sin(angles) / scale
    upper_half = np.concatenate([cosine, -sine_part], axis=1)
    lower_half = np.concatenate([sine_part, cosine], axis=1)
    return np.concatenate([upper_half, lower_half], axis=0).astype(np.float32)


def angular_tables(points):
    positions = jnp.arange(points, dtype=jnp.int32)
    product = positions[:, None] * positions[None, :] % points
    angles = product.astype(jnp.float32) * (2.0 * math.pi / points)
    cosine = jnp.cos(angles) / math.sqrt(points)
    sine_part = jnp.sin(angles) / math.sqrt(points)
    upper_half = jnp.concatenate([cosine, -sine_part], axis=1)
    lower_half = jnp.concatenate([sine_part, cosine], axis=1)
    return jnp.concatenate([upper_half, lower_half], axis=0)


CHUNK = 512
EXTRA = 16


def cross_kernel(
    packed_ref, pose_ref, column_ref, image_hbm, refs_hbm, forward_ref, wrow_ref,
    cross_ref, image_hat_hbm, ref_hat_hbm, count_ref, ent_p_ref, ent_k_ref, ent_e_ref, class_ref,
    image_buf, refs_buf, hat_buf, ref_hat_buf, weighted_ref, in_sem, out_sem,
):
    n_image = image_buf.shape[0] // CHUNK
    n_ref = refs_buf.shape[0] // CHUNK
    n_particle = pose_ref.shape[0]
    n_class = refs_buf.shape[0] // NSHELL

    def rows(c):
        return pl.ds(c * CHUNK, CHUNK)

    loads = []
    for c in range(n_ref):
        copy = pltpu.make_async_copy(refs_hbm.at[rows(c)], refs_buf.at[rows(c)], in_sem.at[c])
        copy.start()
        loads.append(copy)
    for c in range(n_image):
        copy = pltpu.make_async_copy(
            image_hbm.at[rows(c)], image_buf.at[rows(c)], in_sem.at[n_ref + c]
        )
        copy.start()
        loads.append(copy)
    first = column_ref[0] * n_class

    def prep(p, cnt):
        slot = pose_ref[p]
        block = slot // n_particle
        for a in range(LIST):
            k = packed_ref[(block * LIST + a) * n_particle + slot - block * n_particle] - first
            e = p * LIST + a
            class_ref[e] = k
            ins = jnp.logical_and(k >= 0, k < n_class)
            ent_p_ref[cnt] = p
            ent_k_ref[cnt] = k
            ent_e_ref[cnt] = e
            cnt = cnt + ins.astype(jnp.int32)
        return cnt

    count_ref[0] = lax.fori_loop(0, n_particle, prep, 0)
    forward = forward_ref[...]
    wrow = wrow_ref[...][None]
    stores = []
    for c in range(n_ref):
        loads[c].wait()
        hat = jnp.dot(refs_buf[rows(c)], forward, preferred_element_type=F32).astype(jnp.bfloat16)
        ref_hat_buf[rows(c)] = hat
        weighted_ref[rows(c)] = (
            hat.astype(F32).reshape(-1, NSHELL, hat.shape[1]) * wrow
        ).reshape(hat.shape).astype(jnp.bfloat16)
        copy = pltpu.make_async_copy(ref_hat_buf.at[rows(c)], ref_hat_hbm.at[rows(c)], out_sem.at[c])
        copy.start()
        stores.append(copy)
    for c in range(n_image):
        loads[n_ref + c].wait()
        hat_buf[rows(c)] = jnp.dot(
            image_buf[rows(c)], forward, preferred_element_type=F32
        ).astype(jnp.bfloat16)
        copy = pltpu.make_async_copy(
            hat_buf.at[rows(c)], image_hat_hbm.at[rows(c)], out_sem.at[n_ref + c]
        )
        copy.start()
        stores.append(copy)
    cross_ref[...] = jnp.zeros_like(cross_ref)

    def body(e, carry):
        rp = pl.multiple_of(ent_p_ref[e] * NSHELL, NSHELL)
        rk = pl.multiple_of(ent_k_ref[e] * NSHELL, NSHELL)
        x = hat_buf[pl.ds(rp, NSHELL), :].astype(F32)
        w = weighted_ref[pl.ds(rk, NSHELL), :].astype(F32)
        x_re = x[:, :NANG]
        x_im = x[:, NANG:]
        w_re = w[:, :NANG]
        w_im = w[:, NANG:]
        c_re = jnp.sum(x_re * w_re + x_im * w_im, axis=0, keepdims=True)
        c_im = jnp.sum(x_im * w_re - x_re * w_im, axis=0, keepdims=True)
        cross_ref[pl.ds(ent_e_ref[e], 1), :] = jnp.concatenate([c_re, c_im], axis=1)
        return carry

    lax.fori_loop(0, count_ref[0], body, 0)
    for copy in stores:
        copy.wait()


def grad_kernel(
    count_ref, ent_p_ref, ent_k_ref, ent_e_ref, core_ref, image_hat_hbm, coef_ref, ref_hat_hbm,
    volume_ref, extra_ref, give_hbm, keep_hbm, image_buf, ref_buf, acc_ref, out_buf, in_sem, out_sem,
):
    n_image = image_buf.shape[0] // CHUNK
    n_ref = ref_buf.shape[0] // CHUNK
    chunk_classes = CHUNK // NSHELL

    def rows(c):
        return pl.ds(c * CHUNK, CHUNK)

    loads = []
    for c in range(n_ref):
        copy = pltpu.make_async_copy(ref_hat_hbm.at[rows(c)], ref_buf.at[rows(c)], in_sem.at[c])
        copy.start()
        loads.append(copy)
    for c in range(n_image):
        copy = pltpu.make_async_copy(
            image_hat_hbm.at[rows(c)], image_buf.at[rows(c)], in_sem.at[n_ref + c]
        )
        copy.start()
        loads.append(copy)

    acc_ref[...] = jnp.zeros_like(acc_ref)
    for c in range(n_image):
        loads[n_ref + c].wait()

    def body(e, carry):
        rp = pl.multiple_of(ent_p_ref[e] * NSHELL, NSHELL)
        rk = pl.multiple_of(ent_k_ref[e] * NSHELL, NSHELL)
        x = image_buf[pl.ds(rp, NSHELL), :].astype(F32)
        c = coef_ref[pl.ds(ent_e_ref[e], 1), pl.ds(0, 2 * NANG)]
        c_re = c[:, :NANG]
        c_im = c[:, NANG:]
        x_re = x[:, :NANG]
        x_im = x[:, NANG:]
        g_re = x_re * c_re - x_im * c_im
        g_im = x_re * c_im + x_im * c_re
        acc_ref[pl.ds(rk, NSHELL), :] = acc_ref[pl.ds(rk, NSHELL), :] + jnp.concatenate(
            [g_re, g_im], axis=1
        )
        return carry

    lax.fori_loop(0, count_ref[0], body, 0)

    for c in range(n_ref):
        loads[c].wait()
    core = core_ref[0]
    owner_rows = 2 * NSHELL
    chips_per_chunk = CHUNK // (2 * owner_rows)
    stores = []
    for c in range(n_ref):
        vol_half = volume_ref[pl.ds(c * chunk_classes, chunk_classes), :]
        vol = jnp.concatenate([vol_half, vol_half], axis=1)[:, None, :]
        ref_part = ref_buf[rows(c)].astype(F32).reshape(chunk_classes, NSHELL, -1)
        acc_part = acc_ref[rows(c)].reshape(chunk_classes, NSHELL, -1)
        out_buf[rows(c)] = (acc_part - vol * ref_part).reshape(CHUNK, -1).astype(jnp.bfloat16)
        for j in range(chips_per_chunk):
            i = c * chips_per_chunk + j
            for h, target in enumerate((give_hbm, keep_hbm)):
                owner = 2 * i + (1 - core if h == 0 else core)
                r = pl.multiple_of(owner * owner_rows, owner_rows)
                slot = 2 * i + h
                copy = pltpu.make_async_copy(
                    out_buf.at[pl.ds(r, owner_rows)], target.at[i, pl.ds(0, owner_rows)],
                    out_sem.at[slot],
                )
                copy.start()
                stores.append(copy)
                copy = pltpu.make_async_copy(
                    extra_ref.at[owner], target.at[i, pl.ds(owner_rows, EXTRA)],
                    out_sem.at[2 * give_hbm.shape[0] + slot],
                )
                copy.start()
                stores.append(copy)
    for copy in stores:
        copy.wait()


def split_pair(x):
    high = x.astype(jnp.bfloat16)
    low = (x - high.astype(F32)).astype(jnp.bfloat16)
    return high, low


def smem():
    return pl.BlockSpec(memory_space=pltpu.SMEM)


def vmem():
    return pl.BlockSpec(memory_space=pltpu.VMEM)


def local(
    images, pose_slot, references, rotation_response, shell_weight, class_lists, class_counts
):
    dp_index = lax.axis_index("dp")
    column = lax.axis_index("cls")
    dp_count = lax.axis_size("dp")
    blocksize = images.shape[0]
    col_classes = references.shape[0]
    per_owner = col_classes // dp_count
    per_pair = blocksize // dp_count
    row_width = 2 * NANG
    entries = blocksize * LIST
    full_table = table_constant(NANG)
    forward = jnp.asarray(full_table).astype(jnp.bfloat16)
    inverse = jnp.asarray(np.ascontiguousarray(full_table.T))

    packed = class_lists.T
    all_packed = lax.all_to_all(
        jnp.broadcast_to(packed[None], (dp_count,) + packed.shape), "dp", 0, 0, tiled=True
    )
    image_rows = images.shape[0] * NSHELL
    ref_rows = col_classes * NSHELL
    wrow = shell_weight[:, None]
    params = pltpu.CompilerParams(vmem_limit_bytes=60 * 1024 * 1024)
    anywhere = pl.BlockSpec(memory_space=pl.MemorySpace.ANY)
    cross_c, image_hat, ref_hat, count_arr, ent_p, ent_k, ent_e, local_class = pl.pallas_call(
        cross_kernel,
        out_shape=(
            jax.ShapeDtypeStruct((entries, row_width), F32),
            jax.ShapeDtypeStruct((image_rows, row_width), jnp.bfloat16),
            jax.ShapeDtypeStruct((ref_rows, row_width), jnp.bfloat16),
            jax.ShapeDtypeStruct((1,), jnp.int32),
            jax.ShapeDtypeStruct((entries,), jnp.int32),
            jax.ShapeDtypeStruct((entries,), jnp.int32),
            jax.ShapeDtypeStruct((entries,), jnp.int32),
            jax.ShapeDtypeStruct((entries,), jnp.int32),
        ),
        in_specs=[smem(), smem(), smem(), anywhere, anywhere, vmem(), vmem()],
        out_specs=(vmem(), anywhere, anywhere, smem(), smem(), smem(), smem(), smem()),
        scratch_shapes=[
            pltpu.VMEM((image_rows, row_width), jnp.bfloat16),
            pltpu.VMEM((ref_rows, row_width), jnp.bfloat16),
            pltpu.VMEM((image_rows, row_width), jnp.bfloat16),
            pltpu.VMEM((ref_rows, row_width), jnp.bfloat16),
            pltpu.VMEM((ref_rows, row_width), jnp.bfloat16),
            pltpu.SemaphoreType.DMA(((image_rows + ref_rows) // CHUNK,)),
            pltpu.SemaphoreType.DMA(((image_rows + ref_rows) // CHUNK,)),
        ],
        compiler_params=params,
    )(
        all_packed.reshape(-1), pose_slot, column.astype(jnp.int32).reshape(1),
        images.reshape(image_rows, row_width), references.reshape(ref_rows, row_width),
        forward, wrow,
    )
    inside = (local_class >= 0) & (local_class < col_classes)
    safe_class = jnp.clip(local_class, 0, col_classes - 1)

    log_prior = jnp.log1p(class_counts.astype(F32))
    prior = jnp.sum(
        jnp.where(safe_class[:, None] == jnp.arange(col_classes)[None, :], log_prior[None, :], 0.0),
        axis=1,
    )
    scores_c = jnp.dot(cross_c, rotation_response.T, precision=HIGHEST)
    scores = scores_c + prior[:, None]
    scores = jnp.where(inside[:, None], scores, -1e30).reshape(blocksize, LIST, -1)
    inside_pa = inside.reshape(blocksize, LIST)
    top_local = jnp.max(scores, axis=(1, 2))
    total_local = jnp.sum(
        jnp.where(inside_pa[..., None], jnp.exp(scores - top_local[:, None, None]), 0.0), axis=(1, 2)
    )
    gathered = lax.all_gather(jnp.stack([top_local, total_local]), "cls")
    tops = gathered[:, 0]
    totals = gathered[:, 1]
    top_score = jnp.max(tops, axis=0)
    total_sum = jnp.sum(totals * jnp.exp(tops - top_score[None]), axis=0)
    posterior = (
        jnp.where(inside_pa[..., None], jnp.exp(scores - top_score[:, None, None]), 0.0)
        / total_sum[:, None, None]
    )
    evidence = top_score + jnp.log(total_sum)
    post_sum = jnp.sum(posterior, axis=2).reshape(entries)

    rot_re = rotation_response[:, :NANG]
    rot_im = rotation_response[:, NANG:]
    coef_table = jnp.concatenate([rot_re, -rot_im, rot_re * rot_re + rot_im * rot_im], axis=1)
    coef = jnp.dot(posterior.reshape(entries, -1), coef_table, precision=HIGHEST)

    class_pick = (
        (local_class[None, :] == jnp.arange(col_classes, dtype=jnp.int32)[:, None]) & inside[None, :]
    ).astype(F32)
    volume = jnp.dot(class_pick, coef[:, row_width:], precision=HIGHEST)
    denom_part = jnp.dot(class_pick, post_sum, precision=HIGHEST)
    core = dp_index % 2
    dest = pose_slot // blocksize
    dest_hit = dest[None, :] == jnp.arange(dp_count, dtype=jnp.int32)[:, None]
    dest_i = dest_hit.astype(jnp.int32)
    within = jnp.sum((jnp.cumsum(dest_i, axis=1) - dest_i) * dest_i, axis=0)
    sel = dest_hit[:, None, :] & (
        within[None, None, :] == jnp.arange(per_pair, dtype=jnp.int32)[None, :, None]
    )
    send_ev = jnp.sum(jnp.where(sel, evidence[None, None, :], 0.0), axis=2)
    send_pos = jnp.sum(jnp.where(sel, (pose_slot % blocksize).astype(F32)[None, None, :], 0.0), axis=2)
    send_den = denom_part.reshape(dp_count, per_owner)
    ev_hi, ev_lo = split_pair(send_ev)
    den_hi, den_lo = split_pair(send_den)
    small = jnp.concatenate(
        [ev_hi, ev_lo, send_pos.astype(jnp.bfloat16), den_hi, den_lo], axis=1
    )
    slot_w = small.shape[1]
    lane_gap = jnp.zeros((dp_count, row_width - 2 * slot_w), jnp.bfloat16)
    slot_gap = jnp.zeros((dp_count, slot_w), jnp.bfloat16)
    small_row = jnp.where(
        core == 0,
        jnp.concatenate([small, slot_gap, lane_gap], axis=1),
        jnp.concatenate([slot_gap, small, lane_gap], axis=1),
    )
    extra = jnp.concatenate(
        [small_row[:, None, :], jnp.zeros((dp_count, EXTRA - 1, row_width), jnp.bfloat16)], axis=1
    )
    chunk_rows = per_owner * NSHELL
    half_shape = jax.ShapeDtypeStruct((dp_count // 2, chunk_rows + EXTRA, row_width), jnp.bfloat16)
    give, keep = pl.pallas_call(
        grad_kernel,
        out_shape=(half_shape, half_shape),
        in_specs=[smem(), smem(), smem(), smem(), smem(), anywhere, vmem(), anywhere, vmem(), vmem()],
        out_specs=(anywhere, anywhere),
        scratch_shapes=[
            pltpu.VMEM((image_rows, row_width), jnp.bfloat16),
            pltpu.VMEM((ref_rows, row_width), jnp.bfloat16),
            pltpu.VMEM((ref_rows, row_width), F32),
            pltpu.VMEM((ref_rows, row_width), jnp.bfloat16),
            pltpu.SemaphoreType.DMA(((image_rows + ref_rows) // CHUNK,)),
            pltpu.SemaphoreType.DMA((2 * dp_count,)),
        ],
        compiler_params=params,
    )(
        count_arr, ent_p, ent_k, ent_e, core.astype(jnp.int32).reshape(1), image_hat, coef,
        ref_hat, volume, extra,
    )

    taken = lax.ppermute(give, "dp", perm=[(i, i ^ 1) for i in range(dp_count)])
    pair_sum = (keep.astype(F32) + taken.astype(F32)).astype(jnp.bfloat16)
    groups = [list(range(q, dp_count, 2)) for q in range(2)]
    arrived = lax.all_to_all(
        pair_sum, "dp", split_axis=0, concat_axis=0, tiled=True, axis_index_groups=groups
    )
    summed = jnp.sum(arrived[:, :chunk_rows].astype(F32), axis=0)
    summed = jnp.dot(summed, inverse, precision=HIGHEST).reshape(per_owner, NSHELL, row_width)

    got = arrived[:, chunk_rows, : 2 * slot_w].astype(F32).reshape(dp_count, slot_w)
    got_ev = (got[:, :per_pair] + got[:, per_pair : 2 * per_pair]).reshape(-1)
    got_pos = got[:, 2 * per_pair : 3 * per_pair].reshape(-1)
    den_at = 3 * per_pair
    own_denom = jnp.sum(
        got[:, den_at : den_at + per_owner] + got[:, den_at + per_owner : den_at + 2 * per_owner],
        axis=0,
    )
    gradient = summed / (1.0 + own_denom)[:, None, None]
    rows = jnp.arange(blocksize, dtype=F32)
    placed = jnp.sum(jnp.where(got_pos[None, :] == rows[:, None], got_ev[None, :], 0.0), axis=1)
    return (gradient[None], placed)


def solution(mesh):
    return jax.shard_map(
        local,
        mesh=mesh,
        in_specs=(
            P("dp", None, None),
            P("dp"),
            P("cls", None, None),
            P(),
            P(),
            P("dp", None),
            P("cls"),
        ),
        out_specs=(P("cls", "dp", None, None), P("dp")),
        check_vma=False,
    )
```
